32 devices in a mesh: rows: 4 (over x, core), dp: 8 (over z, y).
Axes of the slice: x: 2, y: 2, z: 4, core: 2. Of those that a mesh axis runs over, the one named last changes fastest.
Arguments:
- latents: bfloat16 [8, 8, 128, 640], P('dp', 'rows'), may hold values from -160 to 160
- timesteps: int32 [8], P('dp'), may hold values from 0 to 999
- gn_gain: float32 [640], replicated, may hold values from 0.1 to 1.9
- gn_bias: float32 [640], replicated, may hold values from -3 to 3
- conv_weight: bfloat16 [3, 3, 640, 640], replicated, may hold values from -0.078125 to 0.078125
- conv_bias: float32 [640], replicated, may hold values from -3 to 3
- temb_weight: bfloat16 [1280, 640], replicated, may hold values from -0.25 to 0.25
- cotangent: bfloat16 [8, 8, 128, 640], P('dp', 'rows'), may hold values from -6 to 6
Outputs:
- features_out: bfloat16 [8, 8, 128, 640], P('dp', 'rows')
- input_grad: bfloat16 [8, 8, 128, 640], P('dp', 'rows')
- norm_grads: float32 [3, 640], replicated
The draws below stay inside these ranges and needn't reach their ends.
All inputs are finite; a program needn't handle non-finite values.
Results may differ from the reference program's by a relative error of at most 0.0044.
Values may be sent and summed in bfloat16 or wider, within the bound.
No kernel may reach another device: no remote copies, remote signals or barrier semaphores. Data moves between devices by JAX's collectives and lax.ppermute only.
A program may use at most 64 MiB of HBM per device.

```python
import math
import jax
import jax.numpy as jnp
from jax import lax

C = 640
CH_GROUP = 40
TEMB = 1280
WIDTH = 128
HEIGHT = 8
IMAGES = 8


def draw_latents(key, part):
    keys = jax.random.split(jax.random.fold_in(key, 11), 4)
    shape = (IMAGES, HEIGHT, WIDTH, C)
    values = jnp.clip(jax.random.normal(keys[0], shape, jnp.float32), -4.0, 4.0)
    pixel_scale = jnp.exp(jax.random.uniform(keys[1], (IMAGES, HEIGHT, WIDTH, 1), jnp.float32) * math.log(10.0))
    row_ramp = 3.0 ** (jnp.arange(HEIGHT).astype(jnp.float32) / (HEIGHT - 1))
    channel_scale = jnp.exp(jax.random.uniform(keys[2], (C,), jnp.float32) * math.log(10.0)) / 10.0
    offset = jax.random.uniform(keys[3], (C,), jnp.float32, -1.0, 1.0)
    result = values * pixel_scale * row_ramp[None, :, None, None] * channel_scale + offset
    return result.astype(jnp.bfloat16)


def draw_cotangent(key, part):
    keys = jax.random.split(jax.random.fold_in(key, 23), 2)
    shape = (IMAGES, HEIGHT, WIDTH, C)
    noise = jnp.clip(jax.random.normal(keys[0], shape, jnp.float32), -4.0, 4.0)
    level = jnp.clip(1.2 * jax.random.normal(keys[1], (C,), jnp.float32), -2.0, 2.0)
    image_sign = 1.0 - 2.0 * (jnp.arange(IMAGES) % 2).astype(jnp.float32)
    result = noise + image_sign[:, None, None, None] * level
    return result.astype(jnp.bfloat16)


def plant(entries, rng, least, top_value):
    extent = entries.shape
    place = [jax.random.randint(jax.random.fold_in(rng, axis), (), 0, extent[axis]) for axis in range(len(extent))]
    entries = entries.at[tuple(place)].set(least)
    longest = extent.index(max(extent))
    place[longest] = (place[longest] + 1) % extent[longest]
    return entries.at[tuple(place)].set(top_value)


def scatter_about(key, dims, scale, most, kind=jnp.bfloat16):
    entries = jax.random.normal(key, dims, jnp.float32) * scale
    return jnp.minimum(jnp.maximum(entries, -most), most).astype(kind)


def setup_inputs(seed: int = 0) -> dict:
    key_of = jax.random.split(jax.random.key(seed), 9)
    latents = draw_latents(jax.random.fold_in(key_of[8], 71), 0)
    timesteps = plant(jax.random.randint(key_of[1], (IMAGES,), 0, 1000), jax.random.fold_in(key_of[1], 1), 0, 999).astype(jnp.int32)
    gn_gain = jnp.clip(1.0 + 0.18 * jax.random.normal(key_of[2], (C,), jnp.float32), 0.1, 1.9)
    gn_bias = scatter_about(key_of[3], (C,), 0.5, 3.0, jnp.float32)
    conv_weight = scatter_about(key_of[4], (3, 3, C, C), (9 * C) ** -0.5, 0.078125)
    conv_bias = scatter_about(key_of[5], (C,), 0.5, 3.0, jnp.float32)
    temb_weight = scatter_about(key_of[6], (TEMB, C), (TEMB // 2) ** -0.5, 0.25)
    cotangent = draw_cotangent(jax.random.fold_in(key_of[8], 71), 0)
    return {"latents": latents, "timesteps": timesteps, "gn_gain": gn_gain, "gn_bias": gn_bias, "conv_weight": conv_weight, "conv_bias": conv_bias, "temb_weight": temb_weight, "cotangent": cotangent}


NORM_EPS = 1e-05

def sinusoid(steps, embed_dim):
    half_dim = embed_dim // 2
    frequencies = jnp.exp(-math.log(10000.0) * jnp.arange(half_dim).astype(jnp.float32) / half_dim)
    angles = steps.astype(jnp.float32)[:, None] * frequencies[None, :]
    return jnp.concatenate([jnp.cos(angles), jnp.sin(angles)], axis=1)

def conv_forward(hidden, weight):
    row_count, col_count, channels = hidden.shape
    padded = jnp.pad(hidden, ((1, 1), (1, 1), (0, 0)))
    total = jnp.zeros((row_count * col_count, weight.shape[3]), jnp.float32)
    for tap_row in range(3):
        for tap_col in range(3):
            window = padded[tap_row:tap_row + row_count, tap_col:tap_col + col_count].reshape(row_count * col_count, channels)
            total = total + jnp.dot(window, weight[tap_row, tap_col], preferred_element_type=jnp.float32)
    return total.reshape(row_count, col_count, weight.shape[3])

def conv_backward(grad_out, weight):
    row_count, col_count, channels = grad_out.shape
    padded = jnp.pad(grad_out, ((1, 1), (1, 1), (0, 0)))
    total = jnp.zeros((row_count * col_count, weight.shape[2]), jnp.float32)
    for tap_row in range(3):
        for tap_col in range(3):
            window = padded[2 - tap_row:2 - tap_row + row_count, 2 - tap_col:2 - tap_col + col_count].reshape(row_count * col_count, channels)
            total = total + jnp.dot(window, weight[tap_row, tap_col].T, preferred_element_type=jnp.float32)
    return total.reshape(row_count, col_count, weight.shape[2])

def reference(latents, timesteps, gn_gain, gn_bias, conv_weight, conv_bias, temb_weight, cotangent):
    temb_features = jax.nn.silu(sinusoid(timesteps, TEMB)).astype(jnp.bfloat16)
    time_shift = jnp.dot(temb_features, temb_weight, preferred_element_type=jnp.float32)

    def one_image(inputs_one):
        image, grad_out, shift = inputs_one
        row_count, col_count, channels = image.shape
        groups = channels // CH_GROUP
        group_cells = row_count * col_count * CH_GROUP
        grouped = image.astype(jnp.float32).reshape(row_count, col_count, groups, CH_GROUP)
        group_mean = lax.optimization_barrier(jnp.sum(grouped, axis=(0, 1, 3))) / group_cells
        centered = grouped - group_mean[:, None]
        variance = lax.optimization_barrier(jnp.sum(centered * centered, axis=(0, 1, 3))) / group_cells
        inv_std = lax.rsqrt(variance + NORM_EPS)
        norm_groups = centered * inv_std[:, None]
        normalized = norm_groups.reshape(row_count, col_count, channels)
        pre_act = normalized * gn_gain + gn_bias
        hidden = jax.nn.silu(pre_act).astype(jnp.bfloat16)
        features = (conv_forward(hidden, conv_weight) + conv_bias + shift).astype(jnp.bfloat16)
        hidden_grad = conv_backward(grad_out, conv_weight)
        sigmoid_act = jax.nn.sigmoid(pre_act)
        act_grad = hidden_grad * sigmoid_act * (1.0 + pre_act * (1.0 - sigmoid_act))
        hat_grad = (act_grad * gn_gain).reshape(row_count, col_count, groups, CH_GROUP)
        first_mean = lax.optimization_barrier(jnp.sum(hat_grad, axis=(0, 1, 3))) / group_cells
        second_mean = lax.optimization_barrier(jnp.sum(hat_grad * norm_groups, axis=(0, 1, 3))) / group_cells
        input_grad = inv_std[:, None] * (hat_grad - first_mean[:, None] - norm_groups * second_mean[:, None])
        input_grad = input_grad.reshape(row_count, col_count, channels).astype(jnp.bfloat16)
        sums = jnp.stack([lax.optimization_barrier(jnp.sum(act_grad * normalized, axis=(0, 1))), lax.optimization_barrier(jnp.sum(act_grad, axis=(0, 1))), lax.optimization_barrier(jnp.sum(grad_out.astype(jnp.float32), axis=(0, 1)))])
        return (features, input_grad, sums)
    features_out, input_grad, sums = lax.map(one_image, (latents, cotangent, time_shift))
    norm_grads = lax.optimization_barrier(jnp.sum(sums, axis=0)) / math.sqrt(IMAGES * HEIGHT * WIDTH)
    return (features_out, input_grad, norm_grads)
```

```python
import math

import jax
import jax.numpy as jnp
from jax import lax
from jax.sharding import PartitionSpec as P

CH_GROUP = 40


NORM_EPS = 1e-05


def padded_2(cells, sides, width):
    for axis, dim in sides:
        count = lax.axis_size(axis)
        ends = count - 1
        head = lax.slice_in_dim(cells, 0, width, axis=dim)
        tail = lax.slice_in_dim(cells, cells.shape[dim] - width, cells.shape[dim], axis=dim)
        cells = jnp.concatenate(
            [
                lax.ppermute(tail, axis, [(i, (i + 1) % count) for i in range(ends)]),
                cells,
                lax.ppermute(head, axis, [((i + 1) % count, i) for i in range(ends)]),
            ],
            axis=dim,
        )
    return cells


def is_pow2(count):
    return count & (count - 1) == 0


def all_sum(value, axis):
    count = lax.axis_size(axis)
    if not is_pow2(count):
        return lax.psum(value, axis)
    step = 1
    while step < count:
        other = lax.ppermute(value, axis, [(i, i ^ step) for i in range(count)])
        value = value + other
        step *= 2
    return value


def merge_stats(mean, m2, cells, axis):
    count = lax.axis_size(axis)
    if not is_pow2(count):
        means = lax.all_gather(mean, axis)
        total_mean = jnp.mean(means, axis=0)
        spread = means - total_mean
        return total_mean, jnp.sum(lax.all_gather(m2, axis), axis=0) + cells * jnp.sum(spread * spread, axis=0)
    value = jnp.stack([mean, m2])
    step = 1
    while step < count:
        other = lax.ppermute(value, axis, [(i, i ^ step) for i in range(count)])
        delta = other[0] - value[0]
        value = jnp.stack(
            [(value[0] + other[0]) * 0.5, value[1] + other[1] + delta * delta * (cells * step * 0.5)]
        )
        step *= 2
    return value[0], value[1]


def sinusoid(steps, embed_dim):
    half_dim = embed_dim // 2
    frequencies = jnp.exp(-math.log(10000.0) * jnp.arange(half_dim).astype(jnp.float32) / half_dim)
    angles = steps.astype(jnp.float32)[:, None] * frequencies[None, :]
    return jnp.concatenate([jnp.cos(angles), jnp.sin(angles)], axis=1)


def with_rim(field):
    return padded_2(field, (("rows", 1),), 1)


def conv_taps(extended, weight, slab_rows, col_count, backward):
    padded = jnp.pad(extended, ((0, 0), (0, 0), (1, 1), (0, 0)))
    images = padded.shape[0]
    channels = padded.shape[3]
    total = None
    for tap_row in range(3):
        for tap_col in range(3):
            if backward:
                row_start, col_start = (2 - tap_row, 2 - tap_col)
            else:
                row_start, col_start = (tap_row, tap_col)
            window = padded[
                :, row_start : row_start + slab_rows, col_start : col_start + col_count
            ].reshape(-1, channels)
            if backward:
                tap_term = lax.dot_general(
                    window,
                    weight[tap_row, tap_col],
                    (((1,), (1,)), ((), ())),
                    preferred_element_type=jnp.float32,
                )
            else:
                tap_term = jnp.dot(
                    window, weight[tap_row, tap_col], preferred_element_type=jnp.float32
                )
            total = tap_term if total is None else total + tap_term
    return total.reshape(images, slab_rows, col_count, -1)


def per_device(
    latents, timesteps, gn_gain, gn_bias, conv_weight, conv_bias, temb_weight, cotangent
):
    images, slab_rows, col_count, channels = latents.shape
    groups = channels // CH_GROUP
    row_devices = lax.axis_size("rows")
    group_cells = slab_rows * row_devices * col_count * CH_GROUP
    local_cells = slab_rows * col_count * CH_GROUP
    grouped = latents.astype(jnp.float32).reshape(images, slab_rows, col_count, groups, CH_GROUP)
    local_mean = jnp.sum(grouped, axis=(1, 2, 4)) / local_cells
    local_dev = grouped - local_mean[:, None, None, :, None]
    local_m2 = jnp.sum(local_dev * local_dev, axis=(1, 2, 4))
    group_mean, group_m2 = merge_stats(local_mean, local_m2, local_cells, "rows")
    inv_std = lax.rsqrt(group_m2 / group_cells + NORM_EPS)
    shaped = latents.astype(jnp.float32).reshape(images, -1, col_count, groups, CH_GROUP)
    norm_groups = (shaped - group_mean[:, None, None, :, None]) * inv_std[:, None, None, :, None]
    normalized = norm_groups.reshape(images, -1, col_count, channels)
    norm_groups, normalized, pre_act = (norm_groups, normalized, normalized * gn_gain + gn_bias)
    hidden = jax.nn.silu(pre_act).astype(jnp.bfloat16)
    grad_rim = None
    extended = with_rim(hidden)
    temb_features = jax.nn.silu(sinusoid(timesteps, temb_weight.shape[0])).astype(jnp.bfloat16)
    time_shift = jnp.dot(temb_features, temb_weight, preferred_element_type=jnp.float32)
    features = conv_taps(extended, conv_weight, slab_rows, col_count, False)
    features_out = (features + conv_bias + time_shift[:, None, None, :]).astype(jnp.bfloat16)
    grad_rim = with_rim(cotangent)
    hidden_grad = conv_taps(grad_rim, conv_weight, slab_rows, col_count, True)
    sigmoid_act = jax.nn.sigmoid(pre_act)
    act_grad = hidden_grad * sigmoid_act * (1.0 + pre_act * (1.0 - sigmoid_act))
    hat_groups = (act_grad * gn_gain).reshape(images, slab_rows, col_count, groups, CH_GROUP)
    chan_weighted = jnp.sum(act_grad * normalized, axis=(1, 2))
    chan_plain = jnp.sum(act_grad, axis=(1, 2))
    chan_output = jnp.sum(cotangent.astype(jnp.float32), axis=(1, 2))
    row_sums = all_sum(jnp.stack([chan_weighted, chan_plain, chan_output], axis=1), "rows")
    row_weighted, row_plain = row_sums[:, 0], row_sums[:, 1]
    first_sum = jnp.sum((row_plain * gn_gain).reshape(images, groups, CH_GROUP), axis=2)
    second_sum = jnp.sum((row_weighted * gn_gain).reshape(images, groups, CH_GROUP), axis=2)
    param_sums = all_sum(jnp.sum(row_sums, axis=0), "dp")
    first_mean = first_sum / group_cells
    second_mean = second_sum / group_cells
    expand = (slice(None), None, None, slice(None), None)
    input_grad = inv_std[expand] * (
        hat_groups - first_mean[expand] - norm_groups * second_mean[expand]
    )
    input_grad = input_grad.reshape(images, slab_rows, col_count, channels).astype(jnp.bfloat16)
    grad_scale = 1.0 / math.sqrt(images * lax.axis_size("dp") * slab_rows * row_devices * col_count)
    return (features_out, input_grad, param_sums * grad_scale)


def solution(mesh):
    placed = (
        P("dp", "rows", None, None),
        P("dp"),
        P(),
        P(),
        P(),
        P(),
        P(),
        P("dp", "rows", None, None),
    )
    return jax.shard_map(
        per_device,
        mesh=mesh,
        in_specs=placed,
        out_specs=(P("dp", "rows", None, None), P("dp", "rows", None, None), P()),
        check_vma=False,
    )
```

```python
import math

import jax
import jax.numpy as jnp
from jax import lax
from jax.sharding import PartitionSpec as P

CH_GROUP = 40


NORM_EPS = 1e-05


def padded_2(cells, sides, width):
    for axis, dim in sides:
        count = lax.axis_size(axis)
        ends = count - 1
        head = lax.slice_in_dim(cells, 0, width, axis=dim)
        tail = lax.slice_in_dim(cells, cells.shape[dim] - width, cells.shape[dim], axis=dim)
        cells = jnp.concatenate(
            [
                lax.ppermute(tail, axis, [(i, (i + 1) % count) for i in range(ends)]),
                cells,
                lax.ppermute(head, axis, [((i + 1) % count, i) for i in range(ends)]),
            ],
            axis=dim,
        )
    return cells


def is_pow2(count):
    return count & (count - 1) == 0


def all_sum(value, axis):
    count = lax.axis_size(axis)
    if not is_pow2(count):
        return lax.psum(value, axis)
    step = 1
    while step < count:
        other = lax.ppermute(value, axis, [(i, i ^ step) for i in range(count)])
        value = value + other
        step *= 2
    return value


def merge_stats(mean, m2, cells, axis):
    count = lax.axis_size(axis)
    if not is_pow2(count):
        means = lax.all_gather(mean, axis)
        total_mean = jnp.mean(means, axis=0)
        spread = means - total_mean
        return total_mean, jnp.sum(lax.all_gather(m2, axis), axis=0) + cells * jnp.sum(spread * spread, axis=0)
    value = jnp.stack([mean, m2])
    step = 1
    while step < count:
        other = lax.ppermute(value, axis, [(i, i ^ step) for i in range(count)])
        delta = other[0] - value[0]
        value = jnp.stack(
            [(value[0] + other[0]) * 0.5, value[1] + other[1] + delta * delta * (cells * step * 0.5)]
        )
        step *= 2
    return value[0], value[1]


def sinusoid(steps, embed_dim):
    half_dim = embed_dim // 2
    frequencies = jnp.exp(-math.log(10000.0) * jnp.arange(half_dim).astype(jnp.float32) / half_dim)
    angles = steps.astype(jnp.float32)[:, None] * frequencies[None, :]
    return jnp.concatenate([jnp.cos(angles), jnp.sin(angles)], axis=1)


def with_rim(field):
    return padded_2(field, (("rows", 1),), 1)


def conv_same(extended, kernel, spec):
    return lax.conv_general_dilated(
        extended,
        kernel,
        (1, 1),
        ((0, 0), (1, 1)),
        dimension_numbers=("NHWC", spec, "NHWC"),
        preferred_element_type=jnp.float32,
    )


def per_device(
    latents, timesteps, gn_gain, gn_bias, conv_weight, conv_bias, temb_weight, cotangent
):
    images, slab_rows, col_count, channels = latents.shape
    groups = channels // CH_GROUP
    row_devices = lax.axis_size("rows")
    group_cells = slab_rows * row_devices * col_count * CH_GROUP
    positions = slab_rows * col_count
    values = latents.astype(jnp.float32)
    chan_mean = jnp.sum(values, axis=(1, 2)) / positions
    centered = values - chan_mean[:, None, None, :]
    chan_m2 = jnp.sum(centered * centered, axis=(1, 2))
    chan_mean_g = chan_mean.reshape(images, groups, CH_GROUP)
    local_mean = jnp.mean(chan_mean_g, axis=2)
    spread = chan_mean_g - local_mean[:, :, None]
    local_m2 = jnp.sum(chan_m2.reshape(images, groups, CH_GROUP), axis=2) + positions * jnp.sum(
        spread * spread, axis=2
    )
    group_mean, group_m2 = merge_stats(local_mean, local_m2, positions * CH_GROUP, "rows")
    inv_std = lax.rsqrt(group_m2 / group_cells + NORM_EPS)
    mean_ch = jnp.repeat(group_mean, CH_GROUP, axis=1)[:, None, None, :]
    rstd_ch = jnp.repeat(inv_std, CH_GROUP, axis=1)[:, None, None, :]
    normalized = (values - mean_ch) * rstd_ch
    pre_act = normalized * gn_gain + gn_bias
    hidden = jax.nn.silu(pre_act).astype(jnp.bfloat16)
    extended = with_rim(hidden)
    temb_features = jax.nn.silu(sinusoid(timesteps, temb_weight.shape[0])).astype(jnp.bfloat16)
    time_shift = jnp.dot(temb_features, temb_weight, preferred_element_type=jnp.float32)
    features = conv_same(extended, conv_weight, "HWIO")
    features_out = (features + conv_bias + time_shift[:, None, None, :]).astype(jnp.bfloat16)
    grad_rim = with_rim(cotangent)
    hidden_grad = conv_same(grad_rim, conv_weight[::-1, ::-1], "HWOI")
    sigmoid_act = jax.nn.sigmoid(pre_act)
    act_grad = hidden_grad * sigmoid_act * (1.0 + pre_act * (1.0 - sigmoid_act))
    chan_weighted = jnp.sum(act_grad * normalized, axis=(1, 2))
    chan_plain = jnp.sum(act_grad, axis=(1, 2))
    chan_output = jnp.sum(cotangent.astype(jnp.float32), axis=(1, 2))
    row_sums = all_sum(jnp.stack([chan_weighted, chan_plain, chan_output], axis=1), "rows")
    row_weighted, row_plain = row_sums[:, 0], row_sums[:, 1]
    first_sum = jnp.sum((row_plain * gn_gain).reshape(images, groups, CH_GROUP), axis=2)
    second_sum = jnp.sum((row_weighted * gn_gain).reshape(images, groups, CH_GROUP), axis=2)
    param_sums = all_sum(jnp.sum(row_sums, axis=0), "dp")
    first_ch = jnp.repeat(first_sum / group_cells, CH_GROUP, axis=1)[:, None, None, :]
    second_ch = jnp.repeat(second_sum / group_cells, CH_GROUP, axis=1)[:, None, None, :]
    input_grad = rstd_ch * (act_grad * gn_gain - first_ch - normalized * second_ch)
    input_grad = input_grad.astype(jnp.bfloat16)
    grad_scale = 1.0 / math.sqrt(images * lax.axis_size("dp") * slab_rows * row_devices * col_count)
    return (features_out, input_grad, param_sums * grad_scale)


def solution(mesh):
    placed = (
        P("dp", "rows", None, None),
        P("dp"),
        P(),
        P(),
        P(),
        P(),
        P(),
        P("dp", "rows", None, None),
    )
    return jax.shard_map(
        per_device,
        mesh=mesh,
        in_specs=placed,
        out_specs=(P("dp", "rows", None, None), P("dp", "rows", None, None), P()),
        check_vma=False,
    )
```

```python
import math

import jax
import jax.numpy as jnp
from jax import lax
from jax.sharding import PartitionSpec as P

CH_GROUP = 40


NORM_EPS = 1e-05


def padded_2(cells, sides, width):
    for axis, dim in sides:
        count = lax.axis_size(axis)
        ends = count - 1
        head = lax.slice_in_dim(cells, 0, width, axis=dim)
        tail = lax.slice_in_dim(cells, cells.shape[dim] - width, cells.shape[dim], axis=dim)
        cells = jnp.concatenate(
            [
                lax.ppermute(tail, axis, [(i, (i + 1) % count) for i in range(ends)]),
                cells,
                lax.ppermute(head, axis, [((i + 1) % count, i) for i in range(ends)]),
            ],
            axis=dim,
        )
    return cells


def is_pow2(count):
    return count & (count - 1) == 0


def all_sum(value, axis):
    count = lax.axis_size(axis)
    if not is_pow2(count):
        return lax.psum(value, axis)
    step = 1
    while step < count:
        other = lax.ppermute(value, axis, [(i, i ^ step) for i in range(count)])
        value = value + other
        step *= 2
    return value


def merge_stats(mean, m2, cells, axis):
    count = lax.axis_size(axis)
    if not is_pow2(count):
        means = lax.all_gather(mean, axis)
        total_mean = jnp.mean(means, axis=0)
        spread = means - total_mean
        return total_mean, jnp.sum(lax.all_gather(m2, axis), axis=0) + cells * jnp.sum(spread * spread, axis=0)
    value = jnp.stack([mean, m2])
    step = 1
    while step < count:
        other = lax.ppermute(value, axis, [(i, i ^ step) for i in range(count)])
        delta = other[0] - value[0]
        value = jnp.stack(
            [(value[0] + other[0]) * 0.5, value[1] + other[1] + delta * delta * (cells * step * 0.5)]
        )
        step *= 2
    return value[0], value[1]


def sinusoid(steps, embed_dim):
    half_dim = embed_dim // 2
    frequencies = jnp.exp(-math.log(10000.0) * jnp.arange(half_dim).astype(jnp.float32) / half_dim)
    angles = steps.astype(jnp.float32)[:, None] * frequencies[None, :]
    return jnp.concatenate([jnp.cos(angles), jnp.sin(angles)], axis=1)


def with_rim(field):
    return padded_2(field, (("rows", 2),), 1)


def conv_taps(extended, weight, slab_rows, col_count, backward):
    padded = jnp.pad(extended, ((0, 0), (0, 0), (1, 1), (0, 0)))
    channels = padded.shape[3]
    total = None
    for tap_row in range(3):
        for tap_col in range(3):
            if backward:
                row_start, col_start = (2 - tap_row, 2 - tap_col)
                dims = (((1,), (1,)), ((), ()))
            else:
                row_start, col_start = (tap_row, tap_col)
                dims = (((1,), (0,)), ((), ()))
            window = padded[
                :, row_start : row_start + slab_rows, col_start : col_start + col_count
            ].reshape(-1, channels)
            tap_term = lax.dot_general(
                window, weight[tap_row, tap_col], dims, preferred_element_type=jnp.float32
            )
            total = tap_term if total is None else total + tap_term
    return total.reshape(-1, slab_rows, col_count, weight.shape[3])


def per_device(
    latents, timesteps, gn_gain, gn_bias, conv_weight, conv_bias, temb_weight, cotangent
):
    images, slab_rows, col_count, channels = latents.shape
    groups = channels // CH_GROUP
    row_devices = lax.axis_size("rows")
    group_cells = slab_rows * row_devices * col_count * CH_GROUP
    positions = slab_rows * col_count
    both_ext = with_rim(jnp.stack([latents, cotangent]))
    row_index = lax.axis_index("rows")
    inside = jnp.concatenate(
        [
            jnp.where(row_index > 0, 1.0, 0.0)[None],
            jnp.ones((slab_rows,), jnp.float32),
            jnp.where(row_index < row_devices - 1, 1.0, 0.0)[None],
        ]
    )[None, :, None, None]
    values = latents.astype(jnp.float32)
    chan_mean = jnp.sum(values, axis=(1, 2)) / positions
    centered = values - chan_mean[:, None, None, :]
    chan_m2 = jnp.sum(centered * centered, axis=(1, 2))
    chan_mean_g = chan_mean.reshape(images, groups, CH_GROUP)
    local_mean = jnp.mean(chan_mean_g, axis=2)
    spread = chan_mean_g - local_mean[:, :, None]
    local_m2 = jnp.sum(chan_m2.reshape(images, groups, CH_GROUP), axis=2) + positions * jnp.sum(
        spread * spread, axis=2
    )
    group_mean, group_m2 = merge_stats(local_mean, local_m2, positions * CH_GROUP, "rows")
    inv_std = lax.rsqrt(group_m2 / group_cells + NORM_EPS)
    mean_ch = jnp.repeat(group_mean, CH_GROUP, axis=1)[:, None, None, :]
    rstd_ch = jnp.repeat(inv_std, CH_GROUP, axis=1)[:, None, None, :]
    normalized_ext = (both_ext[0].astype(jnp.float32) - mean_ch) * rstd_ch
    pre_act_ext = normalized_ext * gn_gain + gn_bias
    extended = (jax.nn.silu(pre_act_ext) * inside).astype(jnp.bfloat16)
    normalized = normalized_ext[:, 1 : 1 + slab_rows]
    pre_act = pre_act_ext[:, 1 : 1 + slab_rows]
    temb_features = jax.nn.silu(sinusoid(timesteps, temb_weight.shape[0])).astype(jnp.bfloat16)
    time_shift = jnp.dot(temb_features, temb_weight, preferred_element_type=jnp.float32)
    features = conv_taps(extended, conv_weight, slab_rows, col_count, False)
    features_out = (features + conv_bias + time_shift[:, None, None, :]).astype(jnp.bfloat16)
    hidden_grad = conv_taps(both_ext[1], conv_weight, slab_rows, col_count, True)
    sigmoid_act = jax.nn.sigmoid(pre_act)
    act_grad = hidden_grad * sigmoid_act * (1.0 + pre_act * (1.0 - sigmoid_act))
    chan_weighted = jnp.sum(act_grad * normalized, axis=(1, 2))
    chan_plain = jnp.sum(act_grad, axis=(1, 2))
    chan_output = jnp.sum(cotangent.astype(jnp.float32), axis=(1, 2))
    row_sums = all_sum(jnp.stack([chan_weighted, chan_plain, chan_output], axis=1), "rows")
    row_weighted, row_plain = row_sums[:, 0], row_sums[:, 1]
    first_sum = jnp.sum((row_plain * gn_gain).reshape(images, groups, CH_GROUP), axis=2)
    second_sum = jnp.sum((row_weighted * gn_gain).reshape(images, groups, CH_GROUP), axis=2)
    param_sums = all_sum(jnp.sum(row_sums, axis=0), "dp")
    first_ch = jnp.repeat(first_sum / group_cells, CH_GROUP, axis=1)[:, None, None, :]
    second_ch = jnp.repeat(second_sum / group_cells, CH_GROUP, axis=1)[:, None, None, :]
    input_grad = rstd_ch * (act_grad * gn_gain - first_ch - normalized * second_ch)
    input_grad = input_grad.astype(jnp.bfloat16)
    grad_scale = 1.0 / math.sqrt(images * lax.axis_size("dp") * slab_rows * row_devices * col_count)
    return (features_out, input_grad, param_sums * grad_scale)


def solution(mesh):
    placed = (
        P("dp", "rows", None, None),
        P("dp"),
        P(),
        P(),
        P(),
        P(),
        P(),
        P("dp", "rows", None, None),
    )
    return jax.shard_map(
        per_device,
        mesh=mesh,
        in_specs=placed,
        out_specs=(P("dp", "rows", None, None), P("dp", "rows", None, None), P()),
        check_vma=False,
    )
```

```python
import math

import jax
import jax.numpy as jnp
from jax import lax
from jax.sharding import PartitionSpec as P

CH_GROUP = 40


NORM_EPS = 1e-05


def padded_2(cells, sides, width):
    for axis, dim in sides:
        count = lax.axis_size(axis)
        ends = count - 1
        head = lax.slice_in_dim(cells, 0, width, axis=dim)
        tail = lax.slice_in_dim(cells, cells.shape[dim] - width, cells.shape[dim], axis=dim)
        cells = jnp.concatenate(
            [
                lax.ppermute(tail, axis, [(i, (i + 1) % count) for i in range(ends)]),
                cells,
                lax.ppermute(head, axis, [((i + 1) % count, i) for i in range(ends)]),
            ],
            axis=dim,
        )
    return cells


def is_pow2(count):
    return count & (count - 1) == 0


def all_sum(value, axis):
    count = lax.axis_size(axis)
    if not is_pow2(count):
        return lax.psum(value, axis)
    step = 1
    while step < count:
        other = lax.ppermute(value, axis, [(i, i ^ step) for i in range(count)])
        value = value + other
        step *= 2
    return value


def merge_stats(mean, m2, cells, axis, riders):
    count = lax.axis_size(axis)
    if not is_pow2(count):
        means = lax.all_gather(mean, axis)
        total_mean = jnp.mean(means, axis=0)
        spread = means - total_mean
        total_m2 = jnp.sum(lax.all_gather(m2, axis), axis=0) + cells * jnp.sum(spread * spread, axis=0)
        return total_mean, total_m2, riders
    value = jnp.stack([mean, m2])
    step = 1
    while step < count:
        other = lax.ppermute(value, axis, [(i, i ^ step) for i in range(count)])
        delta = other[0] - value[0]
        value = jnp.stack(
            [(value[0] + other[0]) * 0.5, value[1] + other[1] + delta * delta * (cells * step * 0.5)]
        )
        if step == 1:
            value, riders = lax.optimization_barrier((value, riders))
        step *= 2
    return value[0], value[1], riders


def sinusoid(steps, embed_dim):
    half_dim = embed_dim // 2
    frequencies = jnp.exp(-math.log(10000.0) * jnp.arange(half_dim).astype(jnp.float32) / half_dim)
    angles = steps.astype(jnp.float32)[:, None] * frequencies[None, :]
    return jnp.concatenate([jnp.cos(angles), jnp.sin(angles)], axis=1)


def with_rim(field):
    return padded_2(field, (("rows", 2),), 1)


def conv_taps(extended, weight, slab_rows, col_count, backward):
    padded = jnp.pad(extended, ((0, 0), (0, 0), (1, 1), (0, 0)))
    channels = padded.shape[3]
    total = None
    for tap_row in range(3):
        for tap_col in range(3):
            if backward:
                row_start, col_start = (2 - tap_row, 2 - tap_col)
                dims = (((1,), (1,)), ((), ()))
            else:
                row_start, col_start = (tap_row, tap_col)
                dims = (((1,), (0,)), ((), ()))
            window = padded[
                :, row_start : row_start + slab_rows, col_start : col_start + col_count
            ].reshape(-1, channels)
            tap_term = lax.dot_general(
                window, weight[tap_row, tap_col], dims, preferred_element_type=jnp.float32
            )
            total = tap_term if total is None else total + tap_term
    return total.reshape(-1, slab_rows, col_count, weight.shape[3])


def per_device(
    latents, timesteps, gn_gain, gn_bias, conv_weight, conv_bias, temb_weight, cotangent
):
    images, slab_rows, col_count, channels = latents.shape
    groups = channels // CH_GROUP
    row_devices = lax.axis_size("rows")
    group_cells = slab_rows * row_devices * col_count * CH_GROUP
    positions = slab_rows * col_count
    both_ext = with_rim(jnp.stack([latents, cotangent]))
    row_index = lax.axis_index("rows")
    inside = jnp.concatenate(
        [
            jnp.where(row_index > 0, 1.0, 0.0)[None],
            jnp.ones((slab_rows,), jnp.float32),
            jnp.where(row_index < row_devices - 1, 1.0, 0.0)[None],
        ]
    )[None, :, None, None]
    latents, both_ext = lax.optimization_barrier((latents, both_ext))
    values = latents.astype(jnp.float32)
    chan_mean = jnp.sum(values, axis=(1, 2)) / positions
    centered = values - chan_mean[:, None, None, :]
    chan_m2 = jnp.sum(centered * centered, axis=(1, 2))
    chan_mean_g = chan_mean.reshape(images, groups, CH_GROUP)
    local_mean = jnp.mean(chan_mean_g, axis=2)
    spread = chan_mean_g - local_mean[:, :, None]
    local_m2 = jnp.sum(chan_m2.reshape(images, groups, CH_GROUP), axis=2) + positions * jnp.sum(
        spread * spread, axis=2
    )
    group_mean, group_m2, grad_rim = merge_stats(
        local_mean, local_m2, positions * CH_GROUP, "rows", both_ext[1]
    )
    inv_std = lax.rsqrt(group_m2 / group_cells + NORM_EPS)
    mean_ch = jnp.repeat(group_mean, CH_GROUP, axis=1)[:, None, None, :]
    rstd_ch = jnp.repeat(inv_std, CH_GROUP, axis=1)[:, None, None, :]
    normalized_ext = (both_ext[0].astype(jnp.float32) - mean_ch) * rstd_ch
    pre_act_ext = normalized_ext * gn_gain + gn_bias
    extended = (jax.nn.silu(pre_act_ext) * inside).astype(jnp.bfloat16)
    normalized = normalized_ext[:, 1 : 1 + slab_rows]
    pre_act = pre_act_ext[:, 1 : 1 + slab_rows]
    temb_features = jax.nn.silu(sinusoid(timesteps, temb_weight.shape[0])).astype(jnp.bfloat16)
    time_shift = jnp.dot(temb_features, temb_weight, preferred_element_type=jnp.float32)
    features = conv_taps(extended, conv_weight, slab_rows, col_count, False)
    features_out = (features + conv_bias + time_shift[:, None, None, :]).astype(jnp.bfloat16)
    hidden_grad = conv_taps(grad_rim, conv_weight, slab_rows, col_count, True)
    sigmoid_act = jax.nn.sigmoid(pre_act)
    act_grad = hidden_grad * sigmoid_act * (1.0 + pre_act * (1.0 - sigmoid_act))
    chan_weighted = jnp.sum(act_grad * normalized, axis=(1, 2))
    chan_plain = jnp.sum(act_grad, axis=(1, 2))
    chan_output = jnp.sum(cotangent.astype(jnp.float32), axis=(1, 2))
    row_sums = all_sum(jnp.stack([chan_weighted, chan_plain, chan_output], axis=1), "rows")
    row_weighted, row_plain = row_sums[:, 0], row_sums[:, 1]
    first_sum = jnp.sum((row_plain * gn_gain).reshape(images, groups, CH_GROUP), axis=2)
    second_sum = jnp.sum((row_weighted * gn_gain).reshape(images, groups, CH_GROUP), axis=2)
    param_sums = all_sum(jnp.sum(row_sums, axis=0), "dp")
    first_ch = jnp.repeat(first_sum / group_cells, CH_GROUP, axis=1)[:, None, None, :]
    second_ch = jnp.repeat(second_sum / group_cells, CH_GROUP, axis=1)[:, None, None, :]
    input_grad = rstd_ch * (act_grad * gn_gain - first_ch - normalized * second_ch)
    input_grad = input_grad.astype(jnp.bfloat16)
    grad_scale = 1.0 / math.sqrt(images * lax.axis_size("dp") * slab_rows * row_devices * col_count)
    return (features_out, input_grad, param_sums * grad_scale)


def solution(mesh):
    placed = (
        P("dp", "rows", None, None),
        P("dp"),
        P(),
        P(),
        P(),
        P(),
        P(),
        P("dp", "rows", None, None),
    )
    return jax.shard_map(
        per_device,
        mesh=mesh,
        in_specs=placed,
        out_specs=(P("dp", "rows", None, None), P("dp", "rows", None, None), P()),
        check_vma=False,
    )
```

```python
import math

import jax
import jax.numpy as jnp
from jax import lax
from jax.sharding import PartitionSpec as P

CH_GROUP = 40


NORM_EPS = 1e-05


def padded_2(cells, sides, width):
    for axis, dim in sides:
        count = lax.axis_size(axis)
        ends = count - 1
        head = lax.slice_in_dim(cells, 0, width, axis=dim)
        tail = lax.slice_in_dim(cells, cells.shape[dim] - width, cells.shape[dim], axis=dim)
        cells = jnp.concatenate(
            [
                lax.ppermute(tail, axis, [(i, (i + 1) % count) for i in range(ends)]),
                cells,
                lax.ppermute(head, axis, [((i + 1) % count, i) for i in range(ends)]),
            ],
            axis=dim,
        )
    return cells


def is_pow2(count):
    return count & (count - 1) == 0


def all_sum(value, axis):
    count = lax.axis_size(axis)
    if not is_pow2(count):
        return lax.psum(value, axis)
    step = 1
    while step < count:
        other = lax.ppermute(value, axis, [(i, i ^ step) for i in range(count)])
        value = value + other
        step *= 2
    return value


def merge_stats(mean, m2, cells, axis, riders):
    count = lax.axis_size(axis)
    if not is_pow2(count):
        means = lax.all_gather(mean, axis)
        total_mean = jnp.mean(means, axis=0)
        spread = means - total_mean
        total_m2 = jnp.sum(lax.all_gather(m2, axis), axis=0) + cells * jnp.sum(spread * spread, axis=0)
        return total_mean, total_m2, riders
    value = jnp.stack([mean, m2])
    step = 1
    while step < count:
        other = lax.ppermute(value, axis, [(i, i ^ step) for i in range(count)])
        delta = other[0] - value[0]
        value = jnp.stack(
            [(value[0] + other[0]) * 0.5, value[1] + other[1] + delta * delta * (cells * step * 0.5)]
        )
        if step == 1:
            value, riders = lax.optimization_barrier((value, riders))
        step *= 2
    return value[0], value[1], riders


def sinusoid(steps, embed_dim):
    half_dim = embed_dim // 2
    frequencies = jnp.exp(-math.log(10000.0) * jnp.arange(half_dim).astype(jnp.float32) / half_dim)
    angles = steps.astype(jnp.float32)[:, None] * frequencies[None, :]
    return jnp.concatenate([jnp.cos(angles), jnp.sin(angles)], axis=1)


def with_rim(field):
    return padded_2(field, (("rows", 1),), 1)


def conv_taps(extended, weight, slab_rows, col_count, backward):
    padded = jnp.pad(extended, ((0, 0), (0, 0), (1, 1), (0, 0)))
    channels = padded.shape[3]
    total = None
    for tap_row in range(3):
        for tap_col in range(3):
            if backward:
                row_start, col_start = (2 - tap_row, 2 - tap_col)
                dims = (((1,), (1,)), ((), ()))
            else:
                row_start, col_start = (tap_row, tap_col)
                dims = (((1,), (0,)), ((), ()))
            window = padded[
                :, row_start : row_start + slab_rows, col_start : col_start + col_count
            ].reshape(-1, channels)
            tap_term = lax.dot_general(
                window, weight[tap_row, tap_col], dims, preferred_element_type=jnp.float32
            )
            total = tap_term if total is None else total + tap_term
    return total.reshape(-1, slab_rows, col_count, weight.shape[3])


def edge_taps(edge_row, weight, tap_row, col_count):
    padded = jnp.pad(edge_row, ((0, 0), (0, 0), (1, 1), (0, 0)))
    channels = padded.shape[3]
    total = None
    for tap_col in range(3):
        window = padded[:, :, 2 - tap_col : 2 - tap_col + col_count].reshape(-1, channels)
        tap_term = lax.dot_general(
            window, weight[tap_row, tap_col], (((1,), (1,)), ((), ())), preferred_element_type=jnp.float32
        )
        total = tap_term if total is None else total + tap_term
    return total.reshape(-1, 1, col_count, weight.shape[2])


def per_device(
    latents, timesteps, gn_gain, gn_bias, conv_weight, conv_bias, temb_weight, cotangent
):
    images, slab_rows, col_count, channels = latents.shape
    groups = channels // CH_GROUP
    row_devices = lax.axis_size("rows")
    group_cells = slab_rows * row_devices * col_count * CH_GROUP
    positions = slab_rows * col_count
    values = latents.astype(jnp.float32)
    chan_mean = jnp.sum(values, axis=(1, 2)) / positions
    centered = values - chan_mean[:, None, None, :]
    chan_m2 = jnp.sum(centered * centered, axis=(1, 2))
    chan_mean_g = chan_mean.reshape(images, groups, CH_GROUP)
    local_mean = jnp.mean(chan_mean_g, axis=2)
    spread = chan_mean_g - local_mean[:, :, None]
    local_m2 = jnp.sum(chan_m2.reshape(images, groups, CH_GROUP), axis=2) + positions * jnp.sum(
        spread * spread, axis=2
    )
    group_mean, group_m2, _ = merge_stats(local_mean, local_m2, positions * CH_GROUP, "rows", ())
    inv_std = lax.rsqrt(group_m2 / group_cells + NORM_EPS)
    mean_ch = jnp.repeat(group_mean, CH_GROUP, axis=1)[:, None, None, :]
    rstd_ch = jnp.repeat(inv_std, CH_GROUP, axis=1)[:, None, None, :]
    normalized = (values - mean_ch) * rstd_ch
    pre_act = normalized * gn_gain + gn_bias
    hidden = jax.nn.silu(pre_act).astype(jnp.bfloat16)
    pair = jnp.stack([hidden, cotangent])
    pair, grad_in = lax.optimization_barrier((pair, cotangent))
    both_ext = padded_2(pair, (("rows", 2),), 1)
    no_rim = jnp.pad(grad_in, ((0, 0), (1, 1), (0, 0), (0, 0)))
    interior_grad = conv_taps(no_rim, conv_weight, slab_rows, col_count, True)
    both_ext, interior_grad = lax.optimization_barrier((both_ext, interior_grad))
    extended = both_ext[0]
    grad_rim = both_ext[1]
    top_fix = edge_taps(grad_rim[:, :1], conv_weight, 2, col_count)
    bottom_fix = edge_taps(grad_rim[:, slab_rows + 1 :], conv_weight, 0, col_count)
    hidden_grad = (
        interior_grad
        + jnp.pad(top_fix, ((0, 0), (0, slab_rows - 1), (0, 0), (0, 0)))
        + jnp.pad(bottom_fix, ((0, 0), (slab_rows - 1, 0), (0, 0), (0, 0)))
    )
    temb_features = jax.nn.silu(sinusoid(timesteps, temb_weight.shape[0])).astype(jnp.bfloat16)
    time_shift = jnp.dot(temb_features, temb_weight, preferred_element_type=jnp.float32)
    features = conv_taps(extended, conv_weight, slab_rows, col_count, False)
    features_out = (features + conv_bias + time_shift[:, None, None, :]).astype(jnp.bfloat16)
    sigmoid_act = jax.nn.sigmoid(pre_act)
    act_grad = hidden_grad * sigmoid_act * (1.0 + pre_act * (1.0 - sigmoid_act))
    chan_weighted = jnp.sum(act_grad * normalized, axis=(1, 2))
    chan_plain = jnp.sum(act_grad, axis=(1, 2))
    chan_output = jnp.sum(cotangent.astype(jnp.float32), axis=(1, 2))
    row_sums = all_sum(jnp.stack([chan_weighted, chan_plain, chan_output], axis=1), "rows")
    row_weighted, row_plain = row_sums[:, 0], row_sums[:, 1]
    first_sum = jnp.sum((row_plain * gn_gain).reshape(images, groups, CH_GROUP), axis=2)
    second_sum = jnp.sum((row_weighted * gn_gain).reshape(images, groups, CH_GROUP), axis=2)
    param_sums = all_sum(jnp.sum(row_sums, axis=0), "dp")
    first_ch = jnp.repeat(first_sum / group_cells, CH_GROUP, axis=1)[:, None, None, :]
    second_ch = jnp.repeat(second_sum / group_cells, CH_GROUP, axis=1)[:, None, None, :]
    input_grad = rstd_ch * (act_grad * gn_gain - first_ch - normalized * second_ch)
    input_grad = input_grad.astype(jnp.bfloat16)
    grad_scale = 1.0 / math.sqrt(images * lax.axis_size("dp") * slab_rows * row_devices * col_count)
    return (features_out, input_grad, param_sums * grad_scale)


def solution(mesh):
    placed = (
        P("dp", "rows", None, None),
        P("dp"),
        P(),
        P(),
        P(),
        P(),
        P(),
        P("dp", "rows", None, None),
    )
    return jax.shard_map(
        per_device,
        mesh=mesh,
        in_specs=placed,
        out_specs=(P("dp", "rows", None, None), P("dp", "rows", None, None), P()),
        check_vma=False,
    )
```

```python
import math

import jax
import jax.numpy as jnp
from jax import lax
from jax.experimental.scheduling_groups import scheduling_group
from jax.sharding import PartitionSpec as P

CH_GROUP = 40


NORM_EPS = 1e-05


def padded_2(cells, sides, width):
    for axis, dim in sides:
        count = lax.axis_size(axis)
        ends = count - 1
        head = lax.slice_in_dim(cells, 0, width, axis=dim)
        tail = lax.slice_in_dim(cells, cells.shape[dim] - width, cells.shape[dim], axis=dim)
        cells = jnp.concatenate(
            [
                lax.ppermute(tail, axis, [(i, (i + 1) % count) for i in range(ends)]),
                cells,
                lax.ppermute(head, axis, [((i + 1) % count, i) for i in range(ends)]),
            ],
            axis=dim,
        )
    return cells


def is_pow2(count):
    return count & (count - 1) == 0


def all_sum(value, axis):
    count = lax.axis_size(axis)
    if not is_pow2(count):
        return lax.psum(value, axis)
    step = 1
    while step < count:
        other = lax.ppermute(value, axis, [(i, i ^ step) for i in range(count)])
        value = value + other
        step *= 2
    return value


def merge_stats(mean, m2, cells, axis):
    count = lax.axis_size(axis)
    if not is_pow2(count):
        means = lax.all_gather(mean, axis)
        total_mean = jnp.mean(means, axis=0)
        spread = means - total_mean
        return total_mean, jnp.sum(lax.all_gather(m2, axis), axis=0) + cells * jnp.sum(spread * spread, axis=0)
    value = jnp.stack([mean, m2])
    step = 1
    while step < count:
        other = lax.ppermute(value, axis, [(i, i ^ step) for i in range(count)])
        delta = other[0] - value[0]
        value = jnp.stack(
            [(value[0] + other[0]) * 0.5, value[1] + other[1] + delta * delta * (cells * step * 0.5)]
        )
        step *= 2
    return value[0], value[1]


def sinusoid(steps, embed_dim):
    half_dim = embed_dim // 2
    frequencies = jnp.exp(-math.log(10000.0) * jnp.arange(half_dim).astype(jnp.float32) / half_dim)
    angles = steps.astype(jnp.float32)[:, None] * frequencies[None, :]
    return jnp.concatenate([jnp.cos(angles), jnp.sin(angles)], axis=1)


def with_rim(field):
    return padded_2(field, (("rows", 2),), 1)


def conv_taps(extended, weight, slab_rows, col_count, backward):
    padded = jnp.pad(extended, ((0, 0), (0, 0), (1, 1), (0, 0)))
    channels = padded.shape[3]
    total = None
    for tap_row in range(3):
        for tap_col in range(3):
            if backward:
                row_start, col_start = (2 - tap_row, 2 - tap_col)
                dims = (((1,), (1,)), ((), ()))
            else:
                row_start, col_start = (tap_row, tap_col)
                dims = (((1,), (0,)), ((), ()))
            window = padded[
                :, row_start : row_start + slab_rows, col_start : col_start + col_count
            ].reshape(-1, channels)
            tap_term = lax.dot_general(
                window, weight[tap_row, tap_col], dims, preferred_element_type=jnp.float32
            )
            total = tap_term if total is None else total + tap_term
    return total.reshape(-1, slab_rows, col_count, weight.shape[3])


def edge_taps(edge_row, weight, tap_row, col_count):
    padded = jnp.pad(edge_row, ((0, 0), (0, 0), (1, 1), (0, 0)))
    channels = padded.shape[3]
    total = None
    for tap_col in range(3):
        window = padded[:, :, 2 - tap_col : 2 - tap_col + col_count].reshape(-1, channels)
        tap_term = lax.dot_general(
            window, weight[tap_row, tap_col], (((1,), (1,)), ((), ())), preferred_element_type=jnp.float32
        )
        total = tap_term if total is None else total + tap_term
    return total.reshape(-1, 1, col_count, weight.shape[2])


def halo_front(latents, cotangent, conv_weight):
    slab_rows, col_count = latents.shape[1], latents.shape[2]
    both_ext = with_rim(jnp.stack([latents, cotangent]))
    no_rim = jnp.pad(cotangent, ((0, 0), (1, 1), (0, 0), (0, 0)))
    interior_grad = conv_taps(no_rim, conv_weight, slab_rows, col_count, True)
    return both_ext, interior_grad


def per_device(
    latents, timesteps, gn_gain, gn_bias, conv_weight, conv_bias, temb_weight, cotangent
):
    images, slab_rows, col_count, channels = latents.shape
    groups = channels // CH_GROUP
    row_devices = lax.axis_size("rows")
    group_cells = slab_rows * row_devices * col_count * CH_GROUP
    positions = slab_rows * col_count
    both_ext, interior_grad = scheduling_group("halo")(halo_front)(latents, cotangent, conv_weight)
    row_index = lax.axis_index("rows")
    inside = jnp.concatenate(
        [
            jnp.where(row_index > 0, 1.0, 0.0)[None],
            jnp.ones((slab_rows,), jnp.float32),
            jnp.where(row_index < row_devices - 1, 1.0, 0.0)[None],
        ]
    )[None, :, None, None]
    values = latents.astype(jnp.float32)
    chan_mean = jnp.sum(values, axis=(1, 2)) / positions
    centered = values - chan_mean[:, None, None, :]
    chan_m2 = jnp.sum(centered * centered, axis=(1, 2))
    chan_mean_g = chan_mean.reshape(images, groups, CH_GROUP)
    local_mean = jnp.mean(chan_mean_g, axis=2)
    spread = chan_mean_g - local_mean[:, :, None]
    local_m2 = jnp.sum(chan_m2.reshape(images, groups, CH_GROUP), axis=2) + positions * jnp.sum(
        spread * spread, axis=2
    )
    group_mean, group_m2 = merge_stats(local_mean, local_m2, positions * CH_GROUP, "rows")
    inv_std = lax.rsqrt(group_m2 / group_cells + NORM_EPS)
    mean_ch = jnp.repeat(group_mean, CH_GROUP, axis=1)[:, None, None, :]
    rstd_ch = jnp.repeat(inv_std, CH_GROUP, axis=1)[:, None, None, :]
    normalized_ext = (both_ext[0].astype(jnp.float32) - mean_ch) * rstd_ch
    pre_act_ext = normalized_ext * gn_gain + gn_bias
    extended = (jax.nn.silu(pre_act_ext) * inside).astype(jnp.bfloat16)
    normalized = normalized_ext[:, 1 : 1 + slab_rows]
    pre_act = pre_act_ext[:, 1 : 1 + slab_rows]
    temb_features = jax.nn.silu(sinusoid(timesteps, temb_weight.shape[0])).astype(jnp.bfloat16)
    time_shift = jnp.dot(temb_features, temb_weight, preferred_element_type=jnp.float32)
    features = conv_taps(extended, conv_weight, slab_rows, col_count, False)
    features_out = (features + conv_bias + time_shift[:, None, None, :]).astype(jnp.bfloat16)
    grad_rim = both_ext[1]
    top_fix = edge_taps(grad_rim[:, :1], conv_weight, 2, col_count)
    bottom_fix = edge_taps(grad_rim[:, slab_rows + 1 :], conv_weight, 0, col_count)
    hidden_grad = (
        interior_grad
        + jnp.pad(top_fix, ((0, 0), (0, slab_rows - 1), (0, 0), (0, 0)))
        + jnp.pad(bottom_fix, ((0, 0), (slab_rows - 1, 0), (0, 0), (0, 0)))
    )
    sigmoid_act = jax.nn.sigmoid(pre_act)
    act_grad = hidden_grad * sigmoid_act * (1.0 + pre_act * (1.0 - sigmoid_act))
    chan_weighted = jnp.sum(act_grad * normalized, axis=(1, 2))
    chan_plain = jnp.sum(act_grad, axis=(1, 2))
    chan_output = jnp.sum(cotangent.astype(jnp.float32), axis=(1, 2))
    row_sums = all_sum(jnp.stack([chan_weighted, chan_plain, chan_output], axis=1), "rows")
    row_weighted, row_plain = row_sums[:, 0], row_sums[:, 1]
    first_sum = jnp.sum((row_plain * gn_gain).reshape(images, groups, CH_GROUP), axis=2)
    second_sum = jnp.sum((row_weighted * gn_gain).reshape(images, groups, CH_GROUP), axis=2)
    param_sums = all_sum(jnp.sum(row_sums, axis=0), "dp")
    first_ch = jnp.repeat(first_sum / group_cells, CH_GROUP, axis=1)[:, None, None, :]
    second_ch = jnp.repeat(second_sum / group_cells, CH_GROUP, axis=1)[:, None, None, :]
    input_grad = rstd_ch * (act_grad * gn_gain - first_ch - normalized * second_ch)
    input_grad = input_grad.astype(jnp.bfloat16)
    grad_scale = 1.0 / math.sqrt(images * lax.axis_size("dp") * slab_rows * row_devices * col_count)
    return (features_out, input_grad, param_sums * grad_scale)


def solution(mesh):
    placed = (
        P("dp", "rows", None, None),
        P("dp"),
        P(),
        P(),
        P(),
        P(),
        P(),
        P("dp", "rows", None, None),
    )
    return jax.shard_map(
        per_device,
        mesh=mesh,
        in_specs=placed,
        out_specs=(P("dp", "rows", None, None), P("dp", "rows", None, None), P()),
        check_vma=False,
    )
```

```python
import math

import jax
import jax.numpy as jnp
from jax import lax
from jax.sharding import PartitionSpec as P

CH_GROUP = 40


NORM_EPS = 1e-05


def padded_2(cells, sides, width):
    for axis, dim in sides:
        count = lax.axis_size(axis)
        ends = count - 1
        head = lax.slice_in_dim(cells, 0, width, axis=dim)
        tail = lax.slice_in_dim(cells, cells.shape[dim] - width, cells.shape[dim], axis=dim)
        cells = jnp.concatenate(
            [
                lax.ppermute(tail, axis, [(i, (i + 1) % count) for i in range(ends)]),
                cells,
                lax.ppermute(head, axis, [((i + 1) % count, i) for i in range(ends)]),
            ],
            axis=dim,
        )
    return cells


def is_pow2(count):
    return count & (count - 1) == 0


def all_sum(value, axis):
    count = lax.axis_size(axis)
    if not is_pow2(count):
        return lax.psum(value, axis)
    step = 1
    while step < count:
        other = lax.ppermute(value, axis, [(i, i ^ step) for i in range(count)])
        value = value + other
        step *= 2
    return value


def merge_stats(mean, m2, cells, axis):
    count = lax.axis_size(axis)
    if not is_pow2(count):
        means = lax.all_gather(mean, axis)
        total_mean = jnp.mean(means, axis=0)
        spread = means - total_mean
        return total_mean, jnp.sum(lax.all_gather(m2, axis), axis=0) + cells * jnp.sum(spread * spread, axis=0)
    value = jnp.stack([mean, m2])
    step = 1
    while step < count:
        other = lax.ppermute(value, axis, [(i, i ^ step) for i in range(count)])
        delta = other[0] - value[0]
        value = jnp.stack(
            [(value[0] + other[0]) * 0.5, value[1] + other[1] + delta * delta * (cells * step * 0.5)]
        )
        step *= 2
    return value[0], value[1]


def sinusoid(steps, embed_dim):
    half_dim = embed_dim // 2
    frequencies = jnp.exp(-math.log(10000.0) * jnp.arange(half_dim).astype(jnp.float32) / half_dim)
    angles = steps.astype(jnp.float32)[:, None] * frequencies[None, :]
    return jnp.concatenate([jnp.cos(angles), jnp.sin(angles)], axis=1)


def with_rim(field):
    return padded_2(field, (("rows", 2),), 1)


def conv_taps(extended, weight, slab_rows, col_count, backward):
    padded = jnp.pad(extended, ((0, 0), (0, 0), (1, 1), (0, 0)))
    channels = padded.shape[3]
    total = None
    for tap_row in range(3):
        for tap_col in range(3):
            if backward:
                row_start, col_start = (2 - tap_row, 2 - tap_col)
                dims = (((1,), (1,)), ((), ()))
            else:
                row_start, col_start = (tap_row, tap_col)
                dims = (((1,), (0,)), ((), ()))
            window = padded[
                :, row_start : row_start + slab_rows, col_start : col_start + col_count
            ].reshape(-1, channels)
            tap_term = lax.dot_general(
                window, weight[tap_row, tap_col], dims, preferred_element_type=jnp.float32
            )
            total = tap_term if total is None else total + tap_term
    return total.reshape(-1, slab_rows, col_count, weight.shape[3])


def edge_taps(edge_row, weight, tap_row, col_count):
    padded = jnp.pad(edge_row, ((0, 0), (0, 0), (1, 1), (0, 0)))
    channels = padded.shape[3]
    total = None
    for tap_col in range(3):
        window = padded[:, :, 2 - tap_col : 2 - tap_col + col_count].reshape(-1, channels)
        tap_term = lax.dot_general(
            window, weight[tap_row, tap_col], (((1,), (1,)), ((), ())), preferred_element_type=jnp.float32
        )
        total = tap_term if total is None else total + tap_term
    return total.reshape(-1, 1, col_count, weight.shape[2])


def halo_front(latents, cotangent, conv_weight):
    slab_rows, col_count = latents.shape[1], latents.shape[2]
    both_ext = with_rim(jnp.stack([latents, cotangent]))
    no_rim = jnp.pad(cotangent, ((0, 0), (1, 1), (0, 0), (0, 0)))
    interior_grad = conv_taps(no_rim, conv_weight, slab_rows, col_count, True)
    return both_ext, interior_grad


def per_device(
    latents, timesteps, gn_gain, gn_bias, conv_weight, conv_bias, temb_weight, cotangent
):
    images, slab_rows, col_count, channels = latents.shape
    groups = channels // CH_GROUP
    row_devices = lax.axis_size("rows")
    group_cells = slab_rows * row_devices * col_count * CH_GROUP
    positions = slab_rows * col_count
    both_ext, interior_grad = halo_front(latents, cotangent, conv_weight)
    row_index = lax.axis_index("rows")
    inside = jnp.concatenate(
        [
            jnp.where(row_index > 0, 1.0, 0.0)[None],
            jnp.ones((slab_rows,), jnp.float32),
            jnp.where(row_index < row_devices - 1, 1.0, 0.0)[None],
        ]
    )[None, :, None, None]
    values = latents.astype(jnp.float32)
    chan_mean = jnp.sum(values, axis=(1, 2)) / positions
    centered = values - chan_mean[:, None, None, :]
    chan_m2 = jnp.sum(centered * centered, axis=(1, 2))
    chan_mean_g = chan_mean.reshape(images, groups, CH_GROUP)
    local_mean = jnp.mean(chan_mean_g, axis=2)
    spread = chan_mean_g - local_mean[:, :, None]
    local_m2 = jnp.sum(chan_m2.reshape(images, groups, CH_GROUP), axis=2) + positions * jnp.sum(
        spread * spread, axis=2
    )
    local_mean, local_m2, interior_grad, both_ext = lax.optimization_barrier(
        (local_mean, local_m2, interior_grad, both_ext)
    )
    group_mean, group_m2 = merge_stats(local_mean, local_m2, positions * CH_GROUP, "rows")
    inv_std = lax.rsqrt(group_m2 / group_cells + NORM_EPS)
    mean_ch = jnp.repeat(group_mean, CH_GROUP, axis=1)[:, None, None, :]
    rstd_ch = jnp.repeat(inv_std, CH_GROUP, axis=1)[:, None, None, :]
    normalized_ext = (both_ext[0].astype(jnp.float32) - mean_ch) * rstd_ch
    pre_act_ext = normalized_ext * gn_gain + gn_bias
    extended = (jax.nn.silu(pre_act_ext) * inside).astype(jnp.bfloat16)
    normalized = normalized_ext[:, 1 : 1 + slab_rows]
    pre_act = pre_act_ext[:, 1 : 1 + slab_rows]
    temb_features = jax.nn.silu(sinusoid(timesteps, temb_weight.shape[0])).astype(jnp.bfloat16)
    time_shift = jnp.dot(temb_features, temb_weight, preferred_element_type=jnp.float32)
    features = conv_taps(extended, conv_weight, slab_rows, col_count, False)
    features_out = (features + conv_bias + time_shift[:, None, None, :]).astype(jnp.bfloat16)
    grad_rim = both_ext[1]
    top_fix = edge_taps(grad_rim[:, :1], conv_weight, 2, col_count)
    bottom_fix = edge_taps(grad_rim[:, slab_rows + 1 :], conv_weight, 0, col_count)
    hidden_grad = (
        interior_grad
        + jnp.pad(top_fix, ((0, 0), (0, slab_rows - 1), (0, 0), (0, 0)))
        + jnp.pad(bottom_fix, ((0, 0), (slab_rows - 1, 0), (0, 0), (0, 0)))
    )
    sigmoid_act = jax.nn.sigmoid(pre_act)
    act_grad = hidden_grad * sigmoid_act * (1.0 + pre_act * (1.0 - sigmoid_act))
    chan_weighted = jnp.sum(act_grad * normalized, axis=(1, 2))
    chan_plain = jnp.sum(act_grad, axis=(1, 2))
    chan_output = jnp.sum(cotangent.astype(jnp.float32), axis=(1, 2))
    row_sums = all_sum(jnp.stack([chan_weighted, chan_plain, chan_output], axis=1), "rows")
    row_weighted, row_plain = row_sums[:, 0], row_sums[:, 1]
    first_sum = jnp.sum((row_plain * gn_gain).reshape(images, groups, CH_GROUP), axis=2)
    second_sum = jnp.sum((row_weighted * gn_gain).reshape(images, groups, CH_GROUP), axis=2)
    param_sums = all_sum(jnp.sum(row_sums, axis=0), "dp")
    first_ch = jnp.repeat(first_sum / group_cells, CH_GROUP, axis=1)[:, None, None, :]
    second_ch = jnp.repeat(second_sum / group_cells, CH_GROUP, axis=1)[:, None, None, :]
    input_grad = rstd_ch * (act_grad * gn_gain - first_ch - normalized * second_ch)
    input_grad = input_grad.astype(jnp.bfloat16)
    grad_scale = 1.0 / math.sqrt(images * lax.axis_size("dp") * slab_rows * row_devices * col_count)
    return (features_out, input_grad, param_sums * grad_scale)


def solution(mesh):
    placed = (
        P("dp", "rows", None, None),
        P("dp"),
        P(),
        P(),
        P(),
        P(),
        P(),
        P("dp", "rows", None, None),
    )
    return jax.shard_map(
        per_device,
        mesh=mesh,
        in_specs=placed,
        out_specs=(P("dp", "rows", None, None), P("dp", "rows", None, None), P()),
        check_vma=False,
    )
```

```python
import math

import jax
import jax.numpy as jnp
from jax import lax
from jax.sharding import PartitionSpec as P

CH_GROUP = 40


NORM_EPS = 1e-05


def padded_2(cells, sides, width):
    for axis, dim in sides:
        count = lax.axis_size(axis)
        ends = count - 1
        head = lax.slice_in_dim(cells, 0, width, axis=dim)
        tail = lax.slice_in_dim(cells, cells.shape[dim] - width, cells.shape[dim], axis=dim)
        cells = jnp.concatenate(
            [
                lax.ppermute(tail, axis, [(i, (i + 1) % count) for i in range(ends)]),
                cells,
                lax.ppermute(head, axis, [((i + 1) % count, i) for i in range(ends)]),
            ],
            axis=dim,
        )
    return cells


def is_pow2(count):
    return count & (count - 1) == 0


def all_sum(value, axis):
    count = lax.axis_size(axis)
    if not is_pow2(count):
        return lax.psum(value, axis)
    step = 1
    while step < count:
        other = lax.ppermute(value, axis, [(i, i ^ step) for i in range(count)])
        value = value + other
        step *= 2
    return value


def merge_stats(mean, m2, cells, axis):
    count = lax.axis_size(axis)
    if not is_pow2(count):
        means = lax.all_gather(mean, axis)
        total_mean = jnp.mean(means, axis=0)
        spread = means - total_mean
        return total_mean, jnp.sum(lax.all_gather(m2, axis), axis=0) + cells * jnp.sum(spread * spread, axis=0)
    value = jnp.stack([mean, m2])
    step = count // 2
    size = 1
    while step >= 1:
        other = lax.ppermute(value, axis, [(i, i ^ step) for i in range(count)])
        delta = other[0] - value[0]
        value = jnp.stack(
            [(value[0] + other[0]) * 0.5, value[1] + other[1] + delta * delta * (cells * size * 0.5)]
        )
        step //= 2
        size *= 2
    return value[0], value[1]


def sinusoid(steps, embed_dim):
    half_dim = embed_dim // 2
    frequencies = jnp.exp(-math.log(10000.0) * jnp.arange(half_dim).astype(jnp.float32) / half_dim)
    angles = steps.astype(jnp.float32)[:, None] * frequencies[None, :]
    return jnp.concatenate([jnp.cos(angles), jnp.sin(angles)], axis=1)


def with_rim(field):
    return padded_2(field, (("rows", 2),), 1)


def conv_taps(extended, weight, slab_rows, col_count, backward):
    padded = jnp.pad(extended, ((0, 0), (0, 0), (1, 1), (0, 0)))
    channels = padded.shape[3]
    total = None
    for tap_row in range(3):
        for tap_col in range(3):
            if backward:
                row_start, col_start = (2 - tap_row, 2 - tap_col)
                dims = (((1,), (1,)), ((), ()))
            else:
                row_start, col_start = (tap_row, tap_col)
                dims = (((1,), (0,)), ((), ()))
            window = padded[
                :, row_start : row_start + slab_rows, col_start : col_start + col_count
            ].reshape(-1, channels)
            tap_term = lax.dot_general(
                window, weight[tap_row, tap_col], dims, preferred_element_type=jnp.float32
            )
            total = tap_term if total is None else total + tap_term
    return total.reshape(-1, slab_rows, col_count, weight.shape[3])


def per_device(
    latents, timesteps, gn_gain, gn_bias, conv_weight, conv_bias, temb_weight, cotangent
):
    images, slab_rows, col_count, channels = latents.shape
    groups = channels // CH_GROUP
    row_devices = lax.axis_size("rows")
    group_cells = slab_rows * row_devices * col_count * CH_GROUP
    positions = slab_rows * col_count
    both_ext = with_rim(jnp.stack([latents, cotangent]))
    row_index = lax.axis_index("rows")
    inside = jnp.concatenate(
        [
            jnp.where(row_index > 0, 1.0, 0.0)[None],
            jnp.ones((slab_rows,), jnp.float32),
            jnp.where(row_index < row_devices - 1, 1.0, 0.0)[None],
        ]
    )[None, :, None, None]
    values = latents.astype(jnp.float32)
    chan_mean = jnp.sum(values, axis=(1, 2)) / positions
    centered = values - chan_mean[:, None, None, :]
    chan_m2 = jnp.sum(centered * centered, axis=(1, 2))
    chan_mean_g = chan_mean.reshape(images, groups, CH_GROUP)
    local_mean = jnp.mean(chan_mean_g, axis=2)
    spread = chan_mean_g - local_mean[:, :, None]
    local_m2 = jnp.sum(chan_m2.reshape(images, groups, CH_GROUP), axis=2) + positions * jnp.sum(
        spread * spread, axis=2
    )
    group_mean, group_m2 = merge_stats(local_mean, local_m2, positions * CH_GROUP, "rows")
    inv_std = lax.rsqrt(group_m2 / group_cells + NORM_EPS)
    mean_ch = jnp.repeat(group_mean, CH_GROUP, axis=1)[:, None, None, :]
    rstd_ch = jnp.repeat(inv_std, CH_GROUP, axis=1)[:, None, None, :]
    normalized_ext = (both_ext[0].astype(jnp.float32) - mean_ch) * rstd_ch
    pre_act_ext = normalized_ext * gn_gain + gn_bias
    extended = (jax.nn.silu(pre_act_ext) * inside).astype(jnp.bfloat16)
    normalized = normalized_ext[:, 1 : 1 + slab_rows]
    pre_act = pre_act_ext[:, 1 : 1 + slab_rows]
    temb_features = jax.nn.silu(sinusoid(timesteps, temb_weight.shape[0])).astype(jnp.bfloat16)
    time_shift = jnp.dot(temb_features, temb_weight, preferred_element_type=jnp.float32)
    features = conv_taps(extended, conv_weight, slab_rows, col_count, False)
    features_out = (features + conv_bias + time_shift[:, None, None, :]).astype(jnp.bfloat16)
    hidden_grad = conv_taps(both_ext[1], conv_weight, slab_rows, col_count, True)
    sigmoid_act = jax.nn.sigmoid(pre_act)
    act_grad = hidden_grad * sigmoid_act * (1.0 + pre_act * (1.0 - sigmoid_act))
    chan_weighted = jnp.sum(act_grad * normalized, axis=(1, 2))
    chan_plain = jnp.sum(act_grad, axis=(1, 2))
    chan_output = jnp.sum(cotangent.astype(jnp.float32), axis=(1, 2))
    row_sums = all_sum(jnp.stack([chan_weighted, chan_plain, chan_output], axis=1), "rows")
    row_weighted, row_plain = row_sums[:, 0], row_sums[:, 1]
    first_sum = jnp.sum((row_plain * gn_gain).reshape(images, groups, CH_GROUP), axis=2)
    second_sum = jnp.sum((row_weighted * gn_gain).reshape(images, groups, CH_GROUP), axis=2)
    param_sums = all_sum(jnp.sum(row_sums, axis=0), "dp")
    first_ch = jnp.repeat(first_sum / group_cells, CH_GROUP, axis=1)[:, None, None, :]
    second_ch = jnp.repeat(second_sum / group_cells, CH_GROUP, axis=1)[:, None, None, :]
    input_grad = rstd_ch * (act_grad * gn_gain - first_ch - normalized * second_ch)
    input_grad = input_grad.astype(jnp.bfloat16)
    grad_scale = 1.0 / math.sqrt(images * lax.axis_size("dp") * slab_rows * row_devices * col_count)
    return (features_out, input_grad, param_sums * grad_scale)


def solution(mesh):
    placed = (
        P("dp", "rows", None, None),
        P("dp"),
        P(),
        P(),
        P(),
        P(),
        P(),
        P("dp", "rows", None, None),
    )
    return jax.shard_map(
        per_device,
        mesh=mesh,
        in_specs=placed,
        out_specs=(P("dp", "rows", None, None), P("dp", "rows", None, None), P()),
        check_vma=False,
    )
```

```python
import math

import jax
import jax.numpy as jnp
from jax import lax
from jax.sharding import PartitionSpec as P

CH_GROUP = 40


NORM_EPS = 1e-05


def padded_2(cells, sides, width):
    for axis, dim in sides:
        count = lax.axis_size(axis)
        ends = count - 1
        head = lax.slice_in_dim(cells, 0, width, axis=dim)
        tail = lax.slice_in_dim(cells, cells.shape[dim] - width, cells.shape[dim], axis=dim)
        cells = jnp.concatenate(
            [
                lax.ppermute(tail, axis, [(i, (i + 1) % count) for i in range(ends)]),
                cells,
                lax.ppermute(head, axis, [((i + 1) % count, i) for i in range(ends)]),
            ],
            axis=dim,
        )
    return cells


def is_pow2(count):
    return count & (count - 1) == 0


def all_sum(value, axis):
    count = lax.axis_size(axis)
    if not is_pow2(count):
        return lax.psum(value, axis)
    step = 1
    while step < count:
        other = lax.ppermute(value, axis, [(i, i ^ step) for i in range(count)])
        value = value + other
        step *= 2
    return value


def merge_stats(mean, m2, cells, axis):
    count = lax.axis_size(axis)
    if not is_pow2(count):
        means = lax.all_gather(mean, axis)
        total_mean = jnp.mean(means, axis=0)
        spread = means - total_mean
        return total_mean, jnp.sum(lax.all_gather(m2, axis), axis=0) + cells * jnp.sum(spread * spread, axis=0)
    value = jnp.stack([mean, m2])
    step = count // 2
    size = 1
    while step >= 1:
        other = lax.ppermute(value, axis, [(i, i ^ step) for i in range(count)])
        delta = other[0] - value[0]
        value = jnp.stack(
            [(value[0] + other[0]) * 0.5, value[1] + other[1] + delta * delta * (cells * size * 0.5)]
        )
        step //= 2
        size *= 2
    return value[0], value[1]


def position_sum(field, exact=False):
    flat = field.reshape(field.shape[0], -1, field.shape[-1])
    ones = jnp.ones((flat.shape[1],), field.dtype)
    precision = lax.Precision.HIGHEST if exact else None
    return jnp.einsum(
        "p,ipc->ic", ones, flat, precision=precision, preferred_element_type=jnp.float32
    )


def sinusoid(steps, embed_dim):
    half_dim = embed_dim // 2
    frequencies = jnp.exp(-math.log(10000.0) * jnp.arange(half_dim).astype(jnp.float32) / half_dim)
    angles = steps.astype(jnp.float32)[:, None] * frequencies[None, :]
    return jnp.concatenate([jnp.cos(angles), jnp.sin(angles)], axis=1)


def with_rim(field):
    return padded_2(field, (("rows", 2),), 1)


def conv_taps(extended, weight, slab_rows, col_count, backward):
    padded = jnp.pad(extended, ((0, 0), (0, 0), (1, 1), (0, 0)))
    channels = padded.shape[3]
    total = None
    for tap_row in range(3):
        for tap_col in range(3):
            if backward:
                row_start, col_start = (2 - tap_row, 2 - tap_col)
                dims = (((1,), (1,)), ((), ()))
            else:
                row_start, col_start = (tap_row, tap_col)
                dims = (((1,), (0,)), ((), ()))
            window = padded[
                :, row_start : row_start + slab_rows, col_start : col_start + col_count
            ].reshape(-1, channels)
            tap_term = lax.dot_general(
                window, weight[tap_row, tap_col], dims, preferred_element_type=jnp.float32
            )
            total = tap_term if total is None else total + tap_term
    return total.reshape(-1, slab_rows, col_count, weight.shape[3])


def per_device(
    latents, timesteps, gn_gain, gn_bias, conv_weight, conv_bias, temb_weight, cotangent
):
    images, slab_rows, col_count, channels = latents.shape
    groups = channels // CH_GROUP
    row_devices = lax.axis_size("rows")
    group_cells = slab_rows * row_devices * col_count * CH_GROUP
    positions = slab_rows * col_count
    both_ext = with_rim(jnp.stack([latents, cotangent]))
    row_index = lax.axis_index("rows")
    inside = jnp.concatenate(
        [
            jnp.where(row_index > 0, 1.0, 0.0)[None],
            jnp.ones((slab_rows,), jnp.float32),
            jnp.where(row_index < row_devices - 1, 1.0, 0.0)[None],
        ]
    )[None, :, None, None]
    values = latents.astype(jnp.float32)
    chan_mean = position_sum(latents) / positions
    centered = values - chan_mean[:, None, None, :]
    chan_m2 = position_sum(centered * centered, True)
    chan_mean_g = chan_mean.reshape(images, groups, CH_GROUP)
    local_mean = jnp.mean(chan_mean_g, axis=2)
    spread = chan_mean_g - local_mean[:, :, None]
    local_m2 = jnp.sum(chan_m2.reshape(images, groups, CH_GROUP), axis=2) + positions * jnp.sum(
        spread * spread, axis=2
    )
    group_mean, group_m2 = merge_stats(local_mean, local_m2, positions * CH_GROUP, "rows")
    inv_std = lax.rsqrt(group_m2 / group_cells + NORM_EPS)
    mean_ch = jnp.repeat(group_mean, CH_GROUP, axis=1)[:, None, None, :]
    rstd_ch = jnp.repeat(inv_std, CH_GROUP, axis=1)[:, None, None, :]
    normalized_ext = (both_ext[0].astype(jnp.float32) - mean_ch) * rstd_ch
    pre_act_ext = normalized_ext * gn_gain + gn_bias
    extended = (jax.nn.silu(pre_act_ext) * inside).astype(jnp.bfloat16)
    normalized = normalized_ext[:, 1 : 1 + slab_rows]
    pre_act = pre_act_ext[:, 1 : 1 + slab_rows]
    temb_features = jax.nn.silu(sinusoid(timesteps, temb_weight.shape[0])).astype(jnp.bfloat16)
    time_shift = jnp.dot(temb_features, temb_weight, preferred_element_type=jnp.float32)
    features = conv_taps(extended, conv_weight, slab_rows, col_count, False)
    features_out = (features + conv_bias + time_shift[:, None, None, :]).astype(jnp.bfloat16)
    hidden_grad = conv_taps(both_ext[1], conv_weight, slab_rows, col_count, True)
    sigmoid_act = jax.nn.sigmoid(pre_act)
    act_grad = hidden_grad * sigmoid_act * (1.0 + pre_act * (1.0 - sigmoid_act))
    chan_weighted = position_sum(act_grad * normalized, True)
    chan_plain = position_sum(act_grad, True)
    chan_output = position_sum(cotangent)
    row_sums = all_sum(jnp.stack([chan_weighted, chan_plain, chan_output], axis=1), "rows")
    row_weighted, row_plain = row_sums[:, 0], row_sums[:, 1]
    first_sum = jnp.sum((row_plain * gn_gain).reshape(images, groups, CH_GROUP), axis=2)
    second_sum = jnp.sum((row_weighted * gn_gain).reshape(images, groups, CH_GROUP), axis=2)
    param_sums = all_sum(jnp.sum(row_sums, axis=0), "dp")
    first_ch = jnp.repeat(first_sum / group_cells, CH_GROUP, axis=1)[:, None, None, :]
    second_ch = jnp.repeat(second_sum / group_cells, CH_GROUP, axis=1)[:, None, None, :]
    input_grad = rstd_ch * (act_grad * gn_gain - first_ch - normalized * second_ch)
    input_grad = input_grad.astype(jnp.bfloat16)
    grad_scale = 1.0 / math.sqrt(images * lax.axis_size("dp") * slab_rows * row_devices * col_count)
    return (features_out, input_grad, param_sums * grad_scale)


def solution(mesh):
    placed = (
        P("dp", "rows", None, None),
        P("dp"),
        P(),
        P(),
        P(),
        P(),
        P(),
        P("dp", "rows", None, None),
    )
    return jax.shard_map(
        per_device,
        mesh=mesh,
        in_specs=placed,
        out_specs=(P("dp", "rows", None, None), P("dp", "rows", None, None), P()),
        check_vma=False,
    )
```

```python
import math

import jax
import jax.numpy as jnp
from jax import lax
from jax.sharding import PartitionSpec as P

CH_GROUP = 40


NORM_EPS = 1e-05


def padded_2(cells, sides, width):
    for axis, dim in sides:
        count = lax.axis_size(axis)
        ends = count - 1
        head = lax.slice_in_dim(cells, 0, width, axis=dim)
        tail = lax.slice_in_dim(cells, cells.shape[dim] - width, cells.shape[dim], axis=dim)
        cells = jnp.concatenate(
            [
                lax.ppermute(tail, axis, [(i, (i + 1) % count) for i in range(ends)]),
                cells,
                lax.ppermute(head, axis, [((i + 1) % count, i) for i in range(ends)]),
            ],
            axis=dim,
        )
    return cells


def is_pow2(count):
    return count & (count - 1) == 0


def all_sum(value, axis):
    count = lax.axis_size(axis)
    if not is_pow2(count):
        return lax.psum(value, axis)
    step = count // 2
    while step >= 1:
        other = lax.ppermute(value, axis, [(i, i ^ step) for i in range(count)])
        value = value + other
        step //= 2
    return value


def merge_stats(mean, m2, cells, axis):
    count = lax.axis_size(axis)
    if not is_pow2(count):
        means = lax.all_gather(mean, axis)
        total_mean = jnp.mean(means, axis=0)
        spread = means - total_mean
        return total_mean, jnp.sum(lax.all_gather(m2, axis), axis=0) + cells * jnp.sum(spread * spread, axis=0)
    value = jnp.stack([mean, m2])
    step = count // 2
    size = 1
    while step >= 1:
        other = lax.ppermute(value, axis, [(i, i ^ step) for i in range(count)])
        delta = other[0] - value[0]
        value = jnp.stack(
            [(value[0] + other[0]) * 0.5, value[1] + other[1] + delta * delta * (cells * size * 0.5)]
        )
        step //= 2
        size *= 2
    return value[0], value[1]


def sinusoid(steps, embed_dim):
    half_dim = embed_dim // 2
    frequencies = jnp.exp(-math.log(10000.0) * jnp.arange(half_dim).astype(jnp.float32) / half_dim)
    angles = steps.astype(jnp.float32)[:, None] * frequencies[None, :]
    return jnp.concatenate([jnp.cos(angles), jnp.sin(angles)], axis=1)


def with_rim(field):
    return padded_2(field, (("rows", 2),), 1)


def conv_taps(extended, weight, slab_rows, col_count, backward):
    padded = jnp.pad(extended, ((0, 0), (0, 0), (1, 1), (0, 0)))
    channels = padded.shape[3]
    total = None
    for tap_row in range(3):
        for tap_col in range(3):
            if backward:
                row_start, col_start = (2 - tap_row, 2 - tap_col)
                dims = (((1,), (1,)), ((), ()))
            else:
                row_start, col_start = (tap_row, tap_col)
                dims = (((1,), (0,)), ((), ()))
            window = padded[
                :, row_start : row_start + slab_rows, col_start : col_start + col_count
            ].reshape(-1, channels)
            tap_term = lax.dot_general(
                window, weight[tap_row, tap_col], dims, preferred_element_type=jnp.float32
            )
            total = tap_term if total is None else total + tap_term
    return total.reshape(-1, slab_rows, col_count, weight.shape[3])


def per_device(
    latents, timesteps, gn_gain, gn_bias, conv_weight, conv_bias, temb_weight, cotangent
):
    images, slab_rows, col_count, channels = latents.shape
    groups = channels // CH_GROUP
    row_devices = lax.axis_size("rows")
    group_cells = slab_rows * row_devices * col_count * CH_GROUP
    positions = slab_rows * col_count
    both_ext = with_rim(jnp.stack([latents, cotangent]))
    row_index = lax.axis_index("rows")
    inside = jnp.concatenate(
        [
            jnp.where(row_index > 0, 1.0, 0.0)[None],
            jnp.ones((slab_rows,), jnp.float32),
            jnp.where(row_index < row_devices - 1, 1.0, 0.0)[None],
        ]
    )[None, :, None, None]
    values = latents.astype(jnp.float32)
    chan_mean = jnp.sum(values, axis=(1, 2)) / positions
    centered = values - chan_mean[:, None, None, :]
    chan_m2 = jnp.sum(centered * centered, axis=(1, 2))
    chan_mean_g = chan_mean.reshape(images, groups, CH_GROUP)
    local_mean = jnp.mean(chan_mean_g, axis=2)
    spread = chan_mean_g - local_mean[:, :, None]
    local_m2 = jnp.sum(chan_m2.reshape(images, groups, CH_GROUP), axis=2) + positions * jnp.sum(
        spread * spread, axis=2
    )
    group_mean, group_m2 = merge_stats(local_mean, local_m2, positions * CH_GROUP, "rows")
    inv_std = lax.rsqrt(group_m2 / group_cells + NORM_EPS)
    mean_ch = jnp.repeat(group_mean, CH_GROUP, axis=1)[:, None, None, :]
    rstd_ch = jnp.repeat(inv_std, CH_GROUP, axis=1)[:, None, None, :]
    normalized_ext = (both_ext[0].astype(jnp.float32) - mean_ch) * rstd_ch
    pre_act_ext = normalized_ext * gn_gain + gn_bias
    extended = (jax.nn.silu(pre_act_ext) * inside).astype(jnp.bfloat16)
    normalized = normalized_ext[:, 1 : 1 + slab_rows]
    pre_act = pre_act_ext[:, 1 : 1 + slab_rows]
    temb_features = jax.nn.silu(sinusoid(timesteps, temb_weight.shape[0])).astype(jnp.bfloat16)
    time_shift = jnp.dot(temb_features, temb_weight, preferred_element_type=jnp.float32)
    features = conv_taps(extended, conv_weight, slab_rows, col_count, False)
    features_out = (features + conv_bias + time_shift[:, None, None, :]).astype(jnp.bfloat16)
    hidden_grad = conv_taps(both_ext[1], conv_weight, slab_rows, col_count, True)
    sigmoid_act = jax.nn.sigmoid(pre_act)
    act_grad = hidden_grad * sigmoid_act * (1.0 + pre_act * (1.0 - sigmoid_act))
    chan_weighted = jnp.sum(act_grad * normalized, axis=(1, 2))
    chan_plain = jnp.sum(act_grad, axis=(1, 2))
    chan_output = jnp.sum(cotangent.astype(jnp.float32), axis=(1, 2))
    row_sums = all_sum(jnp.stack([chan_weighted, chan_plain, chan_output], axis=1), "rows")
    row_weighted, row_plain = row_sums[:, 0], row_sums[:, 1]
    first_sum = jnp.sum((row_plain * gn_gain).reshape(images, groups, CH_GROUP), axis=2)
    second_sum = jnp.sum((row_weighted * gn_gain).reshape(images, groups, CH_GROUP), axis=2)
    param_sums = all_sum(jnp.sum(row_sums, axis=0), "dp")
    first_ch = jnp.repeat(first_sum / group_cells, CH_GROUP, axis=1)[:, None, None, :]
    second_ch = jnp.repeat(second_sum / group_cells, CH_GROUP, axis=1)[:, None, None, :]
    input_grad = rstd_ch * (act_grad * gn_gain - first_ch - normalized * second_ch)
    input_grad = input_grad.astype(jnp.bfloat16)
    grad_scale = 1.0 / math.sqrt(images * lax.axis_size("dp") * slab_rows * row_devices * col_count)
    return (features_out, input_grad, param_sums * grad_scale)


def solution(mesh):
    placed = (
        P("dp", "rows", None, None),
        P("dp"),
        P(),
        P(),
        P(),
        P(),
        P(),
        P("dp", "rows", None, None),
    )
    return jax.shard_map(
        per_device,
        mesh=mesh,
        in_specs=placed,
        out_specs=(P("dp", "rows", None, None), P("dp", "rows", None, None), P()),
        check_vma=False,
    )
```

```python
import math

import jax
import jax.numpy as jnp
from jax import lax
from jax.sharding import PartitionSpec as P

CH_GROUP = 40


NORM_EPS = 1e-05


def padded_2(cells, sides, width):
    for axis, dim in sides:
        count = lax.axis_size(axis)
        ends = count - 1
        head = lax.slice_in_dim(cells, 0, width, axis=dim)
        tail = lax.slice_in_dim(cells, cells.shape[dim] - width, cells.shape[dim], axis=dim)
        cells = jnp.concatenate(
            [
                lax.ppermute(tail, axis, [(i, (i + 1) % count) for i in range(ends)]),
                cells,
                lax.ppermute(head, axis, [((i + 1) % count, i) for i in range(ends)]),
            ],
            axis=dim,
        )
    return cells


def is_pow2(count):
    return count & (count - 1) == 0


def all_sum(value, axis):
    count = lax.axis_size(axis)
    if not is_pow2(count):
        return lax.psum(value, axis)
    step = count // 2
    while step >= 1:
        other = lax.ppermute(value, axis, [(i, i ^ step) for i in range(count)])
        value = value + other
        step //= 2
    return value


def merge_stats(mean, m2, cells, axis):
    count = lax.axis_size(axis)
    if not is_pow2(count):
        means = lax.all_gather(mean, axis)
        total_mean = jnp.mean(means, axis=0)
        spread = means - total_mean
        return total_mean, jnp.sum(lax.all_gather(m2, axis), axis=0) + cells * jnp.sum(spread * spread, axis=0)
    value = jnp.stack([mean, m2])
    step = count // 2
    size = 1
    while step >= 1:
        other = lax.ppermute(value, axis, [(i, i ^ step) for i in range(count)])
        delta = other[0] - value[0]
        value = jnp.stack(
            [(value[0] + other[0]) * 0.5, value[1] + other[1] + delta * delta * (cells * size * 0.5)]
        )
        step //= 2
        size *= 2
    return value[0], value[1]


def sinusoid(steps, embed_dim):
    half_dim = embed_dim // 2
    frequencies = jnp.exp(-math.log(10000.0) * jnp.arange(half_dim).astype(jnp.float32) / half_dim)
    angles = steps.astype(jnp.float32)[:, None] * frequencies[None, :]
    return jnp.concatenate([jnp.cos(angles), jnp.sin(angles)], axis=1)


def with_rim(field):
    return padded_2(field, (("rows", 2),), 1)


def conv_taps(extended, weight, slab_rows, col_count, backward):
    padded = jnp.pad(extended, ((0, 0), (0, 0), (1, 1), (0, 0)))
    channels = padded.shape[3]
    total = None
    for tap_row in range(3):
        for tap_col in range(3):
            if backward:
                row_start, col_start = (2 - tap_row, 2 - tap_col)
                dims = (((1,), (1,)), ((), ()))
            else:
                row_start, col_start = (tap_row, tap_col)
                dims = (((1,), (0,)), ((), ()))
            window = padded[
                :, row_start : row_start + slab_rows, col_start : col_start + col_count
            ].reshape(-1, channels)
            tap_term = lax.dot_general(
                window, weight[tap_row, tap_col], dims, preferred_element_type=jnp.float32
            )
            total = tap_term if total is None else total + tap_term
    return total.reshape(-1, slab_rows, col_count, weight.shape[3])


def per_device(
    latents, timesteps, gn_gain, gn_bias, conv_weight, conv_bias, temb_weight, cotangent
):
    images, slab_rows, col_count, channels = latents.shape
    groups = channels // CH_GROUP
    row_devices = lax.axis_size("rows")
    group_cells = slab_rows * row_devices * col_count * CH_GROUP
    positions = slab_rows * col_count
    both_ext = with_rim(jnp.stack([latents, cotangent]))
    row_index = lax.axis_index("rows")
    inside = jnp.concatenate(
        [
            jnp.where(row_index > 0, 1.0, 0.0)[None],
            jnp.ones((slab_rows,), jnp.float32),
            jnp.where(row_index < row_devices - 1, 1.0, 0.0)[None],
        ]
    )[None, :, None, None]
    values = latents.astype(jnp.float32)
    chan_mean = jnp.sum(values, axis=(1, 2)) / positions
    centered = values - chan_mean[:, None, None, :]
    chan_m2 = jnp.sum(centered * centered, axis=(1, 2))
    chan_mean_g = chan_mean.reshape(images, groups, CH_GROUP)
    local_mean = jnp.mean(chan_mean_g, axis=2)
    spread = chan_mean_g - local_mean[:, :, None]
    local_m2 = jnp.sum(chan_m2.reshape(images, groups, CH_GROUP), axis=2) + positions * jnp.sum(
        spread * spread, axis=2
    )
    group_mean, group_m2 = merge_stats(local_mean, local_m2, positions * CH_GROUP, "rows")
    inv_std = lax.rsqrt(group_m2 / group_cells + NORM_EPS)
    mean_ch = jnp.repeat(group_mean, CH_GROUP, axis=1)[:, None, None, :]
    rstd_ch = jnp.repeat(inv_std, CH_GROUP, axis=1)[:, None, None, :]
    normalized_ext = (both_ext[0].astype(jnp.float32) - mean_ch) * rstd_ch
    pre_act_ext = normalized_ext * gn_gain + gn_bias
    extended = (jax.nn.silu(pre_act_ext) * inside).astype(jnp.bfloat16)
    normalized = normalized_ext[:, 1 : 1 + slab_rows]
    pre_act = pre_act_ext[:, 1 : 1 + slab_rows]
    temb_features = jax.nn.silu(sinusoid(timesteps, temb_weight.shape[0])).astype(jnp.bfloat16)
    time_shift = jnp.dot(temb_features, temb_weight, preferred_element_type=jnp.float32)
    hidden_grad = conv_taps(both_ext[1], conv_weight, slab_rows, col_count, True)
    sigmoid_act = jax.nn.sigmoid(pre_act)
    act_grad = hidden_grad * sigmoid_act * (1.0 + pre_act * (1.0 - sigmoid_act))
    chan_weighted = jnp.sum(act_grad * normalized, axis=(1, 2))
    chan_plain = jnp.sum(act_grad, axis=(1, 2))
    chan_output = jnp.sum(cotangent.astype(jnp.float32), axis=(1, 2))
    row_sums = all_sum(jnp.stack([chan_weighted, chan_plain, chan_output], axis=1), "rows")
    row_sums, extended = lax.optimization_barrier((row_sums, extended))
    features = conv_taps(extended, conv_weight, slab_rows, col_count, False)
    features_out = (features + conv_bias + time_shift[:, None, None, :]).astype(jnp.bfloat16)
    row_weighted, row_plain = row_sums[:, 0], row_sums[:, 1]
    first_sum = jnp.sum((row_plain * gn_gain).reshape(images, groups, CH_GROUP), axis=2)
    second_sum = jnp.sum((row_weighted * gn_gain).reshape(images, groups, CH_GROUP), axis=2)
    param_sums = all_sum(jnp.sum(row_sums, axis=0), "dp")
    first_ch = jnp.repeat(first_sum / group_cells, CH_GROUP, axis=1)[:, None, None, :]
    second_ch = jnp.repeat(second_sum / group_cells, CH_GROUP, axis=1)[:, None, None, :]
    input_grad = rstd_ch * (act_grad * gn_gain - first_ch - normalized * second_ch)
    input_grad = input_grad.astype(jnp.bfloat16)
    grad_scale = 1.0 / math.sqrt(images * lax.axis_size("dp") * slab_rows * row_devices * col_count)
    return (features_out, input_grad, param_sums * grad_scale)


def solution(mesh):
    placed = (
        P("dp", "rows", None, None),
        P("dp"),
        P(),
        P(),
        P(),
        P(),
        P(),
        P("dp", "rows", None, None),
    )
    return jax.shard_map(
        per_device,
        mesh=mesh,
        in_specs=placed,
        out_specs=(P("dp", "rows", None, None), P("dp", "rows", None, None), P()),
        check_vma=False,
    )
```

```python
import math

import jax
import jax.numpy as jnp
from jax import lax
from jax.sharding import PartitionSpec as P

CH_GROUP = 40


NORM_EPS = 1e-05


def padded_2(cells, sides, width):
    for axis, dim in sides:
        count = lax.axis_size(axis)
        ends = count - 1
        head = lax.slice_in_dim(cells, 0, width, axis=dim)
        tail = lax.slice_in_dim(cells, cells.shape[dim] - width, cells.shape[dim], axis=dim)
        cells = jnp.concatenate(
            [
                lax.ppermute(tail, axis, [(i, (i + 1) % count) for i in range(ends)]),
                cells,
                lax.ppermute(head, axis, [((i + 1) % count, i) for i in range(ends)]),
            ],
            axis=dim,
        )
    return cells


def is_pow2(count):
    return count & (count - 1) == 0


def all_sum(value, axis):
    count = lax.axis_size(axis)
    if not is_pow2(count):
        return lax.psum(value, axis)
    step = count // 2
    while step >= 1:
        other = lax.ppermute(value, axis, [(i, i ^ step) for i in range(count)])
        value = value + other
        step //= 2
    return value


def merge_stats(mean, m2, cells, axis):
    count = lax.axis_size(axis)
    if not is_pow2(count):
        means = lax.all_gather(mean, axis)
        total_mean = jnp.mean(means, axis=0)
        spread = means - total_mean
        return total_mean, jnp.sum(lax.all_gather(m2, axis), axis=0) + cells * jnp.sum(spread * spread, axis=0)
    value = jnp.stack([mean, m2])
    step = count // 2
    size = 1
    while step >= 1:
        other = lax.ppermute(value, axis, [(i, i ^ step) for i in range(count)])
        delta = other[0] - value[0]
        value = jnp.stack(
            [(value[0] + other[0]) * 0.5, value[1] + other[1] + delta * delta * (cells * size * 0.5)]
        )
        step //= 2
        size *= 2
    return value[0], value[1]


def sinusoid(steps, embed_dim):
    half_dim = embed_dim // 2
    frequencies = jnp.exp(-math.log(10000.0) * jnp.arange(half_dim).astype(jnp.float32) / half_dim)
    angles = steps.astype(jnp.float32)[:, None] * frequencies[None, :]
    return jnp.concatenate([jnp.cos(angles), jnp.sin(angles)], axis=1)


def with_rim(field):
    return padded_2(field, (("rows", 2),), 1)


def conv_taps(extended, weight, slab_rows, col_count, backward):
    padded = jnp.pad(extended, ((0, 0), (0, 0), (1, 1), (0, 0)))
    channels = padded.shape[3]
    total = None
    for tap_row in range(3):
        for tap_col in range(3):
            if backward:
                row_start, col_start = (2 - tap_row, 2 - tap_col)
                dims = (((1,), (1,)), ((), ()))
            else:
                row_start, col_start = (tap_row, tap_col)
                dims = (((1,), (0,)), ((), ()))
            window = padded[
                :, row_start : row_start + slab_rows, col_start : col_start + col_count
            ].reshape(-1, channels)
            tap_term = lax.dot_general(
                window, weight[tap_row, tap_col], dims, preferred_element_type=jnp.float32
            )
            total = tap_term if total is None else total + tap_term
    return total.reshape(-1, slab_rows, col_count, weight.shape[3])


def per_device(
    latents, timesteps, gn_gain, gn_bias, conv_weight, conv_bias, temb_weight, cotangent
):
    images, slab_rows, col_count, channels = latents.shape
    groups = channels // CH_GROUP
    row_devices = lax.axis_size("rows")
    group_cells = slab_rows * row_devices * col_count * CH_GROUP
    positions = slab_rows * col_count
    both_ext = with_rim(jnp.stack([latents, cotangent]))
    row_index = lax.axis_index("rows")
    inside = jnp.concatenate(
        [
            jnp.where(row_index > 0, 1.0, 0.0)[None],
            jnp.ones((slab_rows,), jnp.float32),
            jnp.where(row_index < row_devices - 1, 1.0, 0.0)[None],
        ]
    )[None, :, None, None]
    values = latents.astype(jnp.float32)
    pivot = values[:, 0, 0, :]
    shifted = values - pivot[:, None, None, :]
    shift_sum = jnp.sum(shifted, axis=(1, 2))
    shift_sq = jnp.sum(shifted * shifted, axis=(1, 2))
    chan_mean = pivot + shift_sum / positions
    chan_m2 = jnp.maximum(shift_sq - shift_sum * (shift_sum / positions), 0.0)
    chan_mean_g = chan_mean.reshape(images, groups, CH_GROUP)
    local_mean = jnp.mean(chan_mean_g, axis=2)
    spread = chan_mean_g - local_mean[:, :, None]
    local_m2 = jnp.sum(chan_m2.reshape(images, groups, CH_GROUP), axis=2) + positions * jnp.sum(
        spread * spread, axis=2
    )
    group_mean, group_m2 = merge_stats(local_mean, local_m2, positions * CH_GROUP, "rows")
    inv_std = lax.rsqrt(group_m2 / group_cells + NORM_EPS)
    mean_ch = jnp.repeat(group_mean, CH_GROUP, axis=1)[:, None, None, :]
    rstd_ch = jnp.repeat(inv_std, CH_GROUP, axis=1)[:, None, None, :]
    normalized_ext = (both_ext[0].astype(jnp.float32) - mean_ch) * rstd_ch
    pre_act_ext = normalized_ext * gn_gain + gn_bias
    extended = (jax.nn.silu(pre_act_ext) * inside).astype(jnp.bfloat16)
    normalized = normalized_ext[:, 1 : 1 + slab_rows]
    pre_act = pre_act_ext[:, 1 : 1 + slab_rows]
    temb_features = jax.nn.silu(sinusoid(timesteps, temb_weight.shape[0])).astype(jnp.bfloat16)
    time_shift = jnp.dot(temb_features, temb_weight, preferred_element_type=jnp.float32)
    hidden_grad = conv_taps(both_ext[1], conv_weight, slab_rows, col_count, True)
    sigmoid_act = jax.nn.sigmoid(pre_act)
    act_grad = hidden_grad * sigmoid_act * (1.0 + pre_act * (1.0 - sigmoid_act))
    chan_weighted = jnp.sum(act_grad * normalized, axis=(1, 2))
    chan_plain = jnp.sum(act_grad, axis=(1, 2))
    chan_output = jnp.sum(cotangent.astype(jnp.float32), axis=(1, 2))
    row_sums = all_sum(jnp.stack([chan_weighted, chan_plain, chan_output], axis=1), "rows")
    row_sums, extended = lax.optimization_barrier((row_sums, extended))
    features = conv_taps(extended, conv_weight, slab_rows, col_count, False)
    features_out = (features + conv_bias + time_shift[:, None, None, :]).astype(jnp.bfloat16)
    row_weighted, row_plain = row_sums[:, 0], row_sums[:, 1]
    first_sum = jnp.sum((row_plain * gn_gain).reshape(images, groups, CH_GROUP), axis=2)
    second_sum = jnp.sum((row_weighted * gn_gain).reshape(images, groups, CH_GROUP), axis=2)
    param_sums = all_sum(jnp.sum(row_sums, axis=0), "dp")
    first_ch = jnp.repeat(first_sum / group_cells, CH_GROUP, axis=1)[:, None, None, :]
    second_ch = jnp.repeat(second_sum / group_cells, CH_GROUP, axis=1)[:, None, None, :]
    input_grad = rstd_ch * (act_grad * gn_gain - first_ch - normalized * second_ch)
    input_grad = input_grad.astype(jnp.bfloat16)
    grad_scale = 1.0 / math.sqrt(images * lax.axis_size("dp") * slab_rows * row_devices * col_count)
    return (features_out, input_grad, param_sums * grad_scale)


def solution(mesh):
    placed = (
        P("dp", "rows", None, None),
        P("dp"),
        P(),
        P(),
        P(),
        P(),
        P(),
        P("dp", "rows", None, None),
    )
    return jax.shard_map(
        per_device,
        mesh=mesh,
        in_specs=placed,
        out_specs=(P("dp", "rows", None, None), P("dp", "rows", None, None), P()),
        check_vma=False,
    )
```

```python
import math

import jax
import jax.numpy as jnp
from jax import lax
from jax.sharding import PartitionSpec as P

CH_GROUP = 40


NORM_EPS = 1e-05


def padded_2(cells, sides, width):
    for axis, dim in sides:
        count = lax.axis_size(axis)
        ends = count - 1
        head = lax.slice_in_dim(cells, 0, width, axis=dim)
        tail = lax.slice_in_dim(cells, cells.shape[dim] - width, cells.shape[dim], axis=dim)
        cells = jnp.concatenate(
            [
                lax.ppermute(tail, axis, [(i, (i + 1) % count) for i in range(ends)]),
                cells,
                lax.ppermute(head, axis, [((i + 1) % count, i) for i in range(ends)]),
            ],
            axis=dim,
        )
    return cells


def is_pow2(count):
    return count & (count - 1) == 0


def all_sum(value, axis, riders=(), tie_after=-1):
    count = lax.axis_size(axis)
    if not is_pow2(count):
        return lax.psum(value, axis), riders
    step = count // 2
    done = 0
    while step >= 1:
        other = lax.ppermute(value, axis, [(i, i ^ step) for i in range(count)])
        value = value + other
        if done == tie_after:
            value, riders = lax.optimization_barrier((value, riders))
        done += 1
        step //= 2
    return value, riders


def merge_stats(mean, m2, cells, axis):
    count = lax.axis_size(axis)
    if not is_pow2(count):
        means = lax.all_gather(mean, axis)
        total_mean = jnp.mean(means, axis=0)
        spread = means - total_mean
        return total_mean, jnp.sum(lax.all_gather(m2, axis), axis=0) + cells * jnp.sum(spread * spread, axis=0)
    value = jnp.stack([mean, m2])
    step = count // 2
    size = 1
    while step >= 1:
        other = lax.ppermute(value, axis, [(i, i ^ step) for i in range(count)])
        delta = other[0] - value[0]
        value = jnp.stack(
            [(value[0] + other[0]) * 0.5, value[1] + other[1] + delta * delta * (cells * size * 0.5)]
        )
        step //= 2
        size *= 2
    return value[0], value[1]


def sinusoid(steps, embed_dim):
    half_dim = embed_dim // 2
    frequencies = jnp.exp(-math.log(10000.0) * jnp.arange(half_dim).astype(jnp.float32) / half_dim)
    angles = steps.astype(jnp.float32)[:, None] * frequencies[None, :]
    return jnp.concatenate([jnp.cos(angles), jnp.sin(angles)], axis=1)


def with_rim(field):
    return padded_2(field, (("rows", 2),), 1)


def conv_taps(extended, weight, slab_rows, col_count, backward):
    padded = jnp.pad(extended, ((0, 0), (0, 0), (1, 1), (0, 0)))
    channels = padded.shape[3]
    total = None
    for tap_row in range(3):
        for tap_col in range(3):
            if backward:
                row_start, col_start = (2 - tap_row, 2 - tap_col)
                dims = (((1,), (1,)), ((), ()))
            else:
                row_start, col_start = (tap_row, tap_col)
                dims = (((1,), (0,)), ((), ()))
            window = padded[
                :, row_start : row_start + slab_rows, col_start : col_start + col_count
            ].reshape(-1, channels)
            tap_term = lax.dot_general(
                window, weight[tap_row, tap_col], dims, preferred_element_type=jnp.float32
            )
            total = tap_term if total is None else total + tap_term
    return total.reshape(-1, slab_rows, col_count, weight.shape[3])


def per_device(
    latents, timesteps, gn_gain, gn_bias, conv_weight, conv_bias, temb_weight, cotangent
):
    images, slab_rows, col_count, channels = latents.shape
    groups = channels // CH_GROUP
    row_devices = lax.axis_size("rows")
    group_cells = slab_rows * row_devices * col_count * CH_GROUP
    positions = slab_rows * col_count
    both_ext = with_rim(jnp.stack([latents, cotangent]))
    row_index = lax.axis_index("rows")
    inside = jnp.concatenate(
        [
            jnp.where(row_index > 0, 1.0, 0.0)[None],
            jnp.ones((slab_rows,), jnp.float32),
            jnp.where(row_index < row_devices - 1, 1.0, 0.0)[None],
        ]
    )[None, :, None, None]
    values = latents.astype(jnp.float32)
    chan_mean = jnp.sum(values, axis=(1, 2)) / positions
    centered = values - chan_mean[:, None, None, :]
    chan_m2 = jnp.sum(centered * centered, axis=(1, 2))
    chan_mean_g = chan_mean.reshape(images, groups, CH_GROUP)
    local_mean = jnp.mean(chan_mean_g, axis=2)
    spread = chan_mean_g - local_mean[:, :, None]
    local_m2 = jnp.sum(chan_m2.reshape(images, groups, CH_GROUP), axis=2) + positions * jnp.sum(
        spread * spread, axis=2
    )
    group_mean, group_m2 = merge_stats(local_mean, local_m2, positions * CH_GROUP, "rows")
    inv_std = lax.rsqrt(group_m2 / group_cells + NORM_EPS)
    mean_ch = jnp.repeat(group_mean, CH_GROUP, axis=1)[:, None, None, :]
    rstd_ch = jnp.repeat(inv_std, CH_GROUP, axis=1)[:, None, None, :]
    normalized_ext = (both_ext[0].astype(jnp.float32) - mean_ch) * rstd_ch
    pre_act_ext = normalized_ext * gn_gain + gn_bias
    extended = (jax.nn.silu(pre_act_ext) * inside).astype(jnp.bfloat16)
    normalized = normalized_ext[:, 1 : 1 + slab_rows]
    pre_act = pre_act_ext[:, 1 : 1 + slab_rows]
    temb_features = jax.nn.silu(sinusoid(timesteps, temb_weight.shape[0])).astype(jnp.bfloat16)
    time_shift = jnp.dot(temb_features, temb_weight, preferred_element_type=jnp.float32)
    features = conv_taps(extended, conv_weight, slab_rows, col_count, False)
    features_out = (features + conv_bias + time_shift[:, None, None, :]).astype(jnp.bfloat16)
    hidden_grad = conv_taps(both_ext[1], conv_weight, slab_rows, col_count, True)
    sigmoid_act = jax.nn.sigmoid(pre_act)
    act_grad = hidden_grad * sigmoid_act * (1.0 + pre_act * (1.0 - sigmoid_act))
    chan_weighted = jnp.sum(act_grad * normalized, axis=(1, 2))
    chan_plain = jnp.sum(act_grad, axis=(1, 2))
    chan_output = jnp.sum(cotangent.astype(jnp.float32), axis=(1, 2))
    row_sums, _ = all_sum(jnp.stack([chan_weighted, chan_plain, chan_output], axis=1), "rows")
    row_weighted, row_plain = row_sums[:, 0], row_sums[:, 1]
    first_sum = jnp.sum((row_plain * gn_gain).reshape(images, groups, CH_GROUP), axis=2)
    second_sum = jnp.sum((row_weighted * gn_gain).reshape(images, groups, CH_GROUP), axis=2)
    first_ch = jnp.repeat(first_sum / group_cells, CH_GROUP, axis=1)[:, None, None, :]
    second_ch = jnp.repeat(second_sum / group_cells, CH_GROUP, axis=1)[:, None, None, :]
    input_grad = rstd_ch * (act_grad * gn_gain - first_ch - normalized * second_ch)
    input_grad = input_grad.astype(jnp.bfloat16)
    param_sums, input_grad = all_sum(jnp.sum(row_sums, axis=0), "dp", input_grad, 1)
    grad_scale = 1.0 / math.sqrt(images * lax.axis_size("dp") * slab_rows * row_devices * col_count)
    return (features_out, input_grad, param_sums * grad_scale)


def solution(mesh):
    placed = (
        P("dp", "rows", None, None),
        P("dp"),
        P(),
        P(),
        P(),
        P(),
        P(),
        P("dp", "rows", None, None),
    )
    return jax.shard_map(
        per_device,
        mesh=mesh,
        in_specs=placed,
        out_specs=(P("dp", "rows", None, None), P("dp", "rows", None, None), P()),
        check_vma=False,
    )
```

```python
import math

import jax
import jax.numpy as jnp
from jax import lax
from jax.sharding import PartitionSpec as P

CH_GROUP = 40


NORM_EPS = 1e-05


def padded_2(cells, sides, width):
    for axis, dim in sides:
        count = lax.axis_size(axis)
        ends = count - 1
        head = lax.slice_in_dim(cells, 0, width, axis=dim)
        tail = lax.slice_in_dim(cells, cells.shape[dim] - width, cells.shape[dim], axis=dim)
        cells = jnp.concatenate(
            [
                lax.ppermute(tail, axis, [(i, (i + 1) % count) for i in range(ends)]),
                cells,
                lax.ppermute(head, axis, [((i + 1) % count, i) for i in range(ends)]),
            ],
            axis=dim,
        )
    return cells


def is_pow2(count):
    return count & (count - 1) == 0


def all_sum(value, axis):
    count = lax.axis_size(axis)
    if not is_pow2(count):
        return lax.psum(value, axis)
    step = count // 2
    while step >= 1:
        other = lax.ppermute(value, axis, [(i, i ^ step) for i in range(count)])
        value = value + other
        step //= 2
    return value


def merge_stats(mean, m2, cells, axis):
    count = lax.axis_size(axis)
    if not is_pow2(count):
        means = lax.all_gather(mean, axis)
        total_mean = jnp.mean(means, axis=0)
        spread = means - total_mean
        return total_mean, jnp.sum(lax.all_gather(m2, axis), axis=0) + cells * jnp.sum(spread * spread, axis=0)
    value = jnp.stack([mean, m2])
    step = count // 2
    size = 1
    while step >= 1:
        other = lax.ppermute(value, axis, [(i, i ^ step) for i in range(count)])
        delta = other[0] - value[0]
        value = jnp.stack(
            [(value[0] + other[0]) * 0.5, value[1] + other[1] + delta * delta * (cells * size * 0.5)]
        )
        step //= 2
        size *= 2
    return value[0], value[1]


def sinusoid(steps, embed_dim):
    half_dim = embed_dim // 2
    frequencies = jnp.exp(-math.log(10000.0) * jnp.arange(half_dim).astype(jnp.float32) / half_dim)
    angles = steps.astype(jnp.float32)[:, None] * frequencies[None, :]
    return jnp.concatenate([jnp.cos(angles), jnp.sin(angles)], axis=1)


def with_rim(field):
    return padded_2(field, (("rows", 2),), 1)


def conv_taps(extended, weight, slab_rows, col_count, backward):
    padded = jnp.pad(extended, ((0, 0), (0, 0), (1, 1), (0, 0)))
    channels = padded.shape[3]
    total = None
    for tap_row in range(3):
        for tap_col in range(3):
            if backward:
                row_start, col_start = (2 - tap_row, 2 - tap_col)
                dims = (((1,), (1,)), ((), ()))
            else:
                row_start, col_start = (tap_row, tap_col)
                dims = (((1,), (0,)), ((), ()))
            window = padded[
                :, row_start : row_start + slab_rows, col_start : col_start + col_count
            ].reshape(-1, channels)
            tap_term = lax.dot_general(
                window, weight[tap_row, tap_col], dims, preferred_element_type=jnp.float32
            )
            total = tap_term if total is None else total + tap_term
    return total.reshape(-1, slab_rows, col_count, weight.shape[3])


def per_device(
    latents, timesteps, gn_gain, gn_bias, conv_weight, conv_bias, temb_weight, cotangent
):
    images, slab_rows, col_count, channels = latents.shape
    groups = channels // CH_GROUP
    row_devices = lax.axis_size("rows")
    group_cells = slab_rows * row_devices * col_count * CH_GROUP
    positions = slab_rows * col_count
    both_ext = with_rim(jnp.stack([latents, cotangent]))
    row_index = lax.axis_index("rows")
    inside = jnp.concatenate(
        [
            jnp.where(row_index > 0, 1.0, 0.0)[None],
            jnp.ones((slab_rows,), jnp.float32),
            jnp.where(row_index < row_devices - 1, 1.0, 0.0)[None],
        ]
    )[None, :, None, None]
    values = latents.astype(jnp.float32)
    pivot = latents[:, 0, 0, :].astype(jnp.float32)
    shifted = latents.astype(jnp.float32) - pivot[:, None, None, :]
    shift_sum = jnp.sum(shifted, axis=(1, 2))
    shift_sq = jnp.sum(shifted * shifted, axis=(1, 2))
    chan_mean = pivot + shift_sum / positions
    chan_m2 = jnp.maximum(shift_sq - shift_sum * (shift_sum / positions), 0.0)
    chan_mean_g = chan_mean.reshape(images, groups, CH_GROUP)
    local_mean = jnp.mean(chan_mean_g, axis=2)
    spread = chan_mean_g - local_mean[:, :, None]
    local_m2 = jnp.sum(chan_m2.reshape(images, groups, CH_GROUP), axis=2) + positions * jnp.sum(
        spread * spread, axis=2
    )
    group_mean, group_m2 = merge_stats(local_mean, local_m2, positions * CH_GROUP, "rows")
    inv_std = lax.rsqrt(group_m2 / group_cells + NORM_EPS)
    mean_ch = jnp.repeat(group_mean, CH_GROUP, axis=1)[:, None, None, :]
    rstd_ch = jnp.repeat(inv_std, CH_GROUP, axis=1)[:, None, None, :]
    normalized_ext = (both_ext[0].astype(jnp.float32) - mean_ch) * rstd_ch
    pre_act_ext = normalized_ext * gn_gain + gn_bias
    extended = (jax.nn.silu(pre_act_ext) * inside).astype(jnp.bfloat16)
    normalized = normalized_ext[:, 1 : 1 + slab_rows]
    pre_act = pre_act_ext[:, 1 : 1 + slab_rows]
    temb_features = jax.nn.silu(sinusoid(timesteps, temb_weight.shape[0])).astype(jnp.bfloat16)
    time_shift = jnp.dot(temb_features, temb_weight, preferred_element_type=jnp.float32)
    features = conv_taps(extended, conv_weight, slab_rows, col_count, False)
    features_out = (features + conv_bias + time_shift[:, None, None, :]).astype(jnp.bfloat16)
    hidden_grad = conv_taps(both_ext[1], conv_weight, slab_rows, col_count, True)
    sigmoid_act = jax.nn.sigmoid(pre_act)
    act_grad = hidden_grad * sigmoid_act * (1.0 + pre_act * (1.0 - sigmoid_act))
    chan_weighted = jnp.sum(act_grad * normalized, axis=(1, 2))
    chan_plain = jnp.sum(act_grad, axis=(1, 2))
    chan_output = jnp.sum(cotangent.astype(jnp.float32), axis=(1, 2))
    row_sums = all_sum(jnp.stack([chan_weighted, chan_plain, chan_output], axis=1), "rows")
    row_weighted, row_plain = row_sums[:, 0], row_sums[:, 1]
    first_sum = jnp.sum((row_plain * gn_gain).reshape(images, groups, CH_GROUP), axis=2)
    second_sum = jnp.sum((row_weighted * gn_gain).reshape(images, groups, CH_GROUP), axis=2)
    param_sums = all_sum(jnp.sum(row_sums, axis=0), "dp")
    first_ch = jnp.repeat(first_sum / group_cells, CH_GROUP, axis=1)[:, None, None, :]
    second_ch = jnp.repeat(second_sum / group_cells, CH_GROUP, axis=1)[:, None, None, :]
    input_grad = rstd_ch * (act_grad * gn_gain - first_ch - normalized * second_ch)
    input_grad = input_grad.astype(jnp.bfloat16)
    grad_scale = 1.0 / math.sqrt(images * lax.axis_size("dp") * slab_rows * row_devices * col_count)
    return (features_out, input_grad, param_sums * grad_scale)


def solution(mesh):
    placed = (
        P("dp", "rows", None, None),
        P("dp"),
        P(),
        P(),
        P(),
        P(),
        P(),
        P("dp", "rows", None, None),
    )
    return jax.shard_map(
        per_device,
        mesh=mesh,
        in_specs=placed,
        out_specs=(P("dp", "rows", None, None), P("dp", "rows", None, None), P()),
        check_vma=False,
    )
```

```python
import math

import jax
import jax.numpy as jnp
from jax import lax
from jax.sharding import PartitionSpec as P

CH_GROUP = 40


NORM_EPS = 1e-05


def padded_2(cells, sides, width):
    for axis, dim in sides:
        count = lax.axis_size(axis)
        ends = count - 1
        head = lax.slice_in_dim(cells, 0, width, axis=dim)
        tail = lax.slice_in_dim(cells, cells.shape[dim] - width, cells.shape[dim], axis=dim)
        cells = jnp.concatenate(
            [
                lax.ppermute(tail, axis, [(i, (i + 1) % count) for i in range(ends)]),
                cells,
                lax.ppermute(head, axis, [((i + 1) % count, i) for i in range(ends)]),
            ],
            axis=dim,
        )
    return cells


def is_pow2(count):
    return count & (count - 1) == 0


def all_sum(value, axis, ascending=False):
    count = lax.axis_size(axis)
    if not is_pow2(count):
        return lax.psum(value, axis)
    steps = []
    step = count // 2
    while step >= 1:
        steps.append(step)
        step //= 2
    for step in steps[::-1] if ascending else steps:
        other = lax.ppermute(value, axis, [(i, i ^ step) for i in range(count)])
        value = value + other
    return value


def merge_stats(mean, m2, cells, axis):
    count = lax.axis_size(axis)
    if not is_pow2(count):
        means = lax.all_gather(mean, axis)
        total_mean = jnp.mean(means, axis=0)
        spread = means - total_mean
        return total_mean, jnp.sum(lax.all_gather(m2, axis), axis=0) + cells * jnp.sum(spread * spread, axis=0)
    value = jnp.stack([mean, m2])
    step = count // 2
    size = 1
    while step >= 1:
        other = lax.ppermute(value, axis, [(i, i ^ step) for i in range(count)])
        delta = other[0] - value[0]
        value = jnp.stack(
            [(value[0] + other[0]) * 0.5, value[1] + other[1] + delta * delta * (cells * size * 0.5)]
        )
        step //= 2
        size *= 2
    return value[0], value[1]


def sinusoid(steps, embed_dim):
    half_dim = embed_dim // 2
    frequencies = jnp.exp(-math.log(10000.0) * jnp.arange(half_dim).astype(jnp.float32) / half_dim)
    angles = steps.astype(jnp.float32)[:, None] * frequencies[None, :]
    return jnp.concatenate([jnp.cos(angles), jnp.sin(angles)], axis=1)


def with_rim(field):
    return padded_2(field, (("rows", 2),), 1)


def conv_taps(extended, weight, slab_rows, col_count, backward):
    padded = jnp.pad(extended, ((0, 0), (0, 0), (1, 1), (0, 0)))
    channels = padded.shape[3]
    total = None
    for tap_row in range(3):
        for tap_col in range(3):
            if backward:
                row_start, col_start = (2 - tap_row, 2 - tap_col)
                dims = (((1,), (1,)), ((), ()))
            else:
                row_start, col_start = (tap_row, tap_col)
                dims = (((1,), (0,)), ((), ()))
            window = padded[
                :, row_start : row_start + slab_rows, col_start : col_start + col_count
            ].reshape(-1, channels)
            tap_term = lax.dot_general(
                window, weight[tap_row, tap_col], dims, preferred_element_type=jnp.float32
            )
            total = tap_term if total is None else total + tap_term
    return total.reshape(-1, slab_rows, col_count, weight.shape[3])


def per_device(
    latents, timesteps, gn_gain, gn_bias, conv_weight, conv_bias, temb_weight, cotangent
):
    images, slab_rows, col_count, channels = latents.shape
    groups = channels // CH_GROUP
    row_devices = lax.axis_size("rows")
    group_cells = slab_rows * row_devices * col_count * CH_GROUP
    positions = slab_rows * col_count
    both_ext = with_rim(jnp.stack([latents, cotangent]))
    row_index = lax.axis_index("rows")
    inside = jnp.concatenate(
        [
            jnp.where(row_index > 0, 1.0, 0.0)[None],
            jnp.ones((slab_rows,), jnp.float32),
            jnp.where(row_index < row_devices - 1, 1.0, 0.0)[None],
        ]
    )[None, :, None, None]
    values = latents.astype(jnp.float32)
    pivot = latents[:, 0, 0, :].astype(jnp.float32)
    shifted = latents.astype(jnp.float32) - pivot[:, None, None, :]
    shift_sum = jnp.sum(shifted, axis=(1, 2))
    shift_sq = jnp.sum(shifted * shifted, axis=(1, 2))
    chan_mean = pivot + shift_sum / positions
    chan_m2 = jnp.maximum(shift_sq - shift_sum * (shift_sum / positions), 0.0)
    chan_mean_g = chan_mean.reshape(images, groups, CH_GROUP)
    local_mean = jnp.mean(chan_mean_g, axis=2)
    spread = chan_mean_g - local_mean[:, :, None]
    local_m2 = jnp.sum(chan_m2.reshape(images, groups, CH_GROUP), axis=2) + positions * jnp.sum(
        spread * spread, axis=2
    )
    group_mean, group_m2 = merge_stats(local_mean, local_m2, positions * CH_GROUP, "rows")
    inv_std = lax.rsqrt(group_m2 / group_cells + NORM_EPS)
    mean_ch = jnp.repeat(group_mean, CH_GROUP, axis=1)[:, None, None, :]
    rstd_ch = jnp.repeat(inv_std, CH_GROUP, axis=1)[:, None, None, :]
    normalized_ext = (both_ext[0].astype(jnp.float32) - mean_ch) * rstd_ch
    pre_act_ext = normalized_ext * gn_gain + gn_bias
    extended = (jax.nn.silu(pre_act_ext) * inside).astype(jnp.bfloat16)
    normalized = normalized_ext[:, 1 : 1 + slab_rows]
    pre_act = pre_act_ext[:, 1 : 1 + slab_rows]
    temb_features = jax.nn.silu(sinusoid(timesteps, temb_weight.shape[0])).astype(jnp.bfloat16)
    time_shift = jnp.dot(temb_features, temb_weight, preferred_element_type=jnp.float32)
    features = conv_taps(extended, conv_weight, slab_rows, col_count, False)
    features_out = (features + conv_bias + time_shift[:, None, None, :]).astype(jnp.bfloat16)
    hidden_grad = conv_taps(both_ext[1], conv_weight, slab_rows, col_count, True)
    sigmoid_act = jax.nn.sigmoid(pre_act)
    act_grad = hidden_grad * sigmoid_act * (1.0 + pre_act * (1.0 - sigmoid_act))
    chan_weighted = jnp.sum(act_grad * normalized, axis=(1, 2))
    chan_plain = jnp.sum(act_grad, axis=(1, 2))
    chan_output = jnp.sum(cotangent.astype(jnp.float32), axis=(1, 2))
    row_sums = all_sum(jnp.stack([chan_weighted, chan_plain, chan_output], axis=1), "rows")
    row_weighted, row_plain = row_sums[:, 0], row_sums[:, 1]
    first_sum = jnp.sum((row_plain * gn_gain).reshape(images, groups, CH_GROUP), axis=2)
    second_sum = jnp.sum((row_weighted * gn_gain).reshape(images, groups, CH_GROUP), axis=2)
    param_sums = all_sum(jnp.sum(row_sums, axis=0), "dp", True)
    first_ch = jnp.repeat(first_sum / group_cells, CH_GROUP, axis=1)[:, None, None, :]
    second_ch = jnp.repeat(second_sum / group_cells, CH_GROUP, axis=1)[:, None, None, :]
    input_grad = rstd_ch * (act_grad * gn_gain - first_ch - normalized * second_ch)
    input_grad = input_grad.astype(jnp.bfloat16)
    grad_scale = 1.0 / math.sqrt(images * lax.axis_size("dp") * slab_rows * row_devices * col_count)
    return (features_out, input_grad, param_sums * grad_scale)


def solution(mesh):
    placed = (
        P("dp", "rows", None, None),
        P("dp"),
        P(),
        P(),
        P(),
        P(),
        P(),
        P("dp", "rows", None, None),
    )
    return jax.shard_map(
        per_device,
        mesh=mesh,
        in_specs=placed,
        out_specs=(P("dp", "rows", None, None), P("dp", "rows", None, None), P()),
        check_vma=False,
    )
```

```python
import math

import jax
import jax.numpy as jnp
from jax import lax
from jax.sharding import PartitionSpec as P

CH_GROUP = 40


NORM_EPS = 1e-05


def padded_2(cells, sides, width):
    for axis, dim in sides:
        count = lax.axis_size(axis)
        ends = count - 1
        head = lax.slice_in_dim(cells, 0, width, axis=dim)
        tail = lax.slice_in_dim(cells, cells.shape[dim] - width, cells.shape[dim], axis=dim)
        cells = jnp.concatenate(
            [
                lax.ppermute(tail, axis, [(i, (i + 1) % count) for i in range(ends)]),
                cells,
                lax.ppermute(head, axis, [((i + 1) % count, i) for i in range(ends)]),
            ],
            axis=dim,
        )
    return cells


def is_pow2(count):
    return count & (count - 1) == 0


def all_sum(value, axis):
    count = lax.axis_size(axis)
    if not is_pow2(count):
        return lax.psum(value, axis)
    step = count // 2
    while step >= 1:
        other = lax.ppermute(value, axis, [(i, i ^ step) for i in range(count)])
        value = value + other
        step //= 2
    return value


def merge_stats(mean, m2, cells, axis):
    count = lax.axis_size(axis)
    if not is_pow2(count):
        means = lax.all_gather(mean, axis)
        total_mean = jnp.mean(means, axis=0)
        spread = means - total_mean
        return total_mean, jnp.sum(lax.all_gather(m2, axis), axis=0) + cells * jnp.sum(spread * spread, axis=0)
    value = jnp.stack([mean, m2])
    step = count // 2
    size = 1
    while step >= 1:
        other = lax.ppermute(value, axis, [(i, i ^ step) for i in range(count)])
        delta = other[0] - value[0]
        value = jnp.stack(
            [(value[0] + other[0]) * 0.5, value[1] + other[1] + delta * delta * (cells * size * 0.5)]
        )
        step //= 2
        size *= 2
    return value[0], value[1]


def position_sum(field):
    flat = field.reshape(field.shape[0], -1, field.shape[-1])
    ones = jnp.ones((flat.shape[1],), field.dtype)
    return jnp.einsum("p,ipc->ic", ones, flat, preferred_element_type=jnp.float32)


def sinusoid(steps, embed_dim):
    half_dim = embed_dim // 2
    frequencies = jnp.exp(-math.log(10000.0) * jnp.arange(half_dim).astype(jnp.float32) / half_dim)
    angles = steps.astype(jnp.float32)[:, None] * frequencies[None, :]
    return jnp.concatenate([jnp.cos(angles), jnp.sin(angles)], axis=1)


def with_rim(field):
    return padded_2(field, (("rows", 2),), 1)


def conv_taps(extended, weight, slab_rows, col_count, backward):
    padded = jnp.pad(extended, ((0, 0), (0, 0), (1, 1), (0, 0)))
    channels = padded.shape[3]
    total = None
    for tap_row in range(3):
        for tap_col in range(3):
            if backward:
                row_start, col_start = (2 - tap_row, 2 - tap_col)
                dims = (((1,), (1,)), ((), ()))
            else:
                row_start, col_start = (tap_row, tap_col)
                dims = (((1,), (0,)), ((), ()))
            window = padded[
                :, row_start : row_start + slab_rows, col_start : col_start + col_count
            ].reshape(-1, channels)
            tap_term = lax.dot_general(
                window, weight[tap_row, tap_col], dims, preferred_element_type=jnp.float32
            )
            total = tap_term if total is None else total + tap_term
    return total.reshape(-1, slab_rows, col_count, weight.shape[3])


def per_device(
    latents, timesteps, gn_gain, gn_bias, conv_weight, conv_bias, temb_weight, cotangent
):
    images, slab_rows, col_count, channels = latents.shape
    groups = channels // CH_GROUP
    row_devices = lax.axis_size("rows")
    group_cells = slab_rows * row_devices * col_count * CH_GROUP
    positions = slab_rows * col_count
    both_ext = with_rim(jnp.stack([latents, cotangent]))
    row_index = lax.axis_index("rows")
    inside = jnp.concatenate(
        [
            jnp.where(row_index > 0, 1.0, 0.0)[None],
            jnp.ones((slab_rows,), jnp.float32),
            jnp.where(row_index < row_devices - 1, 1.0, 0.0)[None],
        ]
    )[None, :, None, None]
    values = latents.astype(jnp.float32)
    pivot = latents[:, 0, 0, :].astype(jnp.float32)
    shifted = latents.astype(jnp.float32) - pivot[:, None, None, :]
    shift_sum = jnp.sum(shifted, axis=(1, 2))
    shift_sq = jnp.sum(shifted * shifted, axis=(1, 2))
    chan_mean = pivot + shift_sum / positions
    chan_m2 = jnp.maximum(shift_sq - shift_sum * (shift_sum / positions), 0.0)
    chan_mean_g = chan_mean.reshape(images, groups, CH_GROUP)
    local_mean = jnp.mean(chan_mean_g, axis=2)
    spread = chan_mean_g - local_mean[:, :, None]
    local_m2 = jnp.sum(chan_m2.reshape(images, groups, CH_GROUP), axis=2) + positions * jnp.sum(
        spread * spread, axis=2
    )
    group_mean, group_m2 = merge_stats(local_mean, local_m2, positions * CH_GROUP, "rows")
    inv_std = lax.rsqrt(group_m2 / group_cells + NORM_EPS)
    mean_ch = jnp.repeat(group_mean, CH_GROUP, axis=1)[:, None, None, :]
    rstd_ch = jnp.repeat(inv_std, CH_GROUP, axis=1)[:, None, None, :]
    normalized_ext = (both_ext[0].astype(jnp.float32) - mean_ch) * rstd_ch
    pre_act_ext = normalized_ext * gn_gain + gn_bias
    extended = (jax.nn.silu(pre_act_ext) * inside).astype(jnp.bfloat16)
    normalized = normalized_ext[:, 1 : 1 + slab_rows]
    pre_act = pre_act_ext[:, 1 : 1 + slab_rows]
    temb_features = jax.nn.silu(sinusoid(timesteps, temb_weight.shape[0])).astype(jnp.bfloat16)
    time_shift = jnp.dot(temb_features, temb_weight, preferred_element_type=jnp.float32)
    features = conv_taps(extended, conv_weight, slab_rows, col_count, False)
    features_out = (features + conv_bias + time_shift[:, None, None, :]).astype(jnp.bfloat16)
    hidden_grad = conv_taps(both_ext[1], conv_weight, slab_rows, col_count, True)
    sigmoid_act = jax.nn.sigmoid(pre_act)
    act_grad = hidden_grad * sigmoid_act * (1.0 + pre_act * (1.0 - sigmoid_act))
    chan_weighted = jnp.sum(act_grad * normalized, axis=(1, 2))
    chan_plain = jnp.sum(act_grad, axis=(1, 2))
    chan_output = position_sum(cotangent)
    row_sums = all_sum(jnp.stack([chan_weighted, chan_plain, chan_output], axis=1), "rows")
    row_weighted, row_plain = row_sums[:, 0], row_sums[:, 1]
    first_sum = jnp.sum((row_plain * gn_gain).reshape(images, groups, CH_GROUP), axis=2)
    second_sum = jnp.sum((row_weighted * gn_gain).reshape(images, groups, CH_GROUP), axis=2)
    param_sums = all_sum(jnp.sum(row_sums, axis=0), "dp")
    first_ch = jnp.repeat(first_sum / group_cells, CH_GROUP, axis=1)[:, None, None, :]
    second_ch = jnp.repeat(second_sum / group_cells, CH_GROUP, axis=1)[:, None, None, :]
    input_grad = rstd_ch * (act_grad * gn_gain - first_ch - normalized * second_ch)
    input_grad = input_grad.astype(jnp.bfloat16)
    grad_scale = 1.0 / math.sqrt(images * lax.axis_size("dp") * slab_rows * row_devices * col_count)
    return (features_out, input_grad, param_sums * grad_scale)


def solution(mesh):
    placed = (
        P("dp", "rows", None, None),
        P("dp"),
        P(),
        P(),
        P(),
        P(),
        P(),
        P("dp", "rows", None, None),
    )
    return jax.shard_map(
        per_device,
        mesh=mesh,
        in_specs=placed,
        out_specs=(P("dp", "rows", None, None), P("dp", "rows", None, None), P()),
        check_vma=False,
    )
```

```python
import math

import jax
import jax.numpy as jnp
from jax import lax
from jax.experimental import pallas as pl
from jax.sharding import PartitionSpec as P

CH_GROUP = 40


NORM_EPS = 1e-05


def padded_2(cells, sides, width):
    for axis, dim in sides:
        count = lax.axis_size(axis)
        ends = count - 1
        head = lax.slice_in_dim(cells, 0, width, axis=dim)
        tail = lax.slice_in_dim(cells, cells.shape[dim] - width, cells.shape[dim], axis=dim)
        cells = jnp.concatenate(
            [
                lax.ppermute(tail, axis, [(i, (i + 1) % count) for i in range(ends)]),
                cells,
                lax.ppermute(head, axis, [((i + 1) % count, i) for i in range(ends)]),
            ],
            axis=dim,
        )
    return cells


def is_pow2(count):
    return count & (count - 1) == 0


def all_sum(value, axis):
    count = lax.axis_size(axis)
    if not is_pow2(count):
        return lax.psum(value, axis)
    step = count // 2
    while step >= 1:
        other = lax.ppermute(value, axis, [(i, i ^ step) for i in range(count)])
        value = value + other
        step //= 2
    return value


def merge_stats(mean, m2, cells, axis):
    count = lax.axis_size(axis)
    if not is_pow2(count):
        means = lax.all_gather(mean, axis)
        total_mean = jnp.mean(means, axis=0)
        spread = means - total_mean
        return total_mean, jnp.sum(lax.all_gather(m2, axis), axis=0) + cells * jnp.sum(spread * spread, axis=0)
    value = jnp.stack([mean, m2])
    step = count // 2
    size = 1
    while step >= 1:
        other = lax.ppermute(value, axis, [(i, i ^ step) for i in range(count)])
        delta = other[0] - value[0]
        value = jnp.stack(
            [(value[0] + other[0]) * 0.5, value[1] + other[1] + delta * delta * (cells * size * 0.5)]
        )
        step //= 2
        size *= 2
    return value[0], value[1]


def front_kernel(lat_ref, ct_ref, pivot_ref, sum_ref, sq_ref, ct_sum_ref, tails_ref, heads_ref):
    slab_rows = lat_ref.shape[1]
    lat = lat_ref[...].astype(jnp.float32)
    pivot = lat[:, 0, 0:1, :]
    shifted = lat - pivot[:, None]
    row_sum = jnp.sum(shifted, axis=1)
    row_sq = jnp.sum(shifted * shifted, axis=1)
    pivot_ref[...] = pivot[:, 0, :]
    sum_ref[...] = jnp.sum(row_sum, axis=1)
    sq_ref[...] = jnp.sum(row_sq, axis=1)
    ct_rows = jnp.sum(ct_ref[...].astype(jnp.float32), axis=1)
    ct_sum_ref[...] = jnp.sum(ct_rows, axis=1)
    tails_ref[0] = lat_ref[:, slab_rows - 1]
    tails_ref[1] = ct_ref[:, slab_rows - 1]
    heads_ref[0] = lat_ref[:, 0]
    heads_ref[1] = ct_ref[:, 0]


def front_pass(latents, cotangent):
    images, _, col_count, channels = latents.shape
    vec = jax.ShapeDtypeStruct((images, channels), jnp.float32)
    edge = jax.ShapeDtypeStruct((2, images, col_count, channels), latents.dtype)
    return pl.pallas_call(front_kernel, out_shape=(vec, vec, vec, vec, edge, edge))(latents, cotangent)


def rims_from(fields, tails, heads):
    count = lax.axis_size("rows")
    from_above = lax.ppermute(tails, "rows", [(i, i + 1) for i in range(count - 1)])
    from_below = lax.ppermute(heads, "rows", [(i + 1, i) for i in range(count - 1)])
    return [
        jnp.concatenate([from_above[k][:, None], field, from_below[k][:, None]], axis=1)
        for k, field in enumerate(fields)
    ]


def sinusoid(steps, embed_dim):
    half_dim = embed_dim // 2
    frequencies = jnp.exp(-math.log(10000.0) * jnp.arange(half_dim).astype(jnp.float32) / half_dim)
    angles = steps.astype(jnp.float32)[:, None] * frequencies[None, :]
    return jnp.concatenate([jnp.cos(angles), jnp.sin(angles)], axis=1)


def with_rim(field):
    return padded_2(field, (("rows", 2),), 1)


def conv_taps(extended, weight, slab_rows, col_count, backward):
    padded = jnp.pad(extended, ((0, 0), (0, 0), (1, 1), (0, 0)))
    channels = padded.shape[3]
    total = None
    for tap_row in range(3):
        for tap_col in range(3):
            if backward:
                row_start, col_start = (2 - tap_row, 2 - tap_col)
                dims = (((1,), (1,)), ((), ()))
            else:
                row_start, col_start = (tap_row, tap_col)
                dims = (((1,), (0,)), ((), ()))
            window = padded[
                :, row_start : row_start + slab_rows, col_start : col_start + col_count
            ].reshape(-1, channels)
            tap_term = lax.dot_general(
                window, weight[tap_row, tap_col], dims, preferred_element_type=jnp.float32
            )
            total = tap_term if total is None else total + tap_term
    return total.reshape(-1, slab_rows, col_count, weight.shape[3])


def per_device(
    latents, timesteps, gn_gain, gn_bias, conv_weight, conv_bias, temb_weight, cotangent
):
    images, slab_rows, col_count, channels = latents.shape
    groups = channels // CH_GROUP
    row_devices = lax.axis_size("rows")
    group_cells = slab_rows * row_devices * col_count * CH_GROUP
    positions = slab_rows * col_count
    pivot, shift_sum, shift_sq, chan_output, tails, heads = front_pass(latents, cotangent)
    both_ext = rims_from((latents, cotangent), tails, heads)
    row_index = lax.axis_index("rows")
    inside = jnp.concatenate(
        [
            jnp.where(row_index > 0, 1.0, 0.0)[None],
            jnp.ones((slab_rows,), jnp.float32),
            jnp.where(row_index < row_devices - 1, 1.0, 0.0)[None],
        ]
    )[None, :, None, None]
    values = latents.astype(jnp.float32)
    chan_mean = pivot + shift_sum / positions
    chan_m2 = jnp.maximum(shift_sq - shift_sum * (shift_sum / positions), 0.0)
    chan_mean_g = chan_mean.reshape(images, groups, CH_GROUP)
    local_mean = jnp.mean(chan_mean_g, axis=2)
    spread = chan_mean_g - local_mean[:, :, None]
    local_m2 = jnp.sum(chan_m2.reshape(images, groups, CH_GROUP), axis=2) + positions * jnp.sum(
        spread * spread, axis=2
    )
    group_mean, group_m2 = merge_stats(local_mean, local_m2, positions * CH_GROUP, "rows")
    inv_std = lax.rsqrt(group_m2 / group_cells + NORM_EPS)
    mean_ch = jnp.repeat(group_mean, CH_GROUP, axis=1)[:, None, None, :]
    rstd_ch = jnp.repeat(inv_std, CH_GROUP, axis=1)[:, None, None, :]
    normalized_ext = (both_ext[0].astype(jnp.float32) - mean_ch) * rstd_ch
    pre_act_ext = normalized_ext * gn_gain + gn_bias
    extended = (jax.nn.silu(pre_act_ext) * inside).astype(jnp.bfloat16)
    normalized = normalized_ext[:, 1 : 1 + slab_rows]
    pre_act = pre_act_ext[:, 1 : 1 + slab_rows]
    temb_features = jax.nn.silu(sinusoid(timesteps, temb_weight.shape[0])).astype(jnp.bfloat16)
    time_shift = jnp.dot(temb_features, temb_weight, preferred_element_type=jnp.float32)
    features = conv_taps(extended, conv_weight, slab_rows, col_count, False)
    features_out = (features + conv_bias + time_shift[:, None, None, :]).astype(jnp.bfloat16)
    hidden_grad = conv_taps(both_ext[1], conv_weight, slab_rows, col_count, True)
    sigmoid_act = jax.nn.sigmoid(pre_act)
    act_grad = hidden_grad * sigmoid_act * (1.0 + pre_act * (1.0 - sigmoid_act))
    chan_weighted = jnp.sum(act_grad * normalized, axis=(1, 2))
    chan_plain = jnp.sum(act_grad, axis=(1, 2))
    row_sums = all_sum(jnp.stack([chan_weighted, chan_plain, chan_output], axis=1), "rows")
    row_weighted, row_plain = row_sums[:, 0], row_sums[:, 1]
    first_sum = jnp.sum((row_plain * gn_gain).reshape(images, groups, CH_GROUP), axis=2)
    second_sum = jnp.sum((row_weighted * gn_gain).reshape(images, groups, CH_GROUP), axis=2)
    param_sums = all_sum(jnp.sum(row_sums, axis=0), "dp")
    first_ch = jnp.repeat(first_sum / group_cells, CH_GROUP, axis=1)[:, None, None, :]
    second_ch = jnp.repeat(second_sum / group_cells, CH_GROUP, axis=1)[:, None, None, :]
    input_grad = rstd_ch * (act_grad * gn_gain - first_ch - normalized * second_ch)
    input_grad = input_grad.astype(jnp.bfloat16)
    grad_scale = 1.0 / math.sqrt(images * lax.axis_size("dp") * slab_rows * row_devices * col_count)
    return (features_out, input_grad, param_sums * grad_scale)


def solution(mesh):
    placed = (
        P("dp", "rows", None, None),
        P("dp"),
        P(),
        P(),
        P(),
        P(),
        P(),
        P("dp", "rows", None, None),
    )
    return jax.shard_map(
        per_device,
        mesh=mesh,
        in_specs=placed,
        out_specs=(P("dp", "rows", None, None), P("dp", "rows", None, None), P()),
        check_vma=False,
    )
```

```python
import math

import jax
import jax.numpy as jnp
from jax import lax
from jax.experimental import pallas as pl
from jax.sharding import PartitionSpec as P

CH_GROUP = 40


NORM_EPS = 1e-05


def padded_2(cells, sides, width):
    for axis, dim in sides:
        count = lax.axis_size(axis)
        ends = count - 1
        head = lax.slice_in_dim(cells, 0, width, axis=dim)
        tail = lax.slice_in_dim(cells, cells.shape[dim] - width, cells.shape[dim], axis=dim)
        cells = jnp.concatenate(
            [
                lax.ppermute(tail, axis, [(i, (i + 1) % count) for i in range(ends)]),
                cells,
                lax.ppermute(head, axis, [((i + 1) % count, i) for i in range(ends)]),
            ],
            axis=dim,
        )
    return cells


def is_pow2(count):
    return count & (count - 1) == 0


def all_sum(value, axis):
    count = lax.axis_size(axis)
    if not is_pow2(count):
        return lax.psum(value, axis)
    step = count // 2
    while step >= 1:
        other = lax.ppermute(value, axis, [(i, i ^ step) for i in range(count)])
        value = value + other
        step //= 2
    return value


def merge_stats(mean, m2, cells, axis):
    count = lax.axis_size(axis)
    if not is_pow2(count):
        means = lax.all_gather(mean, axis)
        total_mean = jnp.mean(means, axis=0)
        spread = means - total_mean
        return total_mean, jnp.sum(lax.all_gather(m2, axis), axis=0) + cells * jnp.sum(spread * spread, axis=0)
    value = jnp.stack([mean, m2])
    step = count // 2
    size = 1
    while step >= 1:
        other = lax.ppermute(value, axis, [(i, i ^ step) for i in range(count)])
        delta = other[0] - value[0]
        value = jnp.stack(
            [(value[0] + other[0]) * 0.5, value[1] + other[1] + delta * delta * (cells * size * 0.5)]
        )
        step //= 2
        size *= 2
    return value[0], value[1]


def edge_kernel(lat_ref, ct_ref, ct_sum_ref, tails_ref, heads_ref):
    slab_rows = lat_ref.shape[1]
    ct_rows = jnp.sum(ct_ref[...].astype(jnp.float32), axis=1)
    ct_sum_ref[...] = jnp.sum(ct_rows, axis=1)
    tails_ref[0] = lat_ref[:, slab_rows - 1]
    tails_ref[1] = ct_ref[:, slab_rows - 1]
    heads_ref[0] = lat_ref[:, 0]
    heads_ref[1] = ct_ref[:, 0]


def edge_pass(latents, cotangent):
    images, _, col_count, channels = latents.shape
    vec = jax.ShapeDtypeStruct((images, channels), jnp.float32)
    edge = jax.ShapeDtypeStruct((2, images, col_count, channels), latents.dtype)
    return pl.pallas_call(edge_kernel, out_shape=(vec, edge, edge))(latents, cotangent)


def rims_from(fields, tails, heads):
    count = lax.axis_size("rows")
    from_above = lax.ppermute(tails, "rows", [(i, i + 1) for i in range(count - 1)])
    from_below = lax.ppermute(heads, "rows", [(i + 1, i) for i in range(count - 1)])
    return [
        jnp.concatenate([from_above[k][:, None], field, from_below[k][:, None]], axis=1)
        for k, field in enumerate(fields)
    ]


def sinusoid(steps, embed_dim):
    half_dim = embed_dim // 2
    frequencies = jnp.exp(-math.log(10000.0) * jnp.arange(half_dim).astype(jnp.float32) / half_dim)
    angles = steps.astype(jnp.float32)[:, None] * frequencies[None, :]
    return jnp.concatenate([jnp.cos(angles), jnp.sin(angles)], axis=1)


def with_rim(field):
    return padded_2(field, (("rows", 2),), 1)


def conv_taps(extended, weight, slab_rows, col_count, backward):
    padded = jnp.pad(extended, ((0, 0), (0, 0), (1, 1), (0, 0)))
    channels = padded.shape[3]
    total = None
    for tap_row in range(3):
        for tap_col in range(3):
            if backward:
                row_start, col_start = (2 - tap_row, 2 - tap_col)
                dims = (((1,), (1,)), ((), ()))
            else:
                row_start, col_start = (tap_row, tap_col)
                dims = (((1,), (0,)), ((), ()))
            window = padded[
                :, row_start : row_start + slab_rows, col_start : col_start + col_count
            ].reshape(-1, channels)
            tap_term = lax.dot_general(
                window, weight[tap_row, tap_col], dims, preferred_element_type=jnp.float32
            )
            total = tap_term if total is None else total + tap_term
    return total.reshape(-1, slab_rows, col_count, weight.shape[3])


def per_device(
    latents, timesteps, gn_gain, gn_bias, conv_weight, conv_bias, temb_weight, cotangent
):
    images, slab_rows, col_count, channels = latents.shape
    groups = channels // CH_GROUP
    row_devices = lax.axis_size("rows")
    group_cells = slab_rows * row_devices * col_count * CH_GROUP
    positions = slab_rows * col_count
    chan_output, tails, heads = edge_pass(latents, cotangent)
    both_ext = rims_from((latents, cotangent), tails, heads)
    row_index = lax.axis_index("rows")
    inside = jnp.concatenate(
        [
            jnp.where(row_index > 0, 1.0, 0.0)[None],
            jnp.ones((slab_rows,), jnp.float32),
            jnp.where(row_index < row_devices - 1, 1.0, 0.0)[None],
        ]
    )[None, :, None, None]
    values = latents.astype(jnp.float32)
    pivot = latents[:, 0, 0, :].astype(jnp.float32)
    shifted = latents.astype(jnp.float32) - pivot[:, None, None, :]
    shift_sum = jnp.sum(shifted, axis=(1, 2))
    shift_sq = jnp.sum(shifted * shifted, axis=(1, 2))
    chan_mean = pivot + shift_sum / positions
    chan_m2 = jnp.maximum(shift_sq - shift_sum * (shift_sum / positions), 0.0)
    chan_mean_g = chan_mean.reshape(images, groups, CH_GROUP)
    local_mean = jnp.mean(chan_mean_g, axis=2)
    spread = chan_mean_g - local_mean[:, :, None]
    local_m2 = jnp.sum(chan_m2.reshape(images, groups, CH_GROUP), axis=2) + positions * jnp.sum(
        spread * spread, axis=2
    )
    group_mean, group_m2 = merge_stats(local_mean, local_m2, positions * CH_GROUP, "rows")
    inv_std = lax.rsqrt(group_m2 / group_cells + NORM_EPS)
    mean_ch = jnp.repeat(group_mean, CH_GROUP, axis=1)[:, None, None, :]
    rstd_ch = jnp.repeat(inv_std, CH_GROUP, axis=1)[:, None, None, :]
    normalized_ext = (both_ext[0].astype(jnp.float32) - mean_ch) * rstd_ch
    pre_act_ext = normalized_ext * gn_gain + gn_bias
    extended = (jax.nn.silu(pre_act_ext) * inside).astype(jnp.bfloat16)
    normalized = normalized_ext[:, 1 : 1 + slab_rows]
    pre_act = pre_act_ext[:, 1 : 1 + slab_rows]
    temb_features = jax.nn.silu(sinusoid(timesteps, temb_weight.shape[0])).astype(jnp.bfloat16)
    time_shift = jnp.dot(temb_features, temb_weight, preferred_element_type=jnp.float32)
    features = conv_taps(extended, conv_weight, slab_rows, col_count, False)
    features_out = (features + conv_bias + time_shift[:, None, None, :]).astype(jnp.bfloat16)
    hidden_grad = conv_taps(both_ext[1], conv_weight, slab_rows, col_count, True)
    sigmoid_act = jax.nn.sigmoid(pre_act)
    act_grad = hidden_grad * sigmoid_act * (1.0 + pre_act * (1.0 - sigmoid_act))
    chan_weighted = jnp.sum(act_grad * normalized, axis=(1, 2))
    chan_plain = jnp.sum(act_grad, axis=(1, 2))
    row_sums = all_sum(jnp.stack([chan_weighted, chan_plain, chan_output], axis=1), "rows")
    row_weighted, row_plain = row_sums[:, 0], row_sums[:, 1]
    first_sum = jnp.sum((row_plain * gn_gain).reshape(images, groups, CH_GROUP), axis=2)
    second_sum = jnp.sum((row_weighted * gn_gain).reshape(images, groups, CH_GROUP), axis=2)
    param_sums = all_sum(jnp.sum(row_sums, axis=0), "dp")
    first_ch = jnp.repeat(first_sum / group_cells, CH_GROUP, axis=1)[:, None, None, :]
    second_ch = jnp.repeat(second_sum / group_cells, CH_GROUP, axis=1)[:, None, None, :]
    input_grad = rstd_ch * (act_grad * gn_gain - first_ch - normalized * second_ch)
    input_grad = input_grad.astype(jnp.bfloat16)
    grad_scale = 1.0 / math.sqrt(images * lax.axis_size("dp") * slab_rows * row_devices * col_count)
    return (features_out, input_grad, param_sums * grad_scale)


def solution(mesh):
    placed = (
        P("dp", "rows", None, None),
        P("dp"),
        P(),
        P(),
        P(),
        P(),
        P(),
        P("dp", "rows", None, None),
    )
    return jax.shard_map(
        per_device,
        mesh=mesh,
        in_specs=placed,
        out_specs=(P("dp", "rows", None, None), P("dp", "rows", None, None), P()),
        check_vma=False,
    )
```

```python
import math

import jax
import jax.numpy as jnp
from jax import lax
from jax.sharding import PartitionSpec as P

CH_GROUP = 40


NORM_EPS = 1e-05


def padded_2(cells, sides, width):
    for axis, dim in sides:
        count = lax.axis_size(axis)
        ends = count - 1
        head = lax.slice_in_dim(cells, 0, width, axis=dim)
        tail = lax.slice_in_dim(cells, cells.shape[dim] - width, cells.shape[dim], axis=dim)
        cells = jnp.concatenate(
            [
                lax.ppermute(tail, axis, [(i, (i + 1) % count) for i in range(ends)]),
                cells,
                lax.ppermute(head, axis, [((i + 1) % count, i) for i in range(ends)]),
            ],
            axis=dim,
        )
    return cells


def is_pow2(count):
    return count & (count - 1) == 0


def all_sum(value, axis):
    count = lax.axis_size(axis)
    if not is_pow2(count):
        return lax.psum(value, axis)
    step = count // 2
    while step >= 1:
        other = lax.ppermute(value, axis, [(i, i ^ step) for i in range(count)])
        value = value + other
        step //= 2
    return value


def merge_stats(mean, m2, cells, axis, riders):
    count = lax.axis_size(axis)
    if not is_pow2(count):
        means = lax.all_gather(mean, axis)
        total_mean = jnp.mean(means, axis=0)
        spread = means - total_mean
        total_m2 = jnp.sum(lax.all_gather(m2, axis), axis=0) + cells * jnp.sum(spread * spread, axis=0)
        return total_mean, total_m2, riders
    value = jnp.stack([mean, m2])
    step = 1
    while step < count:
        other = lax.ppermute(value, axis, [(i, i ^ step) for i in range(count)])
        delta = other[0] - value[0]
        value = jnp.stack(
            [(value[0] + other[0]) * 0.5, value[1] + other[1] + delta * delta * (cells * step * 0.5)]
        )
        if step == 1:
            value, riders = lax.optimization_barrier((value, riders))
        step *= 2
    return value[0], value[1], riders


def sinusoid(steps, embed_dim):
    half_dim = embed_dim // 2
    frequencies = jnp.exp(-math.log(10000.0) * jnp.arange(half_dim).astype(jnp.float32) / half_dim)
    angles = steps.astype(jnp.float32)[:, None] * frequencies[None, :]
    return jnp.concatenate([jnp.cos(angles), jnp.sin(angles)], axis=1)


def with_rim(field):
    return padded_2(field, (("rows", 2),), 1)


def conv_taps(extended, weight, slab_rows, col_count, backward):
    padded = jnp.pad(extended, ((0, 0), (0, 0), (1, 1), (0, 0)))
    channels = padded.shape[3]
    total = None
    for tap_row in range(3):
        for tap_col in range(3):
            if backward:
                row_start, col_start = (2 - tap_row, 2 - tap_col)
                dims = (((1,), (1,)), ((), ()))
            else:
                row_start, col_start = (tap_row, tap_col)
                dims = (((1,), (0,)), ((), ()))
            window = padded[
                :, row_start : row_start + slab_rows, col_start : col_start + col_count
            ].reshape(-1, channels)
            tap_term = lax.dot_general(
                window, weight[tap_row, tap_col], dims, preferred_element_type=jnp.float32
            )
            total = tap_term if total is None else total + tap_term
    return total.reshape(-1, slab_rows, col_count, weight.shape[3])


def per_device(
    latents, timesteps, gn_gain, gn_bias, conv_weight, conv_bias, temb_weight, cotangent
):
    images, slab_rows, col_count, channels = latents.shape
    groups = channels // CH_GROUP
    row_devices = lax.axis_size("rows")
    group_cells = slab_rows * row_devices * col_count * CH_GROUP
    positions = slab_rows * col_count
    row_index = lax.axis_index("rows")
    inside = jnp.concatenate(
        [
            jnp.where(row_index > 0, 1.0, 0.0)[None],
            jnp.ones((slab_rows,), jnp.float32),
            jnp.where(row_index < row_devices - 1, 1.0, 0.0)[None],
        ]
    )[None, :, None, None]
    values = latents.astype(jnp.float32)
    pivot = latents[:, 0, 0, :].astype(jnp.float32)
    shifted = latents.astype(jnp.float32) - pivot[:, None, None, :]
    shift_sum = jnp.sum(shifted, axis=(1, 2))
    shift_sq = jnp.sum(shifted * shifted, axis=(1, 2))
    chan_mean = pivot + shift_sum / positions
    chan_m2 = jnp.maximum(shift_sq - shift_sum * (shift_sum / positions), 0.0)
    chan_mean_g = chan_mean.reshape(images, groups, CH_GROUP)
    local_mean = jnp.mean(chan_mean_g, axis=2)
    spread = chan_mean_g - local_mean[:, :, None]
    local_m2 = jnp.sum(chan_m2.reshape(images, groups, CH_GROUP), axis=2) + positions * jnp.sum(
        spread * spread, axis=2
    )
    group_mean, group_m2, pair = merge_stats(
        local_mean, local_m2, positions * CH_GROUP, "rows", jnp.stack([latents, cotangent])
    )
    both_ext = with_rim(pair)
    inv_std = lax.rsqrt(group_m2 / group_cells + NORM_EPS)
    mean_ch = jnp.repeat(group_mean, CH_GROUP, axis=1)[:, None, None, :]
    rstd_ch = jnp.repeat(inv_std, CH_GROUP, axis=1)[:, None, None, :]
    normalized_ext = (both_ext[0].astype(jnp.float32) - mean_ch) * rstd_ch
    pre_act_ext = normalized_ext * gn_gain + gn_bias
    extended = (jax.nn.silu(pre_act_ext) * inside).astype(jnp.bfloat16)
    normalized = normalized_ext[:, 1 : 1 + slab_rows]
    pre_act = pre_act_ext[:, 1 : 1 + slab_rows]
    temb_features = jax.nn.silu(sinusoid(timesteps, temb_weight.shape[0])).astype(jnp.bfloat16)
    time_shift = jnp.dot(temb_features, temb_weight, preferred_element_type=jnp.float32)
    features = conv_taps(extended, conv_weight, slab_rows, col_count, False)
    features_out = (features + conv_bias + time_shift[:, None, None, :]).astype(jnp.bfloat16)
    hidden_grad = conv_taps(both_ext[1], conv_weight, slab_rows, col_count, True)
    sigmoid_act = jax.nn.sigmoid(pre_act)
    act_grad = hidden_grad * sigmoid_act * (1.0 + pre_act * (1.0 - sigmoid_act))
    chan_weighted = jnp.sum(act_grad * normalized, axis=(1, 2))
    chan_plain = jnp.sum(act_grad, axis=(1, 2))
    chan_output = jnp.sum(cotangent.astype(jnp.float32), axis=(1, 2))
    row_sums = all_sum(jnp.stack([chan_weighted, chan_plain, chan_output], axis=1), "rows")
    row_weighted, row_plain = row_sums[:, 0], row_sums[:, 1]
    first_sum = jnp.sum((row_plain * gn_gain).reshape(images, groups, CH_GROUP), axis=2)
    second_sum = jnp.sum((row_weighted * gn_gain).reshape(images, groups, CH_GROUP), axis=2)
    param_sums = all_sum(jnp.sum(row_sums, axis=0), "dp")
    first_ch = jnp.repeat(first_sum / group_cells, CH_GROUP, axis=1)[:, None, None, :]
    second_ch = jnp.repeat(second_sum / group_cells, CH_GROUP, axis=1)[:, None, None, :]
    input_grad = rstd_ch * (act_grad * gn_gain - first_ch - normalized * second_ch)
    input_grad = input_grad.astype(jnp.bfloat16)
    grad_scale = 1.0 / math.sqrt(images * lax.axis_size("dp") * slab_rows * row_devices * col_count)
    return (features_out, input_grad, param_sums * grad_scale)


def solution(mesh):
    placed = (
        P("dp", "rows", None, None),
        P("dp"),
        P(),
        P(),
        P(),
        P(),
        P(),
        P("dp", "rows", None, None),
    )
    return jax.shard_map(
        per_device,
        mesh=mesh,
        in_specs=placed,
        out_specs=(P("dp", "rows", None, None), P("dp", "rows", None, None), P()),
        check_vma=False,
    )
```

```python
import math

import jax
import jax.numpy as jnp
from jax import lax
from jax.sharding import PartitionSpec as P

CH_GROUP = 40


NORM_EPS = 1e-05


def padded_2(cells, sides, width):
    for axis, dim in sides:
        count = lax.axis_size(axis)
        ends = count - 1
        head = lax.slice_in_dim(cells, 0, width, axis=dim)
        tail = lax.slice_in_dim(cells, cells.shape[dim] - width, cells.shape[dim], axis=dim)
        cells = jnp.concatenate(
            [
                lax.ppermute(tail, axis, [(i, (i + 1) % count) for i in range(ends)]),
                cells,
                lax.ppermute(head, axis, [((i + 1) % count, i) for i in range(ends)]),
            ],
            axis=dim,
        )
    return cells


def is_pow2(count):
    return count & (count - 1) == 0


def all_sum(value, axis):
    count = lax.axis_size(axis)
    if not is_pow2(count):
        return lax.psum(value, axis)
    step = count // 2
    while step >= 1:
        other = lax.ppermute(value, axis, [(i, i ^ step) for i in range(count)])
        value = value + other
        step //= 2
    return value


def merge_stats(mean, m2, cells, axis):
    count = lax.axis_size(axis)
    if not is_pow2(count):
        means = lax.all_gather(mean, axis)
        total_mean = jnp.mean(means, axis=0)
        spread = means - total_mean
        return total_mean, jnp.sum(lax.all_gather(m2, axis), axis=0) + cells * jnp.sum(spread * spread, axis=0)
    value = jnp.stack([mean, m2])
    step = count // 2
    size = 1
    while step >= 1:
        other = lax.ppermute(value, axis, [(i, i ^ step) for i in range(count)])
        delta = other[0] - value[0]
        value = jnp.stack(
            [(value[0] + other[0]) * 0.5, value[1] + other[1] + delta * delta * (cells * size * 0.5)]
        )
        step //= 2
        size *= 2
    return value[0], value[1]


def sinusoid(steps, embed_dim):
    half_dim = embed_dim // 2
    frequencies = jnp.exp(-math.log(10000.0) * jnp.arange(half_dim).astype(jnp.float32) / half_dim)
    angles = steps.astype(jnp.float32)[:, None] * frequencies[None, :]
    return jnp.concatenate([jnp.cos(angles), jnp.sin(angles)], axis=1)


def with_rim(field):
    return padded_2(field, (("rows", 2),), 1)


def conv_taps(extended, weight, slab_rows, col_count, backward):
    padded = jnp.pad(extended, ((0, 0), (0, 0), (1, 1), (0, 0)))
    channels = padded.shape[3]
    total = None
    for tap_row in range(3):
        for tap_col in range(3):
            if backward:
                row_start, col_start = (2 - tap_row, 2 - tap_col)
                dims = (((1,), (1,)), ((), ()))
            else:
                row_start, col_start = (tap_row, tap_col)
                dims = (((1,), (0,)), ((), ()))
            window = padded[
                :, row_start : row_start + slab_rows, col_start : col_start + col_count
            ].reshape(-1, channels)
            tap_term = lax.dot_general(
                window, weight[tap_row, tap_col], dims, preferred_element_type=jnp.float32
            )
            total = tap_term if total is None else total + tap_term
    return total.reshape(-1, slab_rows, col_count, weight.shape[3])


def per_device(
    latents, timesteps, gn_gain, gn_bias, conv_weight, conv_bias, temb_weight, cotangent
):
    images, slab_rows, col_count, channels = latents.shape
    groups = channels // CH_GROUP
    row_devices = lax.axis_size("rows")
    group_cells = slab_rows * row_devices * col_count * CH_GROUP
    positions = slab_rows * col_count
    both_ext = with_rim(jnp.stack([latents, cotangent]))
    row_index = lax.axis_index("rows")
    inside = jnp.concatenate(
        [
            jnp.where(row_index > 0, 1.0, 0.0)[None],
            jnp.ones((slab_rows,), jnp.float32),
            jnp.where(row_index < row_devices - 1, 1.0, 0.0)[None],
        ]
    )[None, :, None, None]
    values = latents.astype(jnp.float32)
    pivot = latents[:, 0, 0, :].astype(jnp.float32)
    shifted = latents.astype(jnp.float32) - pivot[:, None, None, :]
    shift_sum = jnp.sum(shifted, axis=(1, 2))
    shift_sq = jnp.sum(shifted * shifted, axis=(1, 2))
    chan_mean = pivot + shift_sum / positions
    chan_m2 = jnp.maximum(shift_sq - shift_sum * (shift_sum / positions), 0.0)
    chan_mean_g = chan_mean.reshape(images, groups, CH_GROUP)
    local_mean = jnp.mean(chan_mean_g, axis=2)
    spread = chan_mean_g - local_mean[:, :, None]
    local_m2 = jnp.sum(chan_m2.reshape(images, groups, CH_GROUP), axis=2) + positions * jnp.sum(
        spread * spread, axis=2
    )
    group_mean, group_m2 = merge_stats(local_mean, local_m2, positions * CH_GROUP, "rows")
    inv_std = lax.rsqrt(group_m2 / group_cells + NORM_EPS)
    inv_std, grad_src = lax.optimization_barrier((inv_std, cotangent))
    chan_output = jnp.sum(grad_src.astype(jnp.float32), axis=(1, 2))
    mean_ch = jnp.repeat(group_mean, CH_GROUP, axis=1)[:, None, None, :]
    rstd_ch = jnp.repeat(inv_std, CH_GROUP, axis=1)[:, None, None, :]
    normalized_ext = (both_ext[0].astype(jnp.float32) - mean_ch) * rstd_ch
    pre_act_ext = normalized_ext * gn_gain + gn_bias
    extended = (jax.nn.silu(pre_act_ext) * inside).astype(jnp.bfloat16)
    normalized = normalized_ext[:, 1 : 1 + slab_rows]
    pre_act = pre_act_ext[:, 1 : 1 + slab_rows]
    temb_features = jax.nn.silu(sinusoid(timesteps, temb_weight.shape[0])).astype(jnp.bfloat16)
    time_shift = jnp.dot(temb_features, temb_weight, preferred_element_type=jnp.float32)
    features = conv_taps(extended, conv_weight, slab_rows, col_count, False)
    features_out = (features + conv_bias + time_shift[:, None, None, :]).astype(jnp.bfloat16)
    hidden_grad = conv_taps(both_ext[1], conv_weight, slab_rows, col_count, True)
    sigmoid_act = jax.nn.sigmoid(pre_act)
    act_grad = hidden_grad * sigmoid_act * (1.0 + pre_act * (1.0 - sigmoid_act))
    chan_weighted = jnp.sum(act_grad * normalized, axis=(1, 2))
    chan_plain = jnp.sum(act_grad, axis=(1, 2))
    row_sums = all_sum(jnp.stack([chan_weighted, chan_plain, chan_output], axis=1), "rows")
    row_weighted, row_plain = row_sums[:, 0], row_sums[:, 1]
    first_sum = jnp.sum((row_plain * gn_gain).reshape(images, groups, CH_GROUP), axis=2)
    second_sum = jnp.sum((row_weighted * gn_gain).reshape(images, groups, CH_GROUP), axis=2)
    param_sums = all_sum(jnp.sum(row_sums, axis=0), "dp")
    first_ch = jnp.repeat(first_sum / group_cells, CH_GROUP, axis=1)[:, None, None, :]
    second_ch = jnp.repeat(second_sum / group_cells, CH_GROUP, axis=1)[:, None, None, :]
    input_grad = rstd_ch * (act_grad * gn_gain - first_ch - normalized * second_ch)
    input_grad = input_grad.astype(jnp.bfloat16)
    grad_scale = 1.0 / math.sqrt(images * lax.axis_size("dp") * slab_rows * row_devices * col_count)
    return (features_out, input_grad, param_sums * grad_scale)


def solution(mesh):
    placed = (
        P("dp", "rows", None, None),
        P("dp"),
        P(),
        P(),
        P(),
        P(),
        P(),
        P("dp", "rows", None, None),
    )
    return jax.shard_map(
        per_device,
        mesh=mesh,
        in_specs=placed,
        out_specs=(P("dp", "rows", None, None), P("dp", "rows", None, None), P()),
        check_vma=False,
    )
```

```python
import math

import jax
import jax.numpy as jnp
from jax import lax
from jax.sharding import PartitionSpec as P

CH_GROUP = 40


NORM_EPS = 1e-05


def padded_2(cells, sides, width):
    for axis, dim in sides:
        count = lax.axis_size(axis)
        ends = count - 1
        head = lax.slice_in_dim(cells, 0, width, axis=dim)
        tail = lax.slice_in_dim(cells, cells.shape[dim] - width, cells.shape[dim], axis=dim)
        cells = jnp.concatenate(
            [
                lax.ppermute(tail, axis, [(i, (i + 1) % count) for i in range(ends)]),
                cells,
                lax.ppermute(head, axis, [((i + 1) % count, i) for i in range(ends)]),
            ],
            axis=dim,
        )
    return cells


def is_pow2(count):
    return count & (count - 1) == 0


def all_sum(value, axis):
    count = lax.axis_size(axis)
    if not is_pow2(count):
        return lax.psum(value, axis)
    step = count // 2
    while step >= 1:
        other = lax.ppermute(value, axis, [(i, i ^ step) for i in range(count)])
        value = value + other
        step //= 2
    return value


def merge_stats(mean, m2, cells, axis):
    count = lax.axis_size(axis)
    if not is_pow2(count):
        means = lax.all_gather(mean, axis)
        total_mean = jnp.mean(means, axis=0)
        spread = means - total_mean
        return total_mean, jnp.sum(lax.all_gather(m2, axis), axis=0) + cells * jnp.sum(spread * spread, axis=0)
    value = jnp.stack([mean, m2])
    step = count // 2
    size = 1
    while step >= 1:
        other = lax.ppermute(value, axis, [(i, i ^ step) for i in range(count)])
        delta = other[0] - value[0]
        value = jnp.stack(
            [(value[0] + other[0]) * 0.5, value[1] + other[1] + delta * delta * (cells * size * 0.5)]
        )
        step //= 2
        size *= 2
    return value[0], value[1]


def sinusoid(steps, embed_dim):
    half_dim = embed_dim // 2
    frequencies = jnp.exp(-math.log(10000.0) * jnp.arange(half_dim).astype(jnp.float32) / half_dim)
    angles = steps.astype(jnp.float32)[:, None] * frequencies[None, :]
    return jnp.concatenate([jnp.cos(angles), jnp.sin(angles)], axis=1)


def with_rim(field):
    return padded_2(field, (("rows", 2),), 1)


def conv_taps(extended, weight, slab_rows, col_count, backward):
    padded = jnp.pad(extended, ((0, 0), (0, 0), (1, 1), (0, 0)))
    channels = padded.shape[3]
    total = None
    for tap_row in range(3):
        for tap_col in range(3):
            if backward:
                row_start, col_start = (2 - tap_row, 2 - tap_col)
                dims = (((1,), (1,)), ((), ()))
            else:
                row_start, col_start = (tap_row, tap_col)
                dims = (((1,), (0,)), ((), ()))
            window = padded[
                :, row_start : row_start + slab_rows, col_start : col_start + col_count
            ].reshape(-1, channels)
            tap_term = lax.dot_general(
                window, weight[tap_row, tap_col], dims, preferred_element_type=jnp.float32
            )
            total = tap_term if total is None else total + tap_term
    return total.reshape(-1, slab_rows, col_count, weight.shape[3])


def per_device(
    latents, timesteps, gn_gain, gn_bias, conv_weight, conv_bias, temb_weight, cotangent
):
    images, slab_rows, col_count, channels = latents.shape
    groups = channels // CH_GROUP
    row_devices = lax.axis_size("rows")
    group_cells = slab_rows * row_devices * col_count * CH_GROUP
    positions = slab_rows * col_count
    both_ext = with_rim(jnp.stack([latents, cotangent]))
    row_index = lax.axis_index("rows")
    inside = jnp.concatenate(
        [
            jnp.where(row_index > 0, 1.0, 0.0)[None],
            jnp.ones((slab_rows,), jnp.float32),
            jnp.where(row_index < row_devices - 1, 1.0, 0.0)[None],
        ]
    )[None, :, None, None]
    values = latents.astype(jnp.float32)
    pivot = latents[:, 0, 0, :].astype(jnp.float32)
    shifted = latents.astype(jnp.float32) - pivot[:, None, None, :]
    shift_sum = jnp.sum(shifted, axis=(1, 2))
    shift_sq = jnp.sum(shifted * shifted, axis=(1, 2))
    chan_mean = pivot + shift_sum / positions
    chan_m2 = jnp.maximum(shift_sq - shift_sum * (shift_sum / positions), 0.0)
    chan_mean_g = chan_mean.reshape(images, groups, CH_GROUP)
    local_mean = jnp.mean(chan_mean_g, axis=2)
    spread = chan_mean_g - local_mean[:, :, None]
    local_m2 = jnp.sum(chan_m2.reshape(images, groups, CH_GROUP), axis=2) + positions * jnp.sum(
        spread * spread, axis=2
    )
    group_mean, group_m2 = merge_stats(local_mean, local_m2, positions * CH_GROUP, "rows")
    inv_std = lax.rsqrt(group_m2 / group_cells + NORM_EPS)
    inv_std, grad_src, steps = lax.optimization_barrier((inv_std, cotangent, timesteps))
    temb_features = jax.nn.silu(sinusoid(steps, temb_weight.shape[0])).astype(jnp.bfloat16)
    time_shift = jnp.dot(temb_features, temb_weight, preferred_element_type=jnp.float32)
    chan_output = jnp.sum(grad_src.astype(jnp.float32), axis=(1, 2))
    mean_ch = jnp.repeat(group_mean, CH_GROUP, axis=1)[:, None, None, :]
    rstd_ch = jnp.repeat(inv_std, CH_GROUP, axis=1)[:, None, None, :]
    normalized_ext = (both_ext[0].astype(jnp.float32) - mean_ch) * rstd_ch
    pre_act_ext = normalized_ext * gn_gain + gn_bias
    extended = (jax.nn.silu(pre_act_ext) * inside).astype(jnp.bfloat16)
    normalized = normalized_ext[:, 1 : 1 + slab_rows]
    pre_act = pre_act_ext[:, 1 : 1 + slab_rows]
    features = conv_taps(extended, conv_weight, slab_rows, col_count, False)
    features_out = (features + conv_bias + time_shift[:, None, None, :]).astype(jnp.bfloat16)
    hidden_grad = conv_taps(both_ext[1], conv_weight, slab_rows, col_count, True)
    sigmoid_act = jax.nn.sigmoid(pre_act)
    act_grad = hidden_grad * sigmoid_act * (1.0 + pre_act * (1.0 - sigmoid_act))
    chan_weighted = jnp.sum(act_grad * normalized, axis=(1, 2))
    chan_plain = jnp.sum(act_grad, axis=(1, 2))
    row_sums = all_sum(jnp.stack([chan_weighted, chan_plain, chan_output], axis=1), "rows")
    row_weighted, row_plain = row_sums[:, 0], row_sums[:, 1]
    first_sum = jnp.sum((row_plain * gn_gain).reshape(images, groups, CH_GROUP), axis=2)
    second_sum = jnp.sum((row_weighted * gn_gain).reshape(images, groups, CH_GROUP), axis=2)
    param_sums = all_sum(jnp.sum(row_sums, axis=0), "dp")
    first_ch = jnp.repeat(first_sum / group_cells, CH_GROUP, axis=1)[:, None, None, :]
    second_ch = jnp.repeat(second_sum / group_cells, CH_GROUP, axis=1)[:, None, None, :]
    input_grad = rstd_ch * (act_grad * gn_gain - first_ch - normalized * second_ch)
    input_grad = input_grad.astype(jnp.bfloat16)
    grad_scale = 1.0 / math.sqrt(images * lax.axis_size("dp") * slab_rows * row_devices * col_count)
    return (features_out, input_grad, param_sums * grad_scale)


def solution(mesh):
    placed = (
        P("dp", "rows", None, None),
        P("dp"),
        P(),
        P(),
        P(),
        P(),
        P(),
        P("dp", "rows", None, None),
    )
    return jax.shard_map(
        per_device,
        mesh=mesh,
        in_specs=placed,
        out_specs=(P("dp", "rows", None, None), P("dp", "rows", None, None), P()),
        check_vma=False,
    )
```

```python
import math

import jax
import jax.numpy as jnp
from jax import lax
from jax.sharding import PartitionSpec as P

CH_GROUP = 40


NORM_EPS = 1e-05


def padded_2(cells, sides, width):
    for axis, dim in sides:
        count = lax.axis_size(axis)
        ends = count - 1
        head = lax.slice_in_dim(cells, 0, width, axis=dim)
        tail = lax.slice_in_dim(cells, cells.shape[dim] - width, cells.shape[dim], axis=dim)
        cells = jnp.concatenate(
            [
                lax.ppermute(tail, axis, [(i, (i + 1) % count) for i in range(ends)]),
                cells,
                lax.ppermute(head, axis, [((i + 1) % count, i) for i in range(ends)]),
            ],
            axis=dim,
        )
    return cells


def is_pow2(count):
    return count & (count - 1) == 0


def all_sum(value, axis):
    count = lax.axis_size(axis)
    if not is_pow2(count):
        return lax.psum(value, axis)
    step = count // 2
    while step >= 1:
        other = lax.ppermute(value, axis, [(i, i ^ step) for i in range(count)])
        value = value + other
        step //= 2
    return value


def merge_stats(mean, m2, cells, axis):
    count = lax.axis_size(axis)
    if not is_pow2(count):
        means = lax.all_gather(mean, axis)
        total_mean = jnp.mean(means, axis=0)
        spread = means - total_mean
        return total_mean, jnp.sum(lax.all_gather(m2, axis), axis=0) + cells * jnp.sum(spread * spread, axis=0)
    value = jnp.stack([mean, m2])
    step = count // 2
    size = 1
    while step >= 1:
        other = lax.ppermute(value, axis, [(i, i ^ step) for i in range(count)])
        delta = other[0] - value[0]
        value = jnp.stack(
            [(value[0] + other[0]) * 0.5, value[1] + other[1] + delta * delta * (cells * size * 0.5)]
        )
        step //= 2
        size *= 2
    return value[0], value[1]


def sinusoid(steps, embed_dim):
    half_dim = embed_dim // 2
    frequencies = jnp.exp(-math.log(10000.0) * jnp.arange(half_dim).astype(jnp.float32) / half_dim)
    angles = steps.astype(jnp.float32)[:, None] * frequencies[None, :]
    return jnp.concatenate([jnp.cos(angles), jnp.sin(angles)], axis=1)


def with_rim(field):
    return padded_2(field, (("rows", 2),), 1)


def conv_taps(extended, weight, slab_rows, col_count, backward):
    padded = jnp.pad(extended, ((0, 0), (0, 0), (1, 1), (0, 0)))
    channels = padded.shape[3]
    total = None
    for tap_row in range(3):
        for tap_col in range(3):
            if backward:
                row_start, col_start = (2 - tap_row, 2 - tap_col)
                dims = (((1,), (1,)), ((), ()))
            else:
                row_start, col_start = (tap_row, tap_col)
                dims = (((1,), (0,)), ((), ()))
            window = padded[
                :, row_start : row_start + slab_rows, col_start : col_start + col_count
            ].reshape(-1, channels)
            tap_term = lax.dot_general(
                window, weight[tap_row, tap_col], dims, preferred_element_type=jnp.float32
            )
            total = tap_term if total is None else total + tap_term
    return total.reshape(-1, slab_rows, col_count, weight.shape[3])


def per_device(
    latents, timesteps, gn_gain, gn_bias, conv_weight, conv_bias, temb_weight, cotangent
):
    images, slab_rows, col_count, channels = latents.shape
    groups = channels // CH_GROUP
    row_devices = lax.axis_size("rows")
    group_cells = slab_rows * row_devices * col_count * CH_GROUP
    positions = slab_rows * col_count
    both_ext = with_rim(jnp.stack([latents, cotangent]))
    row_index = lax.axis_index("rows")
    inside = jnp.concatenate(
        [
            jnp.where(row_index > 0, 1.0, 0.0)[None],
            jnp.ones((slab_rows,), jnp.float32),
            jnp.where(row_index < row_devices - 1, 1.0, 0.0)[None],
        ]
    )[None, :, None, None]
    values = latents.astype(jnp.float32)
    pivot = latents[:, :1, :1, :].astype(jnp.float32)
    shifted = latents.astype(jnp.float32) - pivot
    shift_sum = jnp.sum(shifted, axis=(1, 2))
    shift_sq = jnp.sum(shifted * shifted, axis=(1, 2))
    chan_mean = jnp.sum(latents.astype(jnp.float32), axis=(1, 2)) / positions
    chan_m2 = jnp.maximum(shift_sq - shift_sum * (shift_sum / positions), 0.0)
    chan_mean_g = chan_mean.reshape(images, groups, CH_GROUP)
    local_mean = jnp.mean(chan_mean_g, axis=2)
    spread = chan_mean_g - local_mean[:, :, None]
    local_m2 = jnp.sum(chan_m2.reshape(images, groups, CH_GROUP), axis=2) + positions * jnp.sum(
        spread * spread, axis=2
    )
    group_mean, group_m2 = merge_stats(local_mean, local_m2, positions * CH_GROUP, "rows")
    inv_std = lax.rsqrt(group_m2 / group_cells + NORM_EPS)
    inv_std, grad_src = lax.optimization_barrier((inv_std, cotangent))
    chan_output = jnp.sum(grad_src.astype(jnp.float32), axis=(1, 2))
    mean_ch = jnp.repeat(group_mean, CH_GROUP, axis=1)[:, None, None, :]
    rstd_ch = jnp.repeat(inv_std, CH_GROUP, axis=1)[:, None, None, :]
    normalized_ext = (both_ext[0].astype(jnp.float32) - mean_ch) * rstd_ch
    pre_act_ext = normalized_ext * gn_gain + gn_bias
    extended = (jax.nn.silu(pre_act_ext) * inside).astype(jnp.bfloat16)
    normalized = normalized_ext[:, 1 : 1 + slab_rows]
    pre_act = pre_act_ext[:, 1 : 1 + slab_rows]
    temb_features = jax.nn.silu(sinusoid(timesteps, temb_weight.shape[0])).astype(jnp.bfloat16)
    time_shift = jnp.dot(temb_features, temb_weight, preferred_element_type=jnp.float32)
    features = conv_taps(extended, conv_weight, slab_rows, col_count, False)
    features_out = (features + conv_bias + time_shift[:, None, None, :]).astype(jnp.bfloat16)
    hidden_grad = conv_taps(both_ext[1], conv_weight, slab_rows, col_count, True)
    sigmoid_act = jax.nn.sigmoid(pre_act)
    act_grad = hidden_grad * sigmoid_act * (1.0 + pre_act * (1.0 - sigmoid_act))
    chan_weighted = jnp.sum(act_grad * normalized, axis=(1, 2))
    chan_plain = jnp.sum(act_grad, axis=(1, 2))
    row_sums = all_sum(jnp.stack([chan_weighted, chan_plain, chan_output], axis=1), "rows")
    row_weighted, row_plain = row_sums[:, 0], row_sums[:, 1]
    first_sum = jnp.sum((row_plain * gn_gain).reshape(images, groups, CH_GROUP), axis=2)
    second_sum = jnp.sum((row_weighted * gn_gain).reshape(images, groups, CH_GROUP), axis=2)
    param_sums = all_sum(jnp.sum(row_sums, axis=0), "dp")
    first_ch = jnp.repeat(first_sum / group_cells, CH_GROUP, axis=1)[:, None, None, :]
    second_ch = jnp.repeat(second_sum / group_cells, CH_GROUP, axis=1)[:, None, None, :]
    input_grad = rstd_ch * (act_grad * gn_gain - first_ch - normalized * second_ch)
    input_grad = input_grad.astype(jnp.bfloat16)
    grad_scale = 1.0 / math.sqrt(images * lax.axis_size("dp") * slab_rows * row_devices * col_count)
    return (features_out, input_grad, param_sums * grad_scale)


def solution(mesh):
    placed = (
        P("dp", "rows", None, None),
        P("dp"),
        P(),
        P(),
        P(),
        P(),
        P(),
        P("dp", "rows", None, None),
    )
    return jax.shard_map(
        per_device,
        mesh=mesh,
        in_specs=placed,
        out_specs=(P("dp", "rows", None, None), P("dp", "rows", None, None), P()),
        check_vma=False,
    )
```

```python
import math

import jax
import jax.numpy as jnp
from jax import lax
from jax.sharding import PartitionSpec as P

CH_GROUP = 40


NORM_EPS = 1e-05


def padded_2(cells, sides, width):
    for axis, dim in sides:
        count = lax.axis_size(axis)
        ends = count - 1
        head = lax.slice_in_dim(cells, 0, width, axis=dim)
        tail = lax.slice_in_dim(cells, cells.shape[dim] - width, cells.shape[dim], axis=dim)
        cells = jnp.concatenate(
            [
                lax.ppermute(tail, axis, [(i, (i + 1) % count) for i in range(ends)]),
                cells,
                lax.ppermute(head, axis, [((i + 1) % count, i) for i in range(ends)]),
            ],
            axis=dim,
        )
    return cells


def is_pow2(count):
    return count & (count - 1) == 0


def all_sum(value, axis, riders=(), tie_after=-1):
    count = lax.axis_size(axis)
    if not is_pow2(count):
        return lax.psum(value, axis), riders
    step = count // 2
    done = 0
    while step >= 1:
        other = lax.ppermute(value, axis, [(i, i ^ step) for i in range(count)])
        value = value + other
        if done == tie_after:
            value, riders = lax.optimization_barrier((value, riders))
        done += 1
        step //= 2
    return value, riders


def merge_stats(mean, m2, cells, axis):
    count = lax.axis_size(axis)
    if not is_pow2(count):
        means = lax.all_gather(mean, axis)
        total_mean = jnp.mean(means, axis=0)
        spread = means - total_mean
        return total_mean, jnp.sum(lax.all_gather(m2, axis), axis=0) + cells * jnp.sum(spread * spread, axis=0)
    value = jnp.stack([mean, m2])
    step = count // 2
    size = 1
    while step >= 1:
        other = lax.ppermute(value, axis, [(i, i ^ step) for i in range(count)])
        delta = other[0] - value[0]
        value = jnp.stack(
            [(value[0] + other[0]) * 0.5, value[1] + other[1] + delta * delta * (cells * size * 0.5)]
        )
        step //= 2
        size *= 2
    return value[0], value[1]


def sinusoid(steps, embed_dim):
    half_dim = embed_dim // 2
    frequencies = jnp.exp(-math.log(10000.0) * jnp.arange(half_dim).astype(jnp.float32) / half_dim)
    angles = steps.astype(jnp.float32)[:, None] * frequencies[None, :]
    return jnp.concatenate([jnp.cos(angles), jnp.sin(angles)], axis=1)


def with_rim(field):
    return padded_2(field, (("rows", 2),), 1)


def conv_taps(extended, weight, slab_rows, col_count, backward):
    padded = jnp.pad(extended, ((0, 0), (0, 0), (1, 1), (0, 0)))
    channels = padded.shape[3]
    total = None
    for tap_row in range(3):
        for tap_col in range(3):
            if backward:
                row_start, col_start = (2 - tap_row, 2 - tap_col)
                dims = (((1,), (1,)), ((), ()))
            else:
                row_start, col_start = (tap_row, tap_col)
                dims = (((1,), (0,)), ((), ()))
            window = padded[
                :, row_start : row_start + slab_rows, col_start : col_start + col_count
            ].reshape(-1, channels)
            tap_term = lax.dot_general(
                window, weight[tap_row, tap_col], dims, preferred_element_type=jnp.float32
            )
            total = tap_term if total is None else total + tap_term
    return total.reshape(-1, slab_rows, col_count, weight.shape[3])


def per_device(
    latents, timesteps, gn_gain, gn_bias, conv_weight, conv_bias, temb_weight, cotangent
):
    images, slab_rows, col_count, channels = latents.shape
    groups = channels // CH_GROUP
    row_devices = lax.axis_size("rows")
    group_cells = slab_rows * row_devices * col_count * CH_GROUP
    positions = slab_rows * col_count
    both_ext = with_rim(jnp.stack([latents, cotangent]))
    row_index = lax.axis_index("rows")
    inside = jnp.concatenate(
        [
            jnp.where(row_index > 0, 1.0, 0.0)[None],
            jnp.ones((slab_rows,), jnp.float32),
            jnp.where(row_index < row_devices - 1, 1.0, 0.0)[None],
        ]
    )[None, :, None, None]
    values = latents.astype(jnp.float32)
    pivot = latents[:, 0, 0, :].astype(jnp.float32)
    shifted = latents.astype(jnp.float32) - pivot[:, None, None, :]
    shift_sum = jnp.sum(shifted, axis=(1, 2))
    shift_sq = jnp.sum(shifted * shifted, axis=(1, 2))
    chan_mean = pivot + shift_sum / positions
    chan_m2 = jnp.maximum(shift_sq - shift_sum * (shift_sum / positions), 0.0)
    chan_mean_g = chan_mean.reshape(images, groups, CH_GROUP)
    local_mean = jnp.mean(chan_mean_g, axis=2)
    spread = chan_mean_g - local_mean[:, :, None]
    local_m2 = jnp.sum(chan_m2.reshape(images, groups, CH_GROUP), axis=2) + positions * jnp.sum(
        spread * spread, axis=2
    )
    group_mean, group_m2 = merge_stats(local_mean, local_m2, positions * CH_GROUP, "rows")
    inv_std = lax.rsqrt(group_m2 / group_cells + NORM_EPS)
    inv_std, grad_src = lax.optimization_barrier((inv_std, cotangent))
    chan_output = jnp.sum(grad_src.astype(jnp.float32), axis=(1, 2))
    mean_ch = jnp.repeat(group_mean, CH_GROUP, axis=1)[:, None, None, :]
    rstd_ch = jnp.repeat(inv_std, CH_GROUP, axis=1)[:, None, None, :]
    normalized_ext = (both_ext[0].astype(jnp.float32) - mean_ch) * rstd_ch
    pre_act_ext = normalized_ext * gn_gain + gn_bias
    extended = (jax.nn.silu(pre_act_ext) * inside).astype(jnp.bfloat16)
    normalized = normalized_ext[:, 1 : 1 + slab_rows]
    pre_act = pre_act_ext[:, 1 : 1 + slab_rows]
    temb_features = jax.nn.silu(sinusoid(timesteps, temb_weight.shape[0])).astype(jnp.bfloat16)
    time_shift = jnp.dot(temb_features, temb_weight, preferred_element_type=jnp.float32)
    features = conv_taps(extended, conv_weight, slab_rows, col_count, False)
    features_out = (features + conv_bias + time_shift[:, None, None, :]).astype(jnp.bfloat16)
    hidden_grad = conv_taps(both_ext[1], conv_weight, slab_rows, col_count, True)
    sigmoid_act = jax.nn.sigmoid(pre_act)
    act_grad = hidden_grad * sigmoid_act * (1.0 + pre_act * (1.0 - sigmoid_act))
    chan_weighted = jnp.sum(act_grad * normalized, axis=(1, 2))
    chan_plain = jnp.sum(act_grad, axis=(1, 2))
    row_sums, _ = all_sum(jnp.stack([chan_weighted, chan_plain, chan_output], axis=1), "rows")
    row_weighted, row_plain = row_sums[:, 0], row_sums[:, 1]
    first_sum = jnp.sum((row_plain * gn_gain).reshape(images, groups, CH_GROUP), axis=2)
    second_sum = jnp.sum((row_weighted * gn_gain).reshape(images, groups, CH_GROUP), axis=2)
    first_ch = jnp.repeat(first_sum / group_cells, CH_GROUP, axis=1)[:, None, None, :]
    second_ch = jnp.repeat(second_sum / group_cells, CH_GROUP, axis=1)[:, None, None, :]
    input_grad = rstd_ch * (act_grad * gn_gain - first_ch - normalized * second_ch)
    input_grad = input_grad.astype(jnp.bfloat16)
    param_sums, input_grad = all_sum(jnp.sum(row_sums, axis=0), "dp", input_grad, 1)
    grad_scale = 1.0 / math.sqrt(images * lax.axis_size("dp") * slab_rows * row_devices * col_count)
    return (features_out, input_grad, param_sums * grad_scale)


def solution(mesh):
    placed = (
        P("dp", "rows", None, None),
        P("dp"),
        P(),
        P(),
        P(),
        P(),
        P(),
        P("dp", "rows", None, None),
    )
    return jax.shard_map(
        per_device,
        mesh=mesh,
        in_specs=placed,
        out_specs=(P("dp", "rows", None, None), P("dp", "rows", None, None), P()),
        check_vma=False,
    )
```

```python
import math

import jax
import jax.numpy as jnp
from jax import lax
from jax.experimental import pallas as pl
from jax.sharding import PartitionSpec as P

CH_GROUP = 40


NORM_EPS = 1e-05


def padded_2(cells, sides, width):
    for axis, dim in sides:
        count = lax.axis_size(axis)
        ends = count - 1
        head = lax.slice_in_dim(cells, 0, width, axis=dim)
        tail = lax.slice_in_dim(cells, cells.shape[dim] - width, cells.shape[dim], axis=dim)
        cells = jnp.concatenate(
            [
                lax.ppermute(tail, axis, [(i, (i + 1) % count) for i in range(ends)]),
                cells,
                lax.ppermute(head, axis, [((i + 1) % count, i) for i in range(ends)]),
            ],
            axis=dim,
        )
    return cells


def is_pow2(count):
    return count & (count - 1) == 0


def all_sum(value, axis):
    count = lax.axis_size(axis)
    if not is_pow2(count):
        return lax.psum(value, axis)
    step = count // 2
    while step >= 1:
        other = lax.ppermute(value, axis, [(i, i ^ step) for i in range(count)])
        value = value + other
        step //= 2
    return value


def merge_stats(mean, m2, cells, axis):
    count = lax.axis_size(axis)
    if not is_pow2(count):
        means = lax.all_gather(mean, axis)
        total_mean = jnp.mean(means, axis=0)
        spread = means - total_mean
        return total_mean, jnp.sum(lax.all_gather(m2, axis), axis=0) + cells * jnp.sum(spread * spread, axis=0)
    value = jnp.stack([mean, m2])
    step = count // 2
    size = 1
    while step >= 1:
        other = lax.ppermute(value, axis, [(i, i ^ step) for i in range(count)])
        delta = other[0] - value[0]
        value = jnp.stack(
            [(value[0] + other[0]) * 0.5, value[1] + other[1] + delta * delta * (cells * size * 0.5)]
        )
        step //= 2
        size *= 2
    return value[0], value[1]


def edge_kernel(lat_ref, ct_ref, tails_ref, heads_ref):
    slab_rows = lat_ref.shape[1]
    tails_ref[0] = lat_ref[:, slab_rows - 1]
    tails_ref[1] = ct_ref[:, slab_rows - 1]
    heads_ref[0] = lat_ref[:, 0]
    heads_ref[1] = ct_ref[:, 0]


def rims_of(latents, cotangent):
    images, _, col_count, channels = latents.shape
    edge = jax.ShapeDtypeStruct((2, images, col_count, channels), latents.dtype)
    tails, heads = pl.pallas_call(edge_kernel, out_shape=(edge, edge))(latents, cotangent)
    count = lax.axis_size("rows")
    from_above = lax.ppermute(tails, "rows", [(i, i + 1) for i in range(count - 1)])
    from_below = lax.ppermute(heads, "rows", [(i + 1, i) for i in range(count - 1)])
    return [
        jnp.concatenate([from_above[k][:, None], field, from_below[k][:, None]], axis=1)
        for k, field in enumerate((latents, cotangent))
    ]


def sinusoid(steps, embed_dim):
    half_dim = embed_dim // 2
    frequencies = jnp.exp(-math.log(10000.0) * jnp.arange(half_dim).astype(jnp.float32) / half_dim)
    angles = steps.astype(jnp.float32)[:, None] * frequencies[None, :]
    return jnp.concatenate([jnp.cos(angles), jnp.sin(angles)], axis=1)


def with_rim(field):
    return padded_2(field, (("rows", 2),), 1)


def conv_taps(extended, weight, slab_rows, col_count, backward):
    padded = jnp.pad(extended, ((0, 0), (0, 0), (1, 1), (0, 0)))
    channels = padded.shape[3]
    total = None
    for tap_row in range(3):
        for tap_col in range(3):
            if backward:
                row_start, col_start = (2 - tap_row, 2 - tap_col)
                dims = (((1,), (1,)), ((), ()))
            else:
                row_start, col_start = (tap_row, tap_col)
                dims = (((1,), (0,)), ((), ()))
            window = padded[
                :, row_start : row_start + slab_rows, col_start : col_start + col_count
            ].reshape(-1, channels)
            tap_term = lax.dot_general(
                window, weight[tap_row, tap_col], dims, preferred_element_type=jnp.float32
            )
            total = tap_term if total is None else total + tap_term
    return total.reshape(-1, slab_rows, col_count, weight.shape[3])


def per_device(
    latents, timesteps, gn_gain, gn_bias, conv_weight, conv_bias, temb_weight, cotangent
):
    images, slab_rows, col_count, channels = latents.shape
    groups = channels // CH_GROUP
    row_devices = lax.axis_size("rows")
    group_cells = slab_rows * row_devices * col_count * CH_GROUP
    positions = slab_rows * col_count
    both_ext = rims_of(latents, cotangent)
    row_index = lax.axis_index("rows")
    inside = jnp.concatenate(
        [
            jnp.where(row_index > 0, 1.0, 0.0)[None],
            jnp.ones((slab_rows,), jnp.float32),
            jnp.where(row_index < row_devices - 1, 1.0, 0.0)[None],
        ]
    )[None, :, None, None]
    values = latents.astype(jnp.float32)
    pivot = latents[:, 0, 0, :].astype(jnp.float32)
    shifted = latents.astype(jnp.float32) - pivot[:, None, None, :]
    shift_sum = jnp.sum(shifted, axis=(1, 2))
    shift_sq = jnp.sum(shifted * shifted, axis=(1, 2))
    chan_mean = pivot + shift_sum / positions
    chan_m2 = jnp.maximum(shift_sq - shift_sum * (shift_sum / positions), 0.0)
    chan_mean_g = chan_mean.reshape(images, groups, CH_GROUP)
    local_mean = jnp.mean(chan_mean_g, axis=2)
    spread = chan_mean_g - local_mean[:, :, None]
    local_m2 = jnp.sum(chan_m2.reshape(images, groups, CH_GROUP), axis=2) + positions * jnp.sum(
        spread * spread, axis=2
    )
    group_mean, group_m2 = merge_stats(local_mean, local_m2, positions * CH_GROUP, "rows")
    inv_std = lax.rsqrt(group_m2 / group_cells + NORM_EPS)
    inv_std, grad_src = lax.optimization_barrier((inv_std, cotangent))
    chan_output = jnp.sum(grad_src.astype(jnp.float32), axis=(1, 2))
    mean_ch = jnp.repeat(group_mean, CH_GROUP, axis=1)[:, None, None, :]
    rstd_ch = jnp.repeat(inv_std, CH_GROUP, axis=1)[:, None, None, :]
    normalized_ext = (both_ext[0].astype(jnp.float32) - mean_ch) * rstd_ch
    pre_act_ext = normalized_ext * gn_gain + gn_bias
    extended = (jax.nn.silu(pre_act_ext) * inside).astype(jnp.bfloat16)
    normalized = normalized_ext[:, 1 : 1 + slab_rows]
    pre_act = pre_act_ext[:, 1 : 1 + slab_rows]
    temb_features = jax.nn.silu(sinusoid(timesteps, temb_weight.shape[0])).astype(jnp.bfloat16)
    time_shift = jnp.dot(temb_features, temb_weight, preferred_element_type=jnp.float32)
    features = conv_taps(extended, conv_weight, slab_rows, col_count, False)
    features_out = (features + conv_bias + time_shift[:, None, None, :]).astype(jnp.bfloat16)
    hidden_grad = conv_taps(both_ext[1], conv_weight, slab_rows, col_count, True)
    sigmoid_act = jax.nn.sigmoid(pre_act)
    act_grad = hidden_grad * sigmoid_act * (1.0 + pre_act * (1.0 - sigmoid_act))
    chan_weighted = jnp.sum(act_grad * normalized, axis=(1, 2))
    chan_plain = jnp.sum(act_grad, axis=(1, 2))
    row_sums = all_sum(jnp.stack([chan_weighted, chan_plain, chan_output], axis=1), "rows")
    row_weighted, row_plain = row_sums[:, 0], row_sums[:, 1]
    first_sum = jnp.sum((row_plain * gn_gain).reshape(images, groups, CH_GROUP), axis=2)
    second_sum = jnp.sum((row_weighted * gn_gain).reshape(images, groups, CH_GROUP), axis=2)
    param_sums = all_sum(jnp.sum(row_sums, axis=0), "dp")
    first_ch = jnp.repeat(first_sum / group_cells, CH_GROUP, axis=1)[:, None, None, :]
    second_ch = jnp.repeat(second_sum / group_cells, CH_GROUP, axis=1)[:, None, None, :]
    input_grad = rstd_ch * (act_grad * gn_gain - first_ch - normalized * second_ch)
    input_grad = input_grad.astype(jnp.bfloat16)
    grad_scale = 1.0 / math.sqrt(images * lax.axis_size("dp") * slab_rows * row_devices * col_count)
    return (features_out, input_grad, param_sums * grad_scale)


def solution(mesh):
    placed = (
        P("dp", "rows", None, None),
        P("dp"),
        P(),
        P(),
        P(),
        P(),
        P(),
        P("dp", "rows", None, None),
    )
    return jax.shard_map(
        per_device,
        mesh=mesh,
        in_specs=placed,
        out_specs=(P("dp", "rows", None, None), P("dp", "rows", None, None), P()),
        check_vma=False,
    )
```

```python
import math

import jax
import jax.numpy as jnp
from jax import lax
from jax.sharding import PartitionSpec as P

CH_GROUP = 40


NORM_EPS = 1e-05


def padded_2(cells, sides, width):
    for axis, dim in sides:
        count = lax.axis_size(axis)
        ends = count - 1
        head = lax.slice_in_dim(cells, 0, width, axis=dim)
        tail = lax.slice_in_dim(cells, cells.shape[dim] - width, cells.shape[dim], axis=dim)
        cells = jnp.concatenate(
            [
                lax.ppermute(tail, axis, [(i, (i + 1) % count) for i in range(ends)]),
                cells,
                lax.ppermute(head, axis, [((i + 1) % count, i) for i in range(ends)]),
            ],
            axis=dim,
        )
    return cells


def is_pow2(count):
    return count & (count - 1) == 0


def all_sum(value, axis):
    count = lax.axis_size(axis)
    if not is_pow2(count):
        return lax.psum(value, axis)
    step = count // 2
    while step >= 1:
        other = lax.ppermute(value, axis, [(i, i ^ step) for i in range(count)])
        value = value + other
        step //= 2
    return value


def merge_stats(mean, m2, cells, axis):
    count = lax.axis_size(axis)
    if not is_pow2(count):
        means = lax.all_gather(mean, axis)
        total_mean = jnp.mean(means, axis=0)
        spread = means - total_mean
        return total_mean, jnp.sum(lax.all_gather(m2, axis), axis=0) + cells * jnp.sum(spread * spread, axis=0)
    value = jnp.stack([mean, m2])
    step = count // 2
    size = 1
    while step >= 1:
        other = lax.ppermute(value, axis, [(i, i ^ step) for i in range(count)])
        delta = other[0] - value[0]
        value = jnp.stack(
            [(value[0] + other[0]) * 0.5, value[1] + other[1] + delta * delta * (cells * size * 0.5)]
        )
        step //= 2
        size *= 2
    return value[0], value[1]


def sinusoid(steps, embed_dim):
    half_dim = embed_dim // 2
    frequencies = jnp.exp(-math.log(10000.0) * jnp.arange(half_dim).astype(jnp.float32) / half_dim)
    angles = steps.astype(jnp.float32)[:, None] * frequencies[None, :]
    return jnp.concatenate([jnp.cos(angles), jnp.sin(angles)], axis=1)


def with_rim(field):
    return padded_2(field, (("rows", 2),), 1)


def conv_taps(extended, weight, slab_rows, col_count, backward):
    padded = jnp.pad(extended, ((0, 0), (0, 0), (1, 1), (0, 0)))
    channels = padded.shape[3]
    total = None
    for tap_row in range(3):
        for tap_col in range(3):
            if backward:
                row_start, col_start = (2 - tap_row, 2 - tap_col)
                dims = (((1,), (1,)), ((), ()))
            else:
                row_start, col_start = (tap_row, tap_col)
                dims = (((1,), (0,)), ((), ()))
            window = padded[
                :, row_start : row_start + slab_rows, col_start : col_start + col_count
            ].reshape(-1, channels)
            tap_term = lax.dot_general(
                window, weight[tap_row, tap_col], dims, preferred_element_type=jnp.float32
            )
            total = tap_term if total is None else total + tap_term
    return total.reshape(-1, slab_rows, col_count, weight.shape[3])


def per_device(
    latents, timesteps, gn_gain, gn_bias, conv_weight, conv_bias, temb_weight, cotangent
):
    images, slab_rows, col_count, channels = latents.shape
    groups = channels // CH_GROUP
    row_devices = lax.axis_size("rows")
    group_cells = slab_rows * row_devices * col_count * CH_GROUP
    positions = slab_rows * col_count
    both_ext = with_rim(jnp.stack([latents, cotangent]))
    row_index = lax.axis_index("rows")
    inside = jnp.concatenate(
        [
            jnp.where(row_index > 0, 1.0, 0.0)[None],
            jnp.ones((slab_rows,), jnp.float32),
            jnp.where(row_index < row_devices - 1, 1.0, 0.0)[None],
        ]
    )[None, :, None, None]
    values = latents.astype(jnp.float32)
    pivot = latents[:, 0, 0, :].astype(jnp.float32)
    shifted = latents.astype(jnp.float32) - pivot[:, None, None, :]
    shift_sum = jnp.sum(shifted, axis=(1, 2))
    shift_sq = jnp.sum(shifted * shifted, axis=(1, 2))
    chan_mean = pivot + shift_sum / positions
    chan_m2 = jnp.maximum(shift_sq - shift_sum * (shift_sum / positions), 0.0)
    chan_mean_g = chan_mean.reshape(images, groups, CH_GROUP)
    local_mean = jnp.mean(chan_mean_g, axis=2)
    spread = chan_mean_g - local_mean[:, :, None]
    local_m2 = jnp.sum(chan_m2.reshape(images, groups, CH_GROUP), axis=2) + positions * jnp.sum(
        spread * spread, axis=2
    )
    group_mean, group_m2 = merge_stats(local_mean, local_m2, positions * CH_GROUP, "rows")
    inv_std = lax.rsqrt(group_m2 / group_cells + NORM_EPS)
    inv_std, grad_src = lax.optimization_barrier((inv_std, cotangent))
    chan_output = jnp.sum(grad_src.astype(jnp.float32), axis=(1, 2))
    mean_ch = jnp.repeat(group_mean, CH_GROUP, axis=1)[:, None, None, :]
    rstd_ch = jnp.repeat(inv_std, CH_GROUP, axis=1)[:, None, None, :]
    normalized_ext = (both_ext[0].astype(jnp.float32) - mean_ch) * rstd_ch
    pre_act_ext = normalized_ext * gn_gain + gn_bias
    extended = (jax.nn.silu(pre_act_ext) * inside).astype(jnp.bfloat16)
    normalized = normalized_ext[:, 1 : 1 + slab_rows]
    pre_act = pre_act_ext[:, 1 : 1 + slab_rows]
    temb_features = jax.nn.silu(sinusoid(timesteps, temb_weight.shape[0])).astype(jnp.bfloat16)
    time_shift = jnp.dot(temb_features, temb_weight, preferred_element_type=jnp.float32)
    features = conv_taps(extended, conv_weight, slab_rows, col_count, False)
    features_out = (features + conv_bias + time_shift[:, None, None, :]).astype(jnp.bfloat16)
    hidden_grad = conv_taps(both_ext[1], conv_weight, slab_rows, col_count, True)
    sigmoid_act = jax.nn.sigmoid(pre_act)
    act_grad = hidden_grad * sigmoid_act * (1.0 + pre_act * (1.0 - sigmoid_act))
    chan_weighted = jnp.sum(act_grad * normalized, axis=(1, 2))
    chan_plain = jnp.sum(act_grad, axis=(1, 2))
    row_sums = all_sum(jnp.stack([chan_weighted, chan_plain, chan_output], axis=1), "rows")
    row_weighted, row_plain = row_sums[:, 0], row_sums[:, 1]
    first_sum = jnp.sum((row_plain * gn_gain).reshape(images, groups, CH_GROUP), axis=2)
    second_sum = jnp.sum((row_weighted * gn_gain).reshape(images, groups, CH_GROUP), axis=2)
    grad_scale = 1.0 / math.sqrt(images * lax.axis_size("dp") * slab_rows * row_devices * col_count)
    param_sums = all_sum(jnp.sum(row_sums, axis=0) * grad_scale, "dp")
    first_ch = jnp.repeat(first_sum / group_cells, CH_GROUP, axis=1)[:, None, None, :]
    second_ch = jnp.repeat(second_sum / group_cells, CH_GROUP, axis=1)[:, None, None, :]
    input_grad = rstd_ch * (act_grad * gn_gain - first_ch - normalized * second_ch)
    input_grad = input_grad.astype(jnp.bfloat16)
    return (features_out, input_grad, param_sums)


def solution(mesh):
    placed = (
        P("dp", "rows", None, None),
        P("dp"),
        P(),
        P(),
        P(),
        P(),
        P(),
        P("dp", "rows", None, None),
    )
    return jax.shard_map(
        per_device,
        mesh=mesh,
        in_specs=placed,
        out_specs=(P("dp", "rows", None, None), P("dp", "rows", None, None), P()),
        check_vma=False,
    )
```

```python
import math

import jax
import jax.numpy as jnp
from jax import lax
from jax.sharding import PartitionSpec as P

CH_GROUP = 40


NORM_EPS = 1e-05


def padded_2(cells, sides, width):
    for axis, dim in sides:
        count = lax.axis_size(axis)
        ends = count - 1
        head = lax.slice_in_dim(cells, 0, width, axis=dim)
        tail = lax.slice_in_dim(cells, cells.shape[dim] - width, cells.shape[dim], axis=dim)
        cells = jnp.concatenate(
            [
                lax.ppermute(tail, axis, [(i, (i + 1) % count) for i in range(ends)]),
                cells,
                lax.ppermute(head, axis, [((i + 1) % count, i) for i in range(ends)]),
            ],
            axis=dim,
        )
    return cells


def is_pow2(count):
    return count & (count - 1) == 0


def all_sum(value, axis):
    count = lax.axis_size(axis)
    if not is_pow2(count):
        return lax.psum(value, axis)
    step = count // 2
    while step >= 1:
        other = lax.ppermute(value, axis, [(i, i ^ step) for i in range(count)])
        value = value + other
        step //= 2
    return value


def merge_stats(mean, m2, cells, axis):
    count = lax.axis_size(axis)
    if not is_pow2(count):
        means = lax.all_gather(mean, axis)
        total_mean = jnp.mean(means, axis=0)
        spread = means - total_mean
        return total_mean, jnp.sum(lax.all_gather(m2, axis), axis=0) + cells * jnp.sum(spread * spread, axis=0)
    value = jnp.stack([mean, m2])
    step = count // 2
    size = 1
    while step >= 1:
        other = lax.ppermute(value, axis, [(i, i ^ step) for i in range(count)])
        delta = other[0] - value[0]
        value = jnp.stack(
            [(value[0] + other[0]) * 0.5, value[1] + other[1] + delta * delta * (cells * size * 0.5)]
        )
        step //= 2
        size *= 2
    return value[0], value[1]


def sinusoid(steps, embed_dim):
    half_dim = embed_dim // 2
    frequencies = jnp.exp(-math.log(10000.0) * jnp.arange(half_dim).astype(jnp.float32) / half_dim)
    angles = steps.astype(jnp.float32)[:, None] * frequencies[None, :]
    return jnp.concatenate([jnp.cos(angles), jnp.sin(angles)], axis=1)


def with_rim(field):
    return padded_2(field, (("rows", 2),), 1)


def conv_taps(extended, weight, slab_rows, col_count, backward):
    padded = jnp.pad(extended, ((0, 0), (0, 0), (1, 1), (0, 0)))
    channels = padded.shape[3]
    total = None
    for tap_row in range(3):
        for tap_col in range(3):
            if backward:
                row_start, col_start = (2 - tap_row, 2 - tap_col)
                dims = (((1,), (1,)), ((), ()))
            else:
                row_start, col_start = (tap_row, tap_col)
                dims = (((1,), (0,)), ((), ()))
            window = padded[
                :, row_start : row_start + slab_rows, col_start : col_start + col_count
            ].reshape(-1, channels)
            tap_term = lax.dot_general(
                window, weight[tap_row, tap_col], dims, preferred_element_type=jnp.float32
            )
            total = tap_term if total is None else total + tap_term
    return total.reshape(-1, slab_rows, col_count, weight.shape[3])


def per_device(
    latents, timesteps, gn_gain, gn_bias, conv_weight, conv_bias, temb_weight, cotangent
):
    images, slab_rows, col_count, channels = latents.shape
    groups = channels // CH_GROUP
    row_devices = lax.axis_size("rows")
    group_cells = slab_rows * row_devices * col_count * CH_GROUP
    positions = slab_rows * col_count
    both_ext = with_rim(jnp.stack([latents, cotangent]))
    row_index = lax.axis_index("rows")
    inside = jnp.concatenate(
        [
            jnp.where(row_index > 0, 1.0, 0.0)[None],
            jnp.ones((slab_rows,), jnp.float32),
            jnp.where(row_index < row_devices - 1, 1.0, 0.0)[None],
        ]
    )[None, :, None, None]
    values = latents.astype(jnp.float32)
    pivot = latents[:, 0, 0, :].astype(jnp.float32)
    shifted = latents.astype(jnp.float32) - pivot[:, None, None, :]
    shift_sum = jnp.sum(shifted, axis=(1, 2))
    shift_sq = jnp.sum(shifted * shifted, axis=(1, 2))
    chan_mean = pivot + shift_sum / positions
    chan_m2 = jnp.maximum(shift_sq - shift_sum * (shift_sum / positions), 0.0)
    chan_mean_g = chan_mean.reshape(images, groups, CH_GROUP)
    local_mean = jnp.mean(chan_mean_g, axis=2)
    spread = chan_mean_g - local_mean[:, :, None]
    local_m2 = jnp.sum(chan_m2.reshape(images, groups, CH_GROUP), axis=2) + positions * jnp.sum(
        spread * spread, axis=2
    )
    group_mean, group_m2 = merge_stats(local_mean, local_m2, positions * CH_GROUP, "rows")
    inv_std = lax.rsqrt(group_m2 / group_cells + NORM_EPS)
    inv_std, grad_src, steps = lax.optimization_barrier((inv_std, cotangent, timesteps))
    temb_features = jax.nn.silu(sinusoid(steps, temb_weight.shape[0])).astype(jnp.bfloat16)
    time_shift = jnp.dot(temb_features, temb_weight, preferred_element_type=jnp.float32)
    chan_output = jnp.sum(grad_src.astype(jnp.float32), axis=(1, 2))
    mean_ch = jnp.repeat(group_mean, CH_GROUP, axis=1)[:, None, None, :]
    rstd_ch = jnp.repeat(inv_std, CH_GROUP, axis=1)[:, None, None, :]
    normalized_ext = (both_ext[0].astype(jnp.float32) - mean_ch) * rstd_ch
    pre_act_ext = normalized_ext * gn_gain + gn_bias
    extended = (jax.nn.silu(pre_act_ext) * inside).astype(jnp.bfloat16)
    normalized = normalized_ext[:, 1 : 1 + slab_rows]
    pre_act = pre_act_ext[:, 1 : 1 + slab_rows]
    features = conv_taps(extended, conv_weight, slab_rows, col_count, False)
    features_out = (features + conv_bias + time_shift[:, None, None, :]).astype(jnp.bfloat16)
    hidden_grad = conv_taps(both_ext[1], conv_weight, slab_rows, col_count, True)
    sigmoid_act = jax.nn.sigmoid(pre_act)
    act_grad = hidden_grad * sigmoid_act * (1.0 + pre_act * (1.0 - sigmoid_act))
    chan_weighted = jnp.sum(act_grad * normalized, axis=(1, 2))
    chan_plain = jnp.sum(act_grad, axis=(1, 2))
    row_sums = all_sum(jnp.stack([chan_weighted, chan_plain, chan_output], axis=1), "rows")
    row_weighted, row_plain = row_sums[:, 0], row_sums[:, 1]
    first_sum = jnp.sum((row_plain * gn_gain).reshape(images, groups, CH_GROUP), axis=2)
    second_sum = jnp.sum((row_weighted * gn_gain).reshape(images, groups, CH_GROUP), axis=2)
    grad_scale = 1.0 / math.sqrt(images * lax.axis_size("dp") * slab_rows * row_devices * col_count)
    param_sums = all_sum(jnp.sum(row_sums, axis=0) * grad_scale, "dp")
    first_ch = jnp.repeat(first_sum / group_cells, CH_GROUP, axis=1)[:, None, None, :]
    second_ch = jnp.repeat(second_sum / group_cells, CH_GROUP, axis=1)[:, None, None, :]
    input_grad = rstd_ch * (act_grad * gn_gain - first_ch - normalized * second_ch)
    input_grad = input_grad.astype(jnp.bfloat16)
    return (features_out, input_grad, param_sums)


def solution(mesh):
    placed = (
        P("dp", "rows", None, None),
        P("dp"),
        P(),
        P(),
        P(),
        P(),
        P(),
        P("dp", "rows", None, None),
    )
    return jax.shard_map(
        per_device,
        mesh=mesh,
        in_specs=placed,
        out_specs=(P("dp", "rows", None, None), P("dp", "rows", None, None), P()),
        check_vma=False,
    )
```

```python
import math

import jax
import jax.numpy as jnp
from jax import lax
from jax.sharding import PartitionSpec as P

CH_GROUP = 40


NORM_EPS = 1e-05


def padded_2(cells, sides, width):
    for axis, dim in sides:
        count = lax.axis_size(axis)
        ends = count - 1
        head = lax.slice_in_dim(cells, 0, width, axis=dim)
        tail = lax.slice_in_dim(cells, cells.shape[dim] - width, cells.shape[dim], axis=dim)
        cells = jnp.concatenate(
            [
                lax.ppermute(tail, axis, [(i, (i + 1) % count) for i in range(ends)]),
                cells,
                lax.ppermute(head, axis, [((i + 1) % count, i) for i in range(ends)]),
            ],
            axis=dim,
        )
    return cells


def is_pow2(count):
    return count & (count - 1) == 0


def all_sum(value, axis, ascending=False):
    count = lax.axis_size(axis)
    if not is_pow2(count):
        return lax.psum(value, axis)
    steps = []
    step = count // 2
    while step >= 1:
        steps.append(step)
        step //= 2
    for step in steps[::-1] if ascending else steps:
        other = lax.ppermute(value, axis, [(i, i ^ step) for i in range(count)])
        value = value + other
    return value


def merge_stats(mean, m2, cells, axis):
    count = lax.axis_size(axis)
    if not is_pow2(count):
        means = lax.all_gather(mean, axis)
        total_mean = jnp.mean(means, axis=0)
        spread = means - total_mean
        return total_mean, jnp.sum(lax.all_gather(m2, axis), axis=0) + cells * jnp.sum(spread * spread, axis=0)
    value = jnp.stack([mean, m2])
    step = count // 2
    size = 1
    while step >= 1:
        other = lax.ppermute(value, axis, [(i, i ^ step) for i in range(count)])
        delta = other[0] - value[0]
        value = jnp.stack(
            [(value[0] + other[0]) * 0.5, value[1] + other[1] + delta * delta * (cells * size * 0.5)]
        )
        step //= 2
        size *= 2
    return value[0], value[1]


def sinusoid(steps, embed_dim):
    half_dim = embed_dim // 2
    frequencies = jnp.exp(-math.log(10000.0) * jnp.arange(half_dim).astype(jnp.float32) / half_dim)
    angles = steps.astype(jnp.float32)[:, None] * frequencies[None, :]
    return jnp.concatenate([jnp.cos(angles), jnp.sin(angles)], axis=1)


def with_rim(field):
    return padded_2(field, (("rows", 2),), 1)


def conv_taps(extended, weight, slab_rows, col_count, backward):
    padded = jnp.pad(extended, ((0, 0), (0, 0), (1, 1), (0, 0)))
    channels = padded.shape[3]
    total = None
    for tap_row in range(3):
        for tap_col in range(3):
            if backward:
                row_start, col_start = (2 - tap_row, 2 - tap_col)
                dims = (((1,), (1,)), ((), ()))
            else:
                row_start, col_start = (tap_row, tap_col)
                dims = (((1,), (0,)), ((), ()))
            window = padded[
                :, row_start : row_start + slab_rows, col_start : col_start + col_count
            ].reshape(-1, channels)
            tap_term = lax.dot_general(
                window, weight[tap_row, tap_col], dims, preferred_element_type=jnp.float32
            )
            total = tap_term if total is None else total + tap_term
    return total.reshape(-1, slab_rows, col_count, weight.shape[3])


def per_device(
    latents, timesteps, gn_gain, gn_bias, conv_weight, conv_bias, temb_weight, cotangent
):
    images, slab_rows, col_count, channels = latents.shape
    groups = channels // CH_GROUP
    row_devices = lax.axis_size("rows")
    group_cells = slab_rows * row_devices * col_count * CH_GROUP
    positions = slab_rows * col_count
    both_ext = with_rim(jnp.stack([latents, cotangent]))
    row_index = lax.axis_index("rows")
    inside = jnp.concatenate(
        [
            jnp.where(row_index > 0, 1.0, 0.0)[None],
            jnp.ones((slab_rows,), jnp.float32),
            jnp.where(row_index < row_devices - 1, 1.0, 0.0)[None],
        ]
    )[None, :, None, None]
    values = latents.astype(jnp.float32)
    pivot = latents[:, 0, 0, :].astype(jnp.float32)
    shifted = latents.astype(jnp.float32) - pivot[:, None, None, :]
    shift_sum = jnp.sum(shifted, axis=(1, 2))
    shift_sq = jnp.sum(shifted * shifted, axis=(1, 2))
    chan_mean = pivot + shift_sum / positions
    chan_m2 = jnp.maximum(shift_sq - shift_sum * (shift_sum / positions), 0.0)
    chan_mean_g = chan_mean.reshape(images, groups, CH_GROUP)
    local_mean = jnp.mean(chan_mean_g, axis=2)
    spread = chan_mean_g - local_mean[:, :, None]
    local_m2 = jnp.sum(chan_m2.reshape(images, groups, CH_GROUP), axis=2) + positions * jnp.sum(
        spread * spread, axis=2
    )
    group_mean, group_m2 = merge_stats(local_mean, local_m2, positions * CH_GROUP, "rows")
    inv_std = lax.rsqrt(group_m2 / group_cells + NORM_EPS)
    inv_std, grad_src, steps = lax.optimization_barrier((inv_std, cotangent, timesteps))
    temb_features = jax.nn.silu(sinusoid(steps, temb_weight.shape[0])).astype(jnp.bfloat16)
    time_shift = jnp.dot(temb_features, temb_weight, preferred_element_type=jnp.float32)
    chan_output = jnp.sum(grad_src.astype(jnp.float32), axis=(1, 2))
    mean_ch = jnp.repeat(group_mean, CH_GROUP, axis=1)[:, None, None, :]
    rstd_ch = jnp.repeat(inv_std, CH_GROUP, axis=1)[:, None, None, :]
    normalized_ext = (both_ext[0].astype(jnp.float32) - mean_ch) * rstd_ch
    pre_act_ext = normalized_ext * gn_gain + gn_bias
    extended = (jax.nn.silu(pre_act_ext) * inside).astype(jnp.bfloat16)
    normalized = normalized_ext[:, 1 : 1 + slab_rows]
    pre_act = pre_act_ext[:, 1 : 1 + slab_rows]
    features = conv_taps(extended, conv_weight, slab_rows, col_count, False)
    features_out = (features + conv_bias + time_shift[:, None, None, :]).astype(jnp.bfloat16)
    hidden_grad = conv_taps(both_ext[1], conv_weight, slab_rows, col_count, True)
    sigmoid_act = jax.nn.sigmoid(pre_act)
    act_grad = hidden_grad * sigmoid_act * (1.0 + pre_act * (1.0 - sigmoid_act))
    chan_weighted = jnp.sum(act_grad * normalized, axis=(1, 2))
    chan_plain = jnp.sum(act_grad, axis=(1, 2))
    row_sums = all_sum(jnp.stack([chan_weighted, chan_plain, chan_output], axis=1), "rows")
    row_weighted, row_plain = row_sums[:, 0], row_sums[:, 1]
    first_sum = jnp.sum((row_plain * gn_gain).reshape(images, groups, CH_GROUP), axis=2)
    second_sum = jnp.sum((row_weighted * gn_gain).reshape(images, groups, CH_GROUP), axis=2)
    grad_scale = 1.0 / math.sqrt(images * lax.axis_size("dp") * slab_rows * row_devices * col_count)
    param_sums = all_sum(jnp.sum(row_sums, axis=0) * grad_scale, "dp", True)
    first_ch = jnp.repeat(first_sum / group_cells, CH_GROUP, axis=1)[:, None, None, :]
    second_ch = jnp.repeat(second_sum / group_cells, CH_GROUP, axis=1)[:, None, None, :]
    input_grad = rstd_ch * (act_grad * gn_gain - first_ch - normalized * second_ch)
    input_grad = input_grad.astype(jnp.bfloat16)
    return (features_out, input_grad, param_sums)


def solution(mesh):
    placed = (
        P("dp", "rows", None, None),
        P("dp"),
        P(),
        P(),
        P(),
        P(),
        P(),
        P("dp", "rows", None, None),
    )
    return jax.shard_map(
        per_device,
        mesh=mesh,
        in_specs=placed,
        out_specs=(P("dp", "rows", None, None), P("dp", "rows", None, None), P()),
        check_vma=False,
    )
```
